32 devices in a mesh: groups: 2 (over y), lat: 8 (over z, x), seed: 2 (over core).
Axes of the slice: x: 2, y: 2, z: 4, core: 2. Of those that a mesh axis runs over, the one named last changes fastest.
Arguments:
- activations: bfloat16 [512, 2048], P(('groups', 'seed'), 'lat'), parts along dimension 0, may hold values from -6 to 6
- bag_rows: int32 [4, 256], P(('groups', 'seed')), parts along dimension 0, may hold values from 0 to 255
- keep_cols: int32 [4, 2048], P(('groups', 'seed')), parts along dimension 0, may hold values 0 or 1
- enc_weight: bfloat16 [4, 16384, 2048], P(('groups', 'seed'), 'lat'), parts along dimension 0, may hold values from -0.125 to 0.125
- enc_bias: float32 [4, 16384], P(('groups', 'seed'), 'lat'), parts along dimension 0, may hold values from -3 to 3
- dec_weight: bfloat16 [4, 16384, 2048], P(('groups', 'seed'), 'lat'), parts along dimension 0, may hold values from -0.0625 to 0.0625
- dec_bias: float32 [4, 2048], P(('groups', 'seed')), parts along dimension 0, may hold values from -3 to 3
- first_moment: bfloat16 [4, 16384, 2048], P(('groups', 'seed'), 'lat'), parts along dimension 0, may hold values from -0.3125 to 0.3125
- second_moment: bfloat16 [4, 16384, 2048], P(('groups', 'seed'), 'lat'), parts along dimension 0, may hold values from 9.9658966e-05 to 0.0099487305
Outputs:
- new_weight: bfloat16 [4, 16384, 2048], P(('groups', 'seed'), 'lat'), parts along dimension 0
- new_first: bfloat16 [4, 16384, 2048], P(('groups', 'seed'), 'lat'), parts along dimension 0
- new_second: bfloat16 [4, 16384, 2048], P(('groups', 'seed'), 'lat'), parts along dimension 0
The draws below stay inside these ranges and needn't reach their ends.
There are 2 independent parts, one for each index of `groups`. The reference program is written for one: setup_inputs(seed, part) draws one part's arguments, and reference() takes and returns one part's arrays. A program takes and returns all parts, laid end to end along the dimension named above; each array names one. Nothing has to cross between parts.
All inputs are finite; a program needn't handle non-finite values. No bound on the sum of `keep_cols` on one device may be relied on, other than what follows from the above.
Results may differ from the reference program's by a relative error of at most 0.012.
The reference program's roundings to bfloat16 on the way (of `sample`, `centered`, `latent`, `error` and `d_pre`) count: a program that leaves them out, or rounds other values in their place, can miss the bound.
Values may be sent and summed in bfloat16 or wider, within the bound.
No kernel may reach another device: no remote copies, remote signals or barrier semaphores. Data moves between devices by JAX's collectives and lax.ppermute only.
A program may use at most 128 MiB of HBM per device.

```python
import math
import jax
import jax.numpy as jnp
from jax import lax

D = 2048
L = 16384
TOK = 256
SEEDS = 2


def touch_ends(drawn, rng, smallest, largest):
    dims = drawn.shape
    spot = [jax.random.randint(jax.random.fold_in(rng, axis), (), 0, dims[axis]) for axis in range(len(dims))]
    drawn = drawn.at[tuple(spot)].set(smallest)
    longest = dims.index(max(dims))
    spot[longest] = (spot[longest] + 1) % dims[longest]
    return drawn.at[tuple(spot)].set(largest)


def strengthened(drawn, own_key, source, target, blocks, factor):
    owner, partner = [(jnp.arange(drawn.shape[position]) // (drawn.shape[position] // blocks)).reshape([-1 if axis == position else 1 for axis in range(drawn.ndim)]) for position in (source, target)]
    chosen = jax.random.permutation(own_key, blocks)[partner]
    strong = (owner == chosen) | (owner == (partner + blocks // 2) % blocks)
    return jnp.where(strong, factor * drawn, drawn)


def levels(key, shape, shards, smallest, largest):
    gain = 1.0
    for axis_at, parts in shards:
        heights = jax.random.uniform(jax.random.fold_in(jax.random.fold_in(key, 6), axis_at), (parts,), jnp.float32, smallest / len(shards), largest / len(shards))
        gain = gain * jnp.repeat(jnp.exp(heights), shape[axis_at] // parts).reshape((-1,) + (1,) * (len(shape) - 1 - axis_at))
    return gain


def gaussian(rng, extent, scale, reach, split=(), held_as=jnp.bfloat16):
    values = jax.random.normal(rng, extent, jnp.float32) * scale
    if len(split) > 0:
        values = levels(rng, extent, split, -0.22, 0.18) * values
    return jnp.clip(values, min=-reach, max=reach).astype(held_as)


def bell_draw_with(key, extent, spread, reach, cuts, heavy, held_as=jnp.bfloat16):
    result = spread * jax.random.normal(key, extent, jnp.float32)
    if cuts:
        result = result * levels(key, extent, cuts, -0.22, 0.18)
    return jnp.clip(strengthened(result, jax.random.fold_in(key, 3), *heavy), -reach, reach).astype(held_as)


def setup_inputs(seed: int = 0, part: int = 0) -> dict:
    key_list = jax.random.split(jax.random.key(seed), 10)
    part_keys = jax.random.split(jax.random.fold_in(key_list[9], part), 10)
    return {
        "activations": gaussian(part_keys[0], (TOK, D), 1.0, 6.0, ((0, 2), (1, 8))),
        "bag_rows": touch_ends(jax.random.randint(part_keys[1], (SEEDS, TOK), 0, TOK), jax.random.fold_in(part_keys[1], 1), 0, TOK - 1).astype(jnp.int32),
        "keep_cols": touch_ends((jax.random.randint(part_keys[2], (SEEDS, D), 0, 4) < 3).astype(jnp.int32), jax.random.fold_in(part_keys[2], 1), 0, 1),
        "enc_weight": gaussian(part_keys[3], (SEEDS, L, D), D ** -0.5, 0.125, ((0, 2), (1, 8))),
        "enc_bias": gaussian(part_keys[4], (SEEDS, L), 0.5, 3.0, ((0, 2), (1, 8)), jnp.float32),
        "dec_weight": bell_draw_with(part_keys[5], (SEEDS, L, D), L ** -0.5, 0.0625, ((0, 2), (1, 8)), (1, 2, 8, 2.0)),
        "dec_bias": gaussian(part_keys[6], (SEEDS, D), 0.5, 3.0, ((0, 2),), jnp.float32),
        "first_moment": gaussian(part_keys[7], (SEEDS, L, D), 0.02, 0.3125, ((0, 2), (1, 8))),
        "second_moment": jnp.clip(jnp.exp(math.log(0.0099487305) - 4.603446 * jax.random.uniform(part_keys[8], (SEEDS, L, D), jnp.float32) ** levels(part_keys[8], (SEEDS, L, D), ((0, 2), (1, 8)), -0.2, 0.2)), 9.965896606445312e-05, 0.0099487305).astype(jnp.bfloat16),
    }


sparsity = 0.2
beta_one = 0.9
beta_two = 0.95
corr_one = 1.0 - 0.9 ** 10
corr_two = 1.0 - 0.95 ** 10
adam_eps = 1e-08
rate_step = 0.001
decay_rate = 0.1

def reference(activations, bag_rows, keep_cols, enc_weight, enc_bias, dec_weight, dec_bias, first_moment, second_moment):
    weights_out = []
    firsts_out = []
    seconds_out = []
    for seed_idx in range(SEEDS):
        sample = jnp.take(activations, bag_rows[seed_idx].astype(jnp.int32), axis=0)
        centered = (sample.astype(jnp.float32) - dec_bias[seed_idx]).astype(jnp.bfloat16)
        pre = jnp.dot(centered, enc_weight[seed_idx].T, preferred_element_type=jnp.float32) + enc_bias[seed_idx]
        latent = jnp.maximum(pre, 0.0).astype(jnp.bfloat16)
        recon = jnp.dot(latent, dec_weight[seed_idx], preferred_element_type=jnp.float32) + dec_bias[seed_idx]
        keep = keep_cols[seed_idx].astype(jnp.float32)
        error = ((recon - sample.astype(jnp.float32)) * keep).astype(jnp.bfloat16)
        dec32 = dec_weight[seed_idx].astype(jnp.float32)
        row_norm = jnp.sqrt(lax.optimization_barrier(jnp.sum(dec32 * dec32, axis=1)) + 1e-06)
        back = jnp.dot(error, dec_weight[seed_idx].T, preferred_element_type=jnp.float32)
        d_pre = (jnp.where(pre > 0, 2.0 * back + sparsity * row_norm, 0.0) / TOK).astype(jnp.bfloat16)
        grad = jnp.dot(d_pre.T, centered, preferred_element_type=jnp.float32)
        moment_one = beta_one * first_moment[seed_idx].astype(jnp.float32) + (1.0 - beta_one) * grad
        moment_two = beta_two * second_moment[seed_idx].astype(jnp.float32) + (1.0 - beta_two) * grad * grad
        direction = moment_one / corr_one / (jnp.sqrt(moment_two / corr_two) + adam_eps)
        old = enc_weight[seed_idx].astype(jnp.float32)
        weights_out.append((old - rate_step * (direction + decay_rate * old)).astype(jnp.bfloat16))
        firsts_out.append(moment_one.astype(jnp.bfloat16))
        seconds_out.append(moment_two.astype(jnp.bfloat16))
    return (jnp.stack(weights_out), jnp.stack(firsts_out), jnp.stack(seconds_out))
```

```python
import jax
import jax.numpy as jnp
from jax import lax
from jax.sharding import PartitionSpec as P

sparsity = 0.2
beta_one = 0.9
beta_two = 0.95
corr_one = 1.0 - 0.9**10
corr_two = 1.0 - 0.95**10
adam_eps = 1e-08
rate_step = 0.001
decay_rate = 0.1


def local(
    activations,
    bag_rows,
    keep_cols,
    enc_weight,
    enc_bias,
    dec_weight,
    dec_bias,
    first_moment,
    second_moment,
):
    half_rows = lax.all_gather(activations, "lat", axis=1, tiled=True)
    gathered = lax.all_gather(half_rows, "seed", axis=0, tiled=True)
    row_order = bag_rows[0]
    sample = jnp.take(gathered, row_order, axis=0)
    weight_in = enc_weight[0]
    decoder = dec_weight[0]
    bias_dec = dec_bias[0]
    keep = keep_cols[0].astype(jnp.float32)
    centered = (sample.astype(jnp.float32) - bias_dec).astype(jnp.bfloat16)
    pre_t = lax.dot_general(
        weight_in, centered, (((1,), (1,)), ((), ())), preferred_element_type=jnp.float32
    )
    pre_t = pre_t + enc_bias[0][:, None]
    latent_t = jnp.maximum(pre_t, 0.0).astype(jnp.bfloat16)
    lat_size = lax.psum(1, "lat")
    width = bias_dec.shape[0] // lat_size
    start = lax.axis_index("lat") * width
    decoder_blocks = decoder.reshape(decoder.shape[0], lat_size, width)
    partial_sum = jnp.einsum(
        "lt,lbf->btf", latent_t, decoder_blocks, preferred_element_type=jnp.float32
    )
    total = lax.psum_scatter(partial_sum, "lat", scatter_dimension=0, tiled=True)[0]
    sample_cols = lax.dynamic_slice_in_dim(sample, start, width, axis=1).astype(jnp.float32)
    bias_cols = lax.dynamic_slice_in_dim(bias_dec, start, width)
    keep_cols_f = lax.dynamic_slice_in_dim(keep, start, width)
    error_cols = ((total + bias_cols - sample_cols) * keep_cols_f).astype(jnp.bfloat16)
    error_blocks = lax.all_gather(error_cols, "lat", axis=0, tiled=False)
    error = jnp.transpose(error_blocks, (1, 0, 2)).reshape(error_cols.shape[0], -1)
    back_t = lax.dot_general(
        decoder, error, (((1,), (1,)), ((), ())), preferred_element_type=jnp.float32
    )
    row_norm = jnp.sqrt(jnp.sum(jnp.square(decoder.astype(jnp.float32)), axis=1) + 1e-06)
    token_total = sample.shape[0]
    d_pre_t = (
        jnp.where(pre_t > 0, 2.0 * back_t + sparsity * row_norm[:, None], 0.0) / token_total
    ).astype(jnp.bfloat16)
    grad = jnp.dot(d_pre_t, centered, preferred_element_type=jnp.float32)
    moment_one = beta_one * first_moment[0].astype(jnp.float32) + (1.0 - beta_one) * grad
    moment_two = beta_two * second_moment[0].astype(jnp.float32) + (1.0 - beta_two) * grad * grad
    direction = moment_one / corr_one / (jnp.sqrt(moment_two / corr_two) + adam_eps)
    old = weight_in.astype(jnp.float32)
    updated = (old - rate_step * (direction + decay_rate * old)).astype(jnp.bfloat16)
    return (
        updated[None],
        moment_one.astype(jnp.bfloat16)[None],
        moment_two.astype(jnp.bfloat16)[None],
    )


def solution(mesh):
    return jax.shard_map(
        local,
        mesh=mesh,
        in_specs=(
            P(("groups", "seed"), "lat"),
            P(("groups", "seed"), None),
            P(("groups", "seed"), None),
            P(("groups", "seed"), "lat", None),
            P(("groups", "seed"), "lat"),
            P(("groups", "seed"), "lat", None),
            P(("groups", "seed"), None),
            P(("groups", "seed"), "lat", None),
            P(("groups", "seed"), "lat", None),
        ),
        out_specs=(
            P(("groups", "seed"), "lat", None),
            P(("groups", "seed"), "lat", None),
            P(("groups", "seed"), "lat", None),
        ),
        check_vma=False,
    )
```

```python
import jax
import jax.numpy as jnp
from jax import lax
from jax.sharding import PartitionSpec as P

sparsity = 0.2
beta_one = 0.9
beta_two = 0.95
corr_one = 1.0 - 0.9**10
corr_two = 1.0 - 0.95**10
adam_eps = 1e-08
rate_step = 0.001
decay_rate = 0.1


def _pair_swap(value, axis, mask, size):
    return lax.ppermute(value, axis, [(i, i ^ mask) for i in range(size)])


def _halving_sum(blocks, axis, size, order):
    nbits = size.bit_length() - 1
    me = lax.axis_index(axis)
    cur = blocks.reshape((2,) * nbits + blocks.shape[1:])
    bits = list(range(nbits - 1, -1, -1))
    for bit in order:
        pos = bits.index(bit)
        mine_bit = (me >> bit) & 1
        keep_part = lax.dynamic_index_in_dim(cur, mine_bit, pos, keepdims=False)
        send_part = lax.dynamic_index_in_dim(cur, 1 - mine_bit, pos, keepdims=False)
        cur = keep_part + _pair_swap(send_part, axis, 1 << bit, size)
        bits.pop(pos)
    return cur


def _doubling_gather(value, axis, size, order):
    me = lax.axis_index(axis)
    cur = value
    bits = []
    for bit in order:
        other = _pair_swap(cur, axis, 1 << bit, size)
        low_is_me = ((me >> bit) & 1) == 0
        low = jnp.where(low_is_me, cur, other)
        high = jnp.where(low_is_me, other, cur)
        cur = jnp.stack([low, high], axis=0)
        bits.insert(0, bit)
    want = sorted(bits, reverse=True)
    cur = jnp.transpose(cur, [bits.index(b) for b in want] + list(range(len(bits), cur.ndim)))
    return cur.reshape((size,) + value.shape)


def _orders(size):
    nbits = size.bit_length() - 1
    first = list(range(nbits))
    second = first[:]
    if nbits >= 2:
        second[0], second[1] = 1, 0
    return first, second


def _reduce_scatter(blocks, axis, size):
    first, second = _orders(size)
    half = blocks.shape[1] // 2
    a = _halving_sum(blocks[:, :half], axis, size, first)
    b = _halving_sum(blocks[:, half:], axis, size, second)
    return jnp.concatenate([a, b], axis=0)


def _all_gather(value, axis, size):
    first, second = _orders(size)
    half = value.shape[0] // 2
    a = _doubling_gather(value[:half], axis, size, first[::-1])
    b = _doubling_gather(value[half:], axis, size, second[::-1])
    return jnp.concatenate([a, b], axis=1)


def local(
    activations,
    bag_rows,
    keep_cols,
    enc_weight,
    enc_bias,
    dec_weight,
    dec_bias,
    first_moment,
    second_moment,
):
    lat_size = LAT_SIZE[0]
    act_blocks = _all_gather(activations, "lat", lat_size)
    half_rows = jnp.transpose(act_blocks, (1, 0, 2)).reshape(activations.shape[0], -1)
    gathered = lax.all_gather(half_rows, "seed", axis=0, tiled=True)
    row_order = bag_rows[0]
    sample = jnp.take(gathered, row_order, axis=0)
    weight_in = enc_weight[0]
    decoder = dec_weight[0]
    bias_dec = dec_bias[0]
    keep = keep_cols[0].astype(jnp.float32)
    centered = (sample.astype(jnp.float32) - bias_dec).astype(jnp.bfloat16)
    pre_t = lax.dot_general(
        weight_in, centered, (((1,), (1,)), ((), ())), preferred_element_type=jnp.float32
    )
    pre_t = pre_t + enc_bias[0][:, None]
    latent_t = jnp.maximum(pre_t, 0.0).astype(jnp.bfloat16)
    width = bias_dec.shape[0] // lat_size
    start = lax.axis_index("lat") * width
    decoder_blocks = decoder.reshape(decoder.shape[0], lat_size, width)
    partial_sum = jnp.einsum(
        "lt,lbf->btf", latent_t, decoder_blocks, preferred_element_type=jnp.float32
    )
    total = _reduce_scatter(partial_sum, "lat", lat_size)
    sample_cols = lax.dynamic_slice_in_dim(sample, start, width, axis=1).astype(jnp.float32)
    bias_cols = lax.dynamic_slice_in_dim(bias_dec, start, width)
    keep_cols_f = lax.dynamic_slice_in_dim(keep, start, width)
    error_cols = ((total + bias_cols - sample_cols) * keep_cols_f).astype(jnp.bfloat16)
    error_blocks = _all_gather(error_cols, "lat", lat_size)
    error = jnp.transpose(error_blocks, (1, 0, 2)).reshape(error_cols.shape[0], -1)
    back_t = lax.dot_general(
        decoder, error, (((1,), (1,)), ((), ())), preferred_element_type=jnp.float32
    )
    row_norm = jnp.sqrt(jnp.sum(jnp.square(decoder.astype(jnp.float32)), axis=1) + 1e-06)
    token_total = sample.shape[0]
    d_pre_t = (
        jnp.where(pre_t > 0, 2.0 * back_t + sparsity * row_norm[:, None], 0.0) / token_total
    ).astype(jnp.bfloat16)
    grad = jnp.dot(d_pre_t, centered, preferred_element_type=jnp.float32)
    moment_one = beta_one * first_moment[0].astype(jnp.float32) + (1.0 - beta_one) * grad
    moment_two = beta_two * second_moment[0].astype(jnp.float32) + (1.0 - beta_two) * grad * grad
    direction = moment_one / corr_one / (jnp.sqrt(moment_two / corr_two) + adam_eps)
    old = weight_in.astype(jnp.float32)
    updated = (old - rate_step * (direction + decay_rate * old)).astype(jnp.bfloat16)
    return (
        updated[None],
        moment_one.astype(jnp.bfloat16)[None],
        moment_two.astype(jnp.bfloat16)[None],
    )


LAT_SIZE = [8]


def solution(mesh):
    LAT_SIZE[0] = mesh.shape["lat"]
    return jax.shard_map(
        local,
        mesh=mesh,
        in_specs=(
            P(("groups", "seed"), "lat"),
            P(("groups", "seed"), None),
            P(("groups", "seed"), None),
            P(("groups", "seed"), "lat", None),
            P(("groups", "seed"), "lat"),
            P(("groups", "seed"), "lat", None),
            P(("groups", "seed"), None),
            P(("groups", "seed"), "lat", None),
            P(("groups", "seed"), "lat", None),
        ),
        out_specs=(
            P(("groups", "seed"), "lat", None),
            P(("groups", "seed"), "lat", None),
            P(("groups", "seed"), "lat", None),
        ),
        check_vma=False,
    )
```

```python
import jax
import jax.numpy as jnp
from jax import lax
from jax.sharding import PartitionSpec as P

sparsity = 0.2
beta_one = 0.9
beta_two = 0.95
corr_one = 1.0 - 0.9**10
corr_two = 1.0 - 0.95**10
adam_eps = 1e-08
rate_step = 0.001
decay_rate = 0.1


def _pair_swap(value, axis, mask, size):
    return lax.ppermute(value, axis, [(i, i ^ mask) for i in range(size)])


def _halving_sum(blocks, axis, size, order):
    nbits = size.bit_length() - 1
    me = lax.axis_index(axis)
    cur = blocks.reshape((2,) * nbits + blocks.shape[1:])
    bits = list(range(nbits - 1, -1, -1))
    for bit in order:
        pos = bits.index(bit)
        mine_bit = (me >> bit) & 1
        keep_part = lax.dynamic_index_in_dim(cur, mine_bit, pos, keepdims=False)
        send_part = lax.dynamic_index_in_dim(cur, 1 - mine_bit, pos, keepdims=False)
        cur = keep_part + _pair_swap(send_part, axis, 1 << bit, size)
        bits.pop(pos)
    return cur


def _doubling_gather(value, axis, size, order):
    me = lax.axis_index(axis)
    cur = value
    bits = []
    for bit in order:
        other = _pair_swap(cur, axis, 1 << bit, size)
        low_is_me = ((me >> bit) & 1) == 0
        low = jnp.where(low_is_me, cur, other)
        high = jnp.where(low_is_me, other, cur)
        cur = jnp.stack([low, high], axis=0)
        bits.insert(0, bit)
    want = sorted(bits, reverse=True)
    cur = jnp.transpose(cur, [bits.index(b) for b in want] + list(range(len(bits), cur.ndim)))
    return cur.reshape((size,) + value.shape)


def _orders(size):
    nbits = size.bit_length() - 1
    first = list(range(nbits))
    second = first[:]
    if nbits >= 2:
        second[0], second[1] = 1, 0
    return first, second


def _halving_cols(cols, axis, size, order):
    nbits = size.bit_length() - 1
    me = lax.axis_index(axis)
    cur = cols
    block = 0
    for step, bit in enumerate(order):
        half = cur.shape[1] // 2
        mine_bit = (me >> bit) & 1
        keep_part = lax.dynamic_slice_in_dim(cur, mine_bit * half, half, axis=1)
        send_part = lax.dynamic_slice_in_dim(cur, (1 - mine_bit) * half, half, axis=1)
        cur = keep_part + _pair_swap(send_part, axis, 1 << bit, size)
        block = block + (mine_bit << (nbits - 1 - step))
    return cur, block


def _doubling_cols(cols, axis, size, order):
    me = lax.axis_index(axis)
    cur = cols
    for bit in order[::-1]:
        other = _pair_swap(cur, axis, 1 << bit, size)
        low_is_me = ((me >> bit) & 1) == 0
        low = jnp.where(low_is_me, cur, other)
        high = jnp.where(low_is_me, other, cur)
        cur = jnp.concatenate([low, high], axis=1)
    return cur


def local(
    activations,
    bag_rows,
    keep_cols,
    enc_weight,
    enc_bias,
    dec_weight,
    dec_bias,
    first_moment,
    second_moment,
):
    lat_size = LAT_SIZE[0]
    first, second = _orders(lat_size)
    act_blocks = _doubling_gather(activations, "lat", lat_size, first[::-1])
    half_rows = jnp.transpose(act_blocks, (1, 0, 2)).reshape(activations.shape[0], -1)
    gathered = lax.all_gather(half_rows, "seed", axis=0, tiled=True)
    row_order = bag_rows[0]
    sample = jnp.take(gathered, row_order, axis=0)
    weight_in = enc_weight[0]
    decoder = dec_weight[0]
    bias_dec = dec_bias[0]
    keep = keep_cols[0].astype(jnp.float32)
    centered = (sample.astype(jnp.float32) - bias_dec).astype(jnp.bfloat16)
    pre_t = lax.dot_general(
        weight_in, centered, (((1,), (1,)), ((), ())), preferred_element_type=jnp.float32
    )
    pre_t = pre_t + enc_bias[0][:, None]
    latent_t = jnp.maximum(pre_t, 0.0).astype(jnp.bfloat16)
    width = bias_dec.shape[0] // lat_size
    partial_sum = lax.dot_general(
        latent_t, decoder, (((0,), (0,)), ((), ())), preferred_element_type=jnp.float32
    )
    half = partial_sum.shape[0] // 2
    error_parts = []
    for rows, order in ((slice(0, half), first), (slice(half, None), second)):
        total, block = _halving_cols(partial_sum[rows], "lat", lat_size, order)
        start = block * width
        sample_cols = lax.dynamic_slice_in_dim(sample[rows], start, width, axis=1)
        bias_cols = lax.dynamic_slice_in_dim(bias_dec, start, width)
        keep_cols_f = lax.dynamic_slice_in_dim(keep, start, width)
        error_cols = (
            (total + bias_cols - sample_cols.astype(jnp.float32)) * keep_cols_f
        ).astype(jnp.bfloat16)
        error_parts.append(_doubling_cols(error_cols, "lat", lat_size, order))
    error = jnp.concatenate(error_parts, axis=0)
    back_t = lax.dot_general(
        decoder, error, (((1,), (1,)), ((), ())), preferred_element_type=jnp.float32
    )
    row_norm = jnp.sqrt(jnp.sum(jnp.square(decoder.astype(jnp.float32)), axis=1) + 1e-06)
    token_total = sample.shape[0]
    d_pre_t = (
        jnp.where(pre_t > 0, 2.0 * back_t + sparsity * row_norm[:, None], 0.0) / token_total
    ).astype(jnp.bfloat16)
    grad = jnp.dot(d_pre_t, centered, preferred_element_type=jnp.float32)
    moment_one = beta_one * first_moment[0].astype(jnp.float32) + (1.0 - beta_one) * grad
    moment_two = beta_two * second_moment[0].astype(jnp.float32) + (1.0 - beta_two) * grad * grad
    direction = moment_one / corr_one / (jnp.sqrt(moment_two / corr_two) + adam_eps)
    old = weight_in.astype(jnp.float32)
    updated = (old - rate_step * (direction + decay_rate * old)).astype(jnp.bfloat16)
    return (
        updated[None],
        moment_one.astype(jnp.bfloat16)[None],
        moment_two.astype(jnp.bfloat16)[None],
    )


LAT_SIZE = [8]


def solution(mesh):
    LAT_SIZE[0] = mesh.shape["lat"]
    return jax.shard_map(
        local,
        mesh=mesh,
        in_specs=(
            P(("groups", "seed"), "lat"),
            P(("groups", "seed"), None),
            P(("groups", "seed"), None),
            P(("groups", "seed"), "lat", None),
            P(("groups", "seed"), "lat"),
            P(("groups", "seed"), "lat", None),
            P(("groups", "seed"), None),
            P(("groups", "seed"), "lat", None),
            P(("groups", "seed"), "lat", None),
        ),
        out_specs=(
            P(("groups", "seed"), "lat", None),
            P(("groups", "seed"), "lat", None),
            P(("groups", "seed"), "lat", None),
        ),
        check_vma=False,
    )
```

```python
import jax
import jax.numpy as jnp
from jax import lax
from jax.sharding import PartitionSpec as P

sparsity = 0.2
beta_one = 0.9
beta_two = 0.95
corr_one = 1.0 - 0.9**10
corr_two = 1.0 - 0.95**10
adam_eps = 1e-08
rate_step = 0.001
decay_rate = 0.1


def _pair_swap(value, axis, mask, size):
    return lax.ppermute(value, axis, [(i, i ^ mask) for i in range(size)])


def _halving_sum(blocks, axis, size, order):
    nbits = size.bit_length() - 1
    me = lax.axis_index(axis)
    cur = blocks.reshape((2,) * nbits + blocks.shape[1:])
    bits = list(range(nbits - 1, -1, -1))
    for bit in order:
        pos = bits.index(bit)
        mine_bit = (me >> bit) & 1
        keep_part = lax.dynamic_index_in_dim(cur, mine_bit, pos, keepdims=False)
        send_part = lax.dynamic_index_in_dim(cur, 1 - mine_bit, pos, keepdims=False)
        cur = keep_part + _pair_swap(send_part, axis, 1 << bit, size)
        bits.pop(pos)
    return cur


def _doubling_gather(value, axis, size, order):
    me = lax.axis_index(axis)
    cur = value
    bits = []
    for bit in order:
        other = _pair_swap(cur, axis, 1 << bit, size)
        low_is_me = ((me >> bit) & 1) == 0
        low = jnp.where(low_is_me, cur, other)
        high = jnp.where(low_is_me, other, cur)
        cur = jnp.stack([low, high], axis=0)
        bits.insert(0, bit)
    want = sorted(bits, reverse=True)
    cur = jnp.transpose(cur, [bits.index(b) for b in want] + list(range(len(bits), cur.ndim)))
    return cur.reshape((size,) + value.shape)


def _orders(size):
    nbits = size.bit_length() - 1
    first = list(range(nbits))
    second = first[:]
    if nbits >= 2:
        second[0], second[1] = 1, 0
    return first, second


def _halving_cols(cols, axis, size, order):
    nbits = size.bit_length() - 1
    me = lax.axis_index(axis)
    cur = cols
    block = 0
    for step, bit in enumerate(order):
        half = cur.shape[1] // 2
        mine_bit = (me >> bit) & 1
        keep_part = lax.dynamic_slice_in_dim(cur, mine_bit * half, half, axis=1)
        send_part = lax.dynamic_slice_in_dim(cur, (1 - mine_bit) * half, half, axis=1)
        cur = keep_part + _pair_swap(send_part, axis, 1 << bit, size)
        block = block + (mine_bit << (nbits - 1 - step))
    return cur, block


def _block_owners(size, order):
    nbits = size.bit_length() - 1
    owned = [
        sum(((d >> bit) & 1) << (nbits - 1 - step) for step, bit in enumerate(order))
        for d in range(size)
    ]
    return [owned.index(k) for k in range(size)]


def _doubling_cols(cols, axis, size, order):
    me = lax.axis_index(axis)
    cur = cols
    for bit in order[::-1]:
        other = _pair_swap(cur, axis, 1 << bit, size)
        low_is_me = ((me >> bit) & 1) == 0
        low = jnp.where(low_is_me, cur, other)
        high = jnp.where(low_is_me, other, cur)
        cur = jnp.concatenate([low, high], axis=1)
    return cur


def local(
    activations,
    bag_rows,
    keep_cols,
    enc_weight,
    enc_bias,
    dec_weight,
    dec_bias,
    first_moment,
    second_moment,
):
    lat_size = LAT_SIZE[0]
    first, second = _orders(lat_size)
    act_blocks = _doubling_gather(activations, "lat", lat_size, first[::-1])
    half_rows = jnp.transpose(act_blocks, (1, 0, 2)).reshape(activations.shape[0], -1)
    gathered = lax.all_gather(half_rows, "seed", axis=0, tiled=True)
    row_order = bag_rows[0]
    sample = jnp.take(gathered, row_order, axis=0)
    weight_in = enc_weight[0]
    decoder = dec_weight[0]
    bias_dec = dec_bias[0]
    keep = keep_cols[0].astype(jnp.float32)
    centered = (sample.astype(jnp.float32) - bias_dec).astype(jnp.bfloat16)
    pre_t = lax.dot_general(
        weight_in, centered, (((1,), (1,)), ((), ())), preferred_element_type=jnp.float32
    )
    pre_t = pre_t + enc_bias[0][:, None]
    latent_t = jnp.maximum(pre_t, 0.0).astype(jnp.bfloat16)
    width = bias_dec.shape[0] // lat_size
    partial_sum = lax.dot_general(
        latent_t, decoder, (((0,), (0,)), ((), ())), preferred_element_type=jnp.float32
    )
    half = partial_sum.shape[0] // 2
    error_parts = []
    for rows, order in ((slice(0, half), first), (slice(half, None), second)):
        total, block = _halving_cols(partial_sum[rows], "lat", lat_size, order)
        start = block * width
        sample_cols = lax.dynamic_slice_in_dim(sample[rows], start, width, axis=1)
        bias_cols = lax.dynamic_slice_in_dim(bias_dec, start, width)
        keep_cols_f = lax.dynamic_slice_in_dim(keep, start, width)
        error_cols = (
            (total + bias_cols - sample_cols.astype(jnp.float32)) * keep_cols_f
        ).astype(jnp.bfloat16)
        stacked = _doubling_gather(error_cols, "lat", lat_size, order[::-1])
        error_parts.append(stacked[jnp.array(_block_owners(lat_size, order))])
    error_blocks = jnp.concatenate(error_parts, axis=1)
    error = jnp.transpose(error_blocks, (1, 0, 2)).reshape(error_blocks.shape[1], -1)
    back_t = lax.dot_general(
        decoder, error, (((1,), (1,)), ((), ())), preferred_element_type=jnp.float32
    )
    row_norm = jnp.sqrt(jnp.sum(jnp.square(decoder.astype(jnp.float32)), axis=1) + 1e-06)
    token_total = sample.shape[0]
    d_pre_t = (
        jnp.where(pre_t > 0, 2.0 * back_t + sparsity * row_norm[:, None], 0.0) / token_total
    ).astype(jnp.bfloat16)
    grad = jnp.dot(d_pre_t, centered, preferred_element_type=jnp.float32)
    moment_one = beta_one * first_moment[0].astype(jnp.float32) + (1.0 - beta_one) * grad
    moment_two = beta_two * second_moment[0].astype(jnp.float32) + (1.0 - beta_two) * grad * grad
    direction = moment_one / corr_one / (jnp.sqrt(moment_two / corr_two) + adam_eps)
    old = weight_in.astype(jnp.float32)
    updated = (old - rate_step * (direction + decay_rate * old)).astype(jnp.bfloat16)
    return (
        updated[None],
        moment_one.astype(jnp.bfloat16)[None],
        moment_two.astype(jnp.bfloat16)[None],
    )


LAT_SIZE = [8]


def solution(mesh):
    LAT_SIZE[0] = mesh.shape["lat"]
    return jax.shard_map(
        local,
        mesh=mesh,
        in_specs=(
            P(("groups", "seed"), "lat"),
            P(("groups", "seed"), None),
            P(("groups", "seed"), None),
            P(("groups", "seed"), "lat", None),
            P(("groups", "seed"), "lat"),
            P(("groups", "seed"), "lat", None),
            P(("groups", "seed"), None),
            P(("groups", "seed"), "lat", None),
            P(("groups", "seed"), "lat", None),
        ),
        out_specs=(
            P(("groups", "seed"), "lat", None),
            P(("groups", "seed"), "lat", None),
            P(("groups", "seed"), "lat", None),
        ),
        check_vma=False,
    )
```

```python
import jax
import jax.numpy as jnp
from jax import lax
from jax.sharding import PartitionSpec as P

sparsity = 0.2
beta_one = 0.9
beta_two = 0.95
corr_one = 1.0 - 0.9**10
corr_two = 1.0 - 0.95**10
adam_eps = 1e-08
rate_step = 0.001
decay_rate = 0.1


def _pair_swap(value, axis, mask, size):
    return lax.ppermute(value, axis, [(i, i ^ mask) for i in range(size)])


def _halving_sum(blocks, axis, size, order):
    nbits = size.bit_length() - 1
    me = lax.axis_index(axis)
    cur = blocks.reshape((2,) * nbits + blocks.shape[1:])
    bits = list(range(nbits - 1, -1, -1))
    for bit in order:
        pos = bits.index(bit)
        mine_bit = (me >> bit) & 1
        keep_part = lax.dynamic_index_in_dim(cur, mine_bit, pos, keepdims=False)
        send_part = lax.dynamic_index_in_dim(cur, 1 - mine_bit, pos, keepdims=False)
        cur = keep_part + _pair_swap(send_part, axis, 1 << bit, size)
        bits.pop(pos)
    return cur


def _doubling_gather(value, axis, size, order):
    me = lax.axis_index(axis)
    cur = value
    bits = []
    for bit in order:
        other = _pair_swap(cur, axis, 1 << bit, size)
        low_is_me = ((me >> bit) & 1) == 0
        low = jnp.where(low_is_me, cur, other)
        high = jnp.where(low_is_me, other, cur)
        cur = jnp.stack([low, high], axis=0)
        bits.insert(0, bit)
    want = sorted(bits, reverse=True)
    cur = jnp.transpose(cur, [bits.index(b) for b in want] + list(range(len(bits), cur.ndim)))
    return cur.reshape((size,) + value.shape)


def _direct_gather(value, axis, size):
    me = lax.axis_index(axis)
    parts = [value] + [
        lax.ppermute(value, axis, [(i, (i + k) % size) for i in range(size)])
        for k in range(1, size)
    ]
    stacked = jnp.stack(parts, axis=0)
    return jnp.take(stacked, (me - jnp.arange(size)) % size, axis=0)


def _orders(size):
    nbits = size.bit_length() - 1
    first = list(range(nbits))
    second = first[:]
    if nbits >= 2:
        second[0], second[1] = 1, 0
    return first, second


def _halving_cols(cols, axis, size, order):
    nbits = size.bit_length() - 1
    me = lax.axis_index(axis)
    cur = cols
    block = 0
    for step, bit in enumerate(order):
        half = cur.shape[1] // 2
        mine_bit = (me >> bit) & 1
        keep_part = lax.dynamic_slice_in_dim(cur, mine_bit * half, half, axis=1)
        send_part = lax.dynamic_slice_in_dim(cur, (1 - mine_bit) * half, half, axis=1)
        cur = keep_part + _pair_swap(send_part, axis, 1 << bit, size)
        block = block + (mine_bit << (nbits - 1 - step))
    return cur, block


def _block_owners(size, order):
    nbits = size.bit_length() - 1
    owned = [
        sum(((d >> bit) & 1) << (nbits - 1 - step) for step, bit in enumerate(order))
        for d in range(size)
    ]
    return [owned.index(k) for k in range(size)]


def _doubling_cols(cols, axis, size, order):
    me = lax.axis_index(axis)
    cur = cols
    for bit in order[::-1]:
        other = _pair_swap(cur, axis, 1 << bit, size)
        low_is_me = ((me >> bit) & 1) == 0
        low = jnp.where(low_is_me, cur, other)
        high = jnp.where(low_is_me, other, cur)
        cur = jnp.concatenate([low, high], axis=1)
    return cur


def local(
    activations,
    bag_rows,
    keep_cols,
    enc_weight,
    enc_bias,
    dec_weight,
    dec_bias,
    first_moment,
    second_moment,
):
    lat_size = LAT_SIZE[0]
    first, second = _orders(lat_size)
    if lat_size <= 8:
        act_blocks = _direct_gather(activations, "lat", lat_size)
    else:
        act_blocks = _doubling_gather(activations, "lat", lat_size, first[::-1])
    half_rows = jnp.transpose(act_blocks, (1, 0, 2)).reshape(activations.shape[0], -1)
    other_rows = lax.ppermute(half_rows, "seed", [(0, 1), (1, 0)])
    seed_first = lax.axis_index("seed") == 0
    gathered = jnp.concatenate(
        [jnp.where(seed_first, half_rows, other_rows), jnp.where(seed_first, other_rows, half_rows)],
        axis=0,
    )
    row_order = bag_rows[0]
    sample = jnp.take(gathered, row_order, axis=0)
    weight_in = enc_weight[0]
    decoder = dec_weight[0]
    bias_dec = dec_bias[0]
    keep = keep_cols[0].astype(jnp.float32)
    centered = (sample.astype(jnp.float32) - bias_dec).astype(jnp.bfloat16)
    pre_t = lax.dot_general(
        weight_in, centered, (((1,), (1,)), ((), ())), preferred_element_type=jnp.float32
    )
    pre_t = pre_t + enc_bias[0][:, None]
    latent_t = jnp.maximum(pre_t, 0.0).astype(jnp.bfloat16)
    width = bias_dec.shape[0] // lat_size
    partial_sum = lax.dot_general(
        latent_t, decoder, (((0,), (0,)), ((), ())), preferred_element_type=jnp.float32
    )
    half = partial_sum.shape[0] // 2
    error_parts = []
    for rows, order in ((slice(0, half), first), (slice(half, None), second)):
        total, block = _halving_cols(partial_sum[rows], "lat", lat_size, order)
        start = block * width
        sample_cols = lax.dynamic_slice_in_dim(sample[rows], start, width, axis=1)
        bias_cols = lax.dynamic_slice_in_dim(bias_dec, start, width)
        keep_cols_f = lax.dynamic_slice_in_dim(keep, start, width)
        error_cols = (
            (total + bias_cols - sample_cols.astype(jnp.float32)) * keep_cols_f
        ).astype(jnp.bfloat16)
        stacked = _doubling_gather(error_cols, "lat", lat_size, order[::-1])
        error_parts.append(stacked[jnp.array(_block_owners(lat_size, order))])
    error_blocks = jnp.concatenate(error_parts, axis=1)
    error = jnp.transpose(error_blocks, (1, 0, 2)).reshape(error_blocks.shape[1], -1)
    back_t = lax.dot_general(
        decoder, error, (((1,), (1,)), ((), ())), preferred_element_type=jnp.float32
    )
    row_norm = jnp.sqrt(jnp.sum(jnp.square(decoder.astype(jnp.float32)), axis=1) + 1e-06)
    token_total = sample.shape[0]
    d_pre_t = (
        jnp.where(pre_t > 0, 2.0 * back_t + sparsity * row_norm[:, None], 0.0) / token_total
    ).astype(jnp.bfloat16)
    grad = jnp.dot(d_pre_t, centered, preferred_element_type=jnp.float32)
    moment_one = beta_one * first_moment[0].astype(jnp.float32) + (1.0 - beta_one) * grad
    moment_two = beta_two * second_moment[0].astype(jnp.float32) + (1.0 - beta_two) * grad * grad
    direction = moment_one / corr_one / (jnp.sqrt(moment_two / corr_two) + adam_eps)
    old = weight_in.astype(jnp.float32)
    updated = (old - rate_step * (direction + decay_rate * old)).astype(jnp.bfloat16)
    return (
        updated[None],
        moment_one.astype(jnp.bfloat16)[None],
        moment_two.astype(jnp.bfloat16)[None],
    )


LAT_SIZE = [8]


def solution(mesh):
    LAT_SIZE[0] = mesh.shape["lat"]
    return jax.shard_map(
        local,
        mesh=mesh,
        in_specs=(
            P(("groups", "seed"), "lat"),
            P(("groups", "seed"), None),
            P(("groups", "seed"), None),
            P(("groups", "seed"), "lat", None),
            P(("groups", "seed"), "lat"),
            P(("groups", "seed"), "lat", None),
            P(("groups", "seed"), None),
            P(("groups", "seed"), "lat", None),
            P(("groups", "seed"), "lat", None),
        ),
        out_specs=(
            P(("groups", "seed"), "lat", None),
            P(("groups", "seed"), "lat", None),
            P(("groups", "seed"), "lat", None),
        ),
        check_vma=False,
    )
```

```python
import jax
import jax.numpy as jnp
from jax import lax
from jax.sharding import PartitionSpec as P
from jax.experimental import pallas as pl
from jax.experimental.pallas import tpu as pltpu

sparsity = 0.2
beta_one = 0.9
beta_two = 0.95
corr_one = 1.0 - 0.9**10
corr_two = 1.0 - 0.95**10
adam_eps = 1e-08
rate_step = 0.001
decay_rate = 0.1


def _tail_kernel(pre_ref, err_ref, cen_ref, dec_ref, enc_ref, m1_ref, m2_ref, w_out, m1_out, m2_out):
    dec = dec_ref[...]
    dec32 = dec.astype(jnp.float32)
    row_norm = jnp.sqrt(jnp.sum(dec32 * dec32, axis=1, keepdims=True) + 1e-06)
    back_t = lax.dot_general(
        dec, err_ref[...], (((1,), (1,)), ((), ())), preferred_element_type=jnp.float32
    )
    tokens = err_ref.shape[0]
    d_pre = (
        jnp.where(pre_ref[...] > 0, 2.0 * back_t + sparsity * row_norm, 0.0) / tokens
    ).astype(jnp.bfloat16)
    grad = jnp.dot(d_pre, cen_ref[...], preferred_element_type=jnp.float32)
    moment_one = beta_one * m1_ref[...].astype(jnp.float32) + (1.0 - beta_one) * grad
    moment_two = beta_two * m2_ref[...].astype(jnp.float32) + (1.0 - beta_two) * grad * grad
    direction = moment_one / corr_one / (jnp.sqrt(moment_two / corr_two) + adam_eps)
    old = enc_ref[...].astype(jnp.float32)
    w_out[...] = (old - rate_step * (direction + decay_rate * old)).astype(jnp.bfloat16)
    m1_out[...] = moment_one.astype(jnp.bfloat16)
    m2_out[...] = moment_two.astype(jnp.bfloat16)


def tail(pre_t, error, centered, decoder, weight_in, first, second, tile=256):
    n_lat, width = decoder.shape
    tokens = error.shape[0]
    row_block = pl.BlockSpec((tile, width), lambda i: (i, 0))
    whole = pl.BlockSpec((tokens, width), lambda i: (0, 0))
    out = jax.ShapeDtypeStruct((n_lat, width), jnp.bfloat16)
    return pl.pallas_call(
        _tail_kernel,
        grid=(n_lat // tile,),
        in_specs=[
            pl.BlockSpec((tile, tokens), lambda i: (i, 0)),
            whole,
            whole,
            row_block,
            row_block,
            row_block,
            row_block,
        ],
        out_specs=[row_block, row_block, row_block],
        out_shape=[out, out, out],
        compiler_params=pltpu.CompilerParams(vmem_limit_bytes=56 * 1024 * 1024),
    )(pre_t, error, centered, decoder, weight_in, first, second)


def _pair_swap(value, axis, mask, size):
    return lax.ppermute(value, axis, [(i, i ^ mask) for i in range(size)])


def _halving_sum(blocks, axis, size, order):
    nbits = size.bit_length() - 1
    me = lax.axis_index(axis)
    cur = blocks.reshape((2,) * nbits + blocks.shape[1:])
    bits = list(range(nbits - 1, -1, -1))
    for bit in order:
        pos = bits.index(bit)
        mine_bit = (me >> bit) & 1
        keep_part = lax.dynamic_index_in_dim(cur, mine_bit, pos, keepdims=False)
        send_part = lax.dynamic_index_in_dim(cur, 1 - mine_bit, pos, keepdims=False)
        cur = keep_part + _pair_swap(send_part, axis, 1 << bit, size)
        bits.pop(pos)
    return cur


def _doubling_gather(value, axis, size, order):
    me = lax.axis_index(axis)
    cur = value
    bits = []
    for bit in order:
        other = _pair_swap(cur, axis, 1 << bit, size)
        low_is_me = ((me >> bit) & 1) == 0
        low = jnp.where(low_is_me, cur, other)
        high = jnp.where(low_is_me, other, cur)
        cur = jnp.stack([low, high], axis=0)
        bits.insert(0, bit)
    want = sorted(bits, reverse=True)
    cur = jnp.transpose(cur, [bits.index(b) for b in want] + list(range(len(bits), cur.ndim)))
    return cur.reshape((size,) + value.shape)


def _direct_gather(value, axis, size):
    me = lax.axis_index(axis)
    parts = [value] + [
        lax.ppermute(value, axis, [(i, (i + k) % size) for i in range(size)])
        for k in range(1, size)
    ]
    stacked = jnp.stack(parts, axis=0)
    return jnp.take(stacked, (me - jnp.arange(size)) % size, axis=0)


def _orders(size):
    nbits = size.bit_length() - 1
    first = list(range(nbits))
    second = first[:]
    if nbits >= 2:
        second[0], second[1] = 1, 0
    return first, second


def _halving_cols(cols, axis, size, order):
    nbits = size.bit_length() - 1
    me = lax.axis_index(axis)
    cur = cols
    block = 0
    for step, bit in enumerate(order):
        half = cur.shape[1] // 2
        mine_bit = (me >> bit) & 1
        keep_part = lax.dynamic_slice_in_dim(cur, mine_bit * half, half, axis=1)
        send_part = lax.dynamic_slice_in_dim(cur, (1 - mine_bit) * half, half, axis=1)
        cur = keep_part + _pair_swap(send_part, axis, 1 << bit, size)
        block = block + (mine_bit << (nbits - 1 - step))
    return cur, block


def _block_owners(size, order):
    nbits = size.bit_length() - 1
    owned = [
        sum(((d >> bit) & 1) << (nbits - 1 - step) for step, bit in enumerate(order))
        for d in range(size)
    ]
    return [owned.index(k) for k in range(size)]


def _doubling_cols(cols, axis, size, order):
    me = lax.axis_index(axis)
    cur = cols
    for bit in order[::-1]:
        other = _pair_swap(cur, axis, 1 << bit, size)
        low_is_me = ((me >> bit) & 1) == 0
        low = jnp.where(low_is_me, cur, other)
        high = jnp.where(low_is_me, other, cur)
        cur = jnp.concatenate([low, high], axis=1)
    return cur


def local(
    activations,
    bag_rows,
    keep_cols,
    enc_weight,
    enc_bias,
    dec_weight,
    dec_bias,
    first_moment,
    second_moment,
):
    lat_size = LAT_SIZE[0]
    first, second = _orders(lat_size)
    if lat_size <= 8:
        act_blocks = _direct_gather(activations, "lat", lat_size)
    else:
        act_blocks = _doubling_gather(activations, "lat", lat_size, first[::-1])
    half_rows = jnp.transpose(act_blocks, (1, 0, 2)).reshape(activations.shape[0], -1)
    other_rows = lax.ppermute(half_rows, "seed", [(0, 1), (1, 0)])
    seed_first = lax.axis_index("seed") == 0
    gathered = jnp.concatenate(
        [jnp.where(seed_first, half_rows, other_rows), jnp.where(seed_first, other_rows, half_rows)],
        axis=0,
    )
    row_order = bag_rows[0]
    sample = jnp.take(gathered, row_order, axis=0)
    weight_in = enc_weight[0]
    decoder = dec_weight[0]
    bias_dec = dec_bias[0]
    keep = keep_cols[0].astype(jnp.float32)
    centered = (sample.astype(jnp.float32) - bias_dec).astype(jnp.bfloat16)
    pre_t = lax.dot_general(
        weight_in, centered, (((1,), (1,)), ((), ())), preferred_element_type=jnp.float32
    )
    pre_t = pre_t + enc_bias[0][:, None]
    latent_t = jnp.maximum(pre_t, 0.0).astype(jnp.bfloat16)
    width = bias_dec.shape[0] // lat_size
    partial_sum = lax.dot_general(
        latent_t, decoder, (((0,), (0,)), ((), ())), preferred_element_type=jnp.float32
    )
    half = partial_sum.shape[0] // 2
    error_parts = []
    for rows, order in ((slice(0, half), first), (slice(half, None), second)):
        total, block = _halving_cols(partial_sum[rows], "lat", lat_size, order)
        start = block * width
        sample_cols = lax.dynamic_slice_in_dim(sample[rows], start, width, axis=1)
        bias_cols = lax.dynamic_slice_in_dim(bias_dec, start, width)
        keep_cols_f = lax.dynamic_slice_in_dim(keep, start, width)
        error_cols = (
            (total + bias_cols - sample_cols.astype(jnp.float32)) * keep_cols_f
        ).astype(jnp.bfloat16)
        stacked = _doubling_gather(error_cols, "lat", lat_size, order[::-1])
        error_parts.append(stacked[jnp.array(_block_owners(lat_size, order))])
    error_blocks = jnp.concatenate(error_parts, axis=1)
    error = jnp.transpose(error_blocks, (1, 0, 2)).reshape(error_blocks.shape[1], -1)
    updated, moment_one, moment_two = tail(
        pre_t, error, centered, decoder, weight_in, first_moment[0], second_moment[0]
    )
    return updated[None], moment_one[None], moment_two[None]


LAT_SIZE = [8]


def solution(mesh):
    LAT_SIZE[0] = mesh.shape["lat"]
    return jax.shard_map(
        local,
        mesh=mesh,
        in_specs=(
            P(("groups", "seed"), "lat"),
            P(("groups", "seed"), None),
            P(("groups", "seed"), None),
            P(("groups", "seed"), "lat", None),
            P(("groups", "seed"), "lat"),
            P(("groups", "seed"), "lat", None),
            P(("groups", "seed"), None),
            P(("groups", "seed"), "lat", None),
            P(("groups", "seed"), "lat", None),
        ),
        out_specs=(
            P(("groups", "seed"), "lat", None),
            P(("groups", "seed"), "lat", None),
            P(("groups", "seed"), "lat", None),
        ),
        check_vma=False,
    )
```

```python
import jax
import jax.numpy as jnp
from jax import lax
from jax.sharding import PartitionSpec as P
from jax.experimental import pallas as pl
from jax.experimental.pallas import tpu as pltpu

sparsity = 0.2
beta_one = 0.9
beta_two = 0.95
corr_one = 1.0 - 0.9**10
corr_two = 1.0 - 0.95**10
adam_eps = 1e-08
rate_step = 0.001
decay_rate = 0.1


def _tail_kernel(pre_ref, err_ref, cen_ref, dec_ref, enc_ref, m1_ref, m2_ref, w_out, m1_out, m2_out):
    dec = dec_ref[...]
    dec32 = dec.astype(jnp.float32)
    row_norm = jnp.sqrt(jnp.sum(dec32 * dec32, axis=1, keepdims=True) + 1e-06)
    back_t = jnp.dot(dec, err_ref[...], preferred_element_type=jnp.float32)
    tokens = err_ref.shape[1]
    d_pre = (
        jnp.where(pre_ref[...] > 0, 2.0 * back_t + sparsity * row_norm, 0.0) / tokens
    ).astype(jnp.bfloat16)
    grad = jnp.dot(d_pre, cen_ref[...], preferred_element_type=jnp.float32)
    moment_one = beta_one * m1_ref[...].astype(jnp.float32) + (1.0 - beta_one) * grad
    moment_two = beta_two * m2_ref[...].astype(jnp.float32) + (1.0 - beta_two) * grad * grad
    direction = (moment_one * (1.0 / corr_one)) / (
        jnp.sqrt(moment_two * (1.0 / corr_two)) + adam_eps
    )
    old = enc_ref[...].astype(jnp.float32)
    w_out[...] = (old - rate_step * (direction + decay_rate * old)).astype(jnp.bfloat16)
    m1_out[...] = moment_one.astype(jnp.bfloat16)
    m2_out[...] = moment_two.astype(jnp.bfloat16)


def tail(pre_t, error, centered, decoder, weight_in, first, second, tile=256):
    n_lat, width = decoder.shape
    tokens = error.shape[0]
    error_t = error.T
    row_block = pl.BlockSpec((tile, width), lambda i: (i, 0))
    whole = pl.BlockSpec((tokens, width), lambda i: (0, 0))
    out = jax.ShapeDtypeStruct((n_lat, width), jnp.bfloat16)
    return pl.pallas_call(
        _tail_kernel,
        grid=(n_lat // tile,),
        in_specs=[
            pl.BlockSpec((tile, tokens), lambda i: (i, 0)),
            pl.BlockSpec((width, tokens), lambda i: (0, 0)),
            whole,
            row_block,
            row_block,
            row_block,
            row_block,
        ],
        out_specs=[row_block, row_block, row_block],
        out_shape=[out, out, out],
        compiler_params=pltpu.CompilerParams(vmem_limit_bytes=56 * 1024 * 1024),
    )(pre_t, error_t, centered, decoder, weight_in, first, second)


def _pair_swap(value, axis, mask, size):
    return lax.ppermute(value, axis, [(i, i ^ mask) for i in range(size)])


def _halving_sum(blocks, axis, size, order):
    nbits = size.bit_length() - 1
    me = lax.axis_index(axis)
    cur = blocks.reshape((2,) * nbits + blocks.shape[1:])
    bits = list(range(nbits - 1, -1, -1))
    for bit in order:
        pos = bits.index(bit)
        mine_bit = (me >> bit) & 1
        keep_part = lax.dynamic_index_in_dim(cur, mine_bit, pos, keepdims=False)
        send_part = lax.dynamic_index_in_dim(cur, 1 - mine_bit, pos, keepdims=False)
        cur = keep_part + _pair_swap(send_part, axis, 1 << bit, size)
        bits.pop(pos)
    return cur


def _doubling_gather(value, axis, size, order):
    me = lax.axis_index(axis)
    cur = value
    bits = []
    for bit in order:
        other = _pair_swap(cur, axis, 1 << bit, size)
        low_is_me = ((me >> bit) & 1) == 0
        low = jnp.where(low_is_me, cur, other)
        high = jnp.where(low_is_me, other, cur)
        cur = jnp.stack([low, high], axis=0)
        bits.insert(0, bit)
    want = sorted(bits, reverse=True)
    cur = jnp.transpose(cur, [bits.index(b) for b in want] + list(range(len(bits), cur.ndim)))
    return cur.reshape((size,) + value.shape)


def _direct_gather(value, axis, size):
    me = lax.axis_index(axis)
    parts = [value] + [
        lax.ppermute(value, axis, [(i, (i + k) % size) for i in range(size)])
        for k in range(1, size)
    ]
    stacked = jnp.stack(parts, axis=0)
    return jnp.take(stacked, (me - jnp.arange(size)) % size, axis=0)


def _orders(size):
    nbits = size.bit_length() - 1
    first = list(range(nbits))
    second = first[:]
    if nbits >= 2:
        second[0], second[1] = 1, 0
    return first, second


def _halving_cols(cols, axis, size, order):
    nbits = size.bit_length() - 1
    me = lax.axis_index(axis)
    cur = cols
    block = 0
    for step, bit in enumerate(order):
        half = cur.shape[1] // 2
        mine_bit = (me >> bit) & 1
        keep_part = lax.dynamic_slice_in_dim(cur, mine_bit * half, half, axis=1)
        send_part = lax.dynamic_slice_in_dim(cur, (1 - mine_bit) * half, half, axis=1)
        cur = keep_part + _pair_swap(send_part, axis, 1 << bit, size)
        block = block + (mine_bit << (nbits - 1 - step))
    return cur, block


def _block_owners(size, order):
    nbits = size.bit_length() - 1
    owned = [
        sum(((d >> bit) & 1) << (nbits - 1 - step) for step, bit in enumerate(order))
        for d in range(size)
    ]
    return [owned.index(k) for k in range(size)]


def _doubling_cols(cols, axis, size, order):
    me = lax.axis_index(axis)
    cur = cols
    for bit in order[::-1]:
        other = _pair_swap(cur, axis, 1 << bit, size)
        low_is_me = ((me >> bit) & 1) == 0
        low = jnp.where(low_is_me, cur, other)
        high = jnp.where(low_is_me, other, cur)
        cur = jnp.concatenate([low, high], axis=1)
    return cur


def local(
    activations,
    bag_rows,
    keep_cols,
    enc_weight,
    enc_bias,
    dec_weight,
    dec_bias,
    first_moment,
    second_moment,
):
    lat_size = LAT_SIZE[0]
    first, second = _orders(lat_size)
    if lat_size <= 8:
        act_blocks = _direct_gather(activations, "lat", lat_size)
    else:
        act_blocks = _doubling_gather(activations, "lat", lat_size, first[::-1])
    half_rows = jnp.transpose(act_blocks, (1, 0, 2)).reshape(activations.shape[0], -1)
    other_rows = lax.ppermute(half_rows, "seed", [(0, 1), (1, 0)])
    seed_first = lax.axis_index("seed") == 0
    gathered = jnp.concatenate(
        [jnp.where(seed_first, half_rows, other_rows), jnp.where(seed_first, other_rows, half_rows)],
        axis=0,
    )
    row_order = bag_rows[0]
    sample = jnp.take(gathered, row_order, axis=0)
    weight_in = enc_weight[0]
    decoder = dec_weight[0]
    bias_dec = dec_bias[0]
    keep = keep_cols[0].astype(jnp.float32)
    centered = (sample.astype(jnp.float32) - bias_dec).astype(jnp.bfloat16)
    pre_t = lax.dot_general(
        weight_in, centered, (((1,), (1,)), ((), ())), preferred_element_type=jnp.float32
    )
    pre_t = pre_t + enc_bias[0][:, None]
    latent_t = jnp.maximum(pre_t, 0.0).astype(jnp.bfloat16)
    width = bias_dec.shape[0] // lat_size
    partial_sum = lax.dot_general(
        latent_t, decoder, (((0,), (0,)), ((), ())), preferred_element_type=jnp.float32
    )
    half = partial_sum.shape[0] // 2
    error_parts = []
    for rows, order in ((slice(0, half), first), (slice(half, None), second)):
        total, block = _halving_cols(partial_sum[rows], "lat", lat_size, order)
        start = block * width
        sample_cols = lax.dynamic_slice_in_dim(sample[rows], start, width, axis=1)
        bias_cols = lax.dynamic_slice_in_dim(bias_dec, start, width)
        keep_cols_f = lax.dynamic_slice_in_dim(keep, start, width)
        error_cols = (
            (total + bias_cols - sample_cols.astype(jnp.float32)) * keep_cols_f
        ).astype(jnp.bfloat16)
        stacked = _doubling_gather(error_cols, "lat", lat_size, order[::-1])
        error_parts.append(stacked[jnp.array(_block_owners(lat_size, order))])
    error_blocks = jnp.concatenate(error_parts, axis=1)
    error = jnp.transpose(error_blocks, (1, 0, 2)).reshape(error_blocks.shape[1], -1)
    updated, moment_one, moment_two = tail(
        pre_t, error, centered, decoder, weight_in, first_moment[0], second_moment[0]
    )
    return updated[None], moment_one[None], moment_two[None]


LAT_SIZE = [8]


def solution(mesh):
    LAT_SIZE[0] = mesh.shape["lat"]
    return jax.shard_map(
        local,
        mesh=mesh,
        in_specs=(
            P(("groups", "seed"), "lat"),
            P(("groups", "seed"), None),
            P(("groups", "seed"), None),
            P(("groups", "seed"), "lat", None),
            P(("groups", "seed"), "lat"),
            P(("groups", "seed"), "lat", None),
            P(("groups", "seed"), None),
            P(("groups", "seed"), "lat", None),
            P(("groups", "seed"), "lat", None),
        ),
        out_specs=(
            P(("groups", "seed"), "lat", None),
            P(("groups", "seed"), "lat", None),
            P(("groups", "seed"), "lat", None),
        ),
        check_vma=False,
    )
```

```python
import jax
import jax.numpy as jnp
from jax import lax
from jax.sharding import PartitionSpec as P
from jax.experimental import pallas as pl
from jax.experimental.pallas import tpu as pltpu

sparsity = 0.2
beta_one = 0.9
beta_two = 0.95
corr_one = 1.0 - 0.9**10
corr_two = 1.0 - 0.95**10
adam_eps = 1e-08
rate_step = 0.001
decay_rate = 0.1


def _tail_kernel(
    pre_ref, norm_ref, err_ref, cen_ref, dec_ref, enc_ref, m1_ref, m2_ref, w_out, m1_out, m2_out
):
    row_norm = norm_ref[...]
    back_t = jnp.dot(dec_ref[...], err_ref[...], preferred_element_type=jnp.float32)
    tokens = err_ref.shape[1]
    d_pre = (
        jnp.where(pre_ref[...] > 0, 2.0 * back_t + sparsity * row_norm, 0.0) / tokens
    ).astype(jnp.bfloat16)
    grad = jnp.dot(d_pre, cen_ref[...], preferred_element_type=jnp.float32)
    moment_one = beta_one * m1_ref[...].astype(jnp.float32) + (1.0 - beta_one) * grad
    moment_two = beta_two * m2_ref[...].astype(jnp.float32) + (1.0 - beta_two) * grad * grad
    direction = moment_one / (
        jnp.sqrt(moment_two * (corr_one * corr_one / corr_two)) + corr_one * adam_eps
    )
    old = enc_ref[...].astype(jnp.float32)
    w_out[...] = (old * (1.0 - rate_step * decay_rate) - rate_step * direction).astype(
        jnp.bfloat16
    )
    m1_out[...] = moment_one.astype(jnp.bfloat16)
    m2_out[...] = moment_two.astype(jnp.bfloat16)


def tail(pre_t, row_norm, error, centered, decoder, weight_in, first, second, tile=256):
    n_lat, width = decoder.shape
    tokens = error.shape[0]
    error_t = error.T
    row_block = pl.BlockSpec((tile, width), lambda i: (i, 0))
    whole = pl.BlockSpec((tokens, width), lambda i: (0, 0))
    out = jax.ShapeDtypeStruct((n_lat, width), jnp.bfloat16)
    return pl.pallas_call(
        _tail_kernel,
        grid=(n_lat // tile,),
        in_specs=[
            pl.BlockSpec((tile, tokens), lambda i: (i, 0)),
            pl.BlockSpec((tile, 1), lambda i: (i, 0)),
            pl.BlockSpec((width, tokens), lambda i: (0, 0)),
            whole,
            row_block,
            row_block,
            row_block,
            row_block,
        ],
        out_specs=[row_block, row_block, row_block],
        out_shape=[out, out, out],
        compiler_params=pltpu.CompilerParams(vmem_limit_bytes=56 * 1024 * 1024),
    )(pre_t, row_norm, error_t, centered, decoder, weight_in, first, second)


def _pair_swap(value, axis, mask, size):
    return lax.ppermute(value, axis, [(i, i ^ mask) for i in range(size)])


def _halving_sum(blocks, axis, size, order):
    nbits = size.bit_length() - 1
    me = lax.axis_index(axis)
    cur = blocks.reshape((2,) * nbits + blocks.shape[1:])
    bits = list(range(nbits - 1, -1, -1))
    for bit in order:
        pos = bits.index(bit)
        mine_bit = (me >> bit) & 1
        keep_part = lax.dynamic_index_in_dim(cur, mine_bit, pos, keepdims=False)
        send_part = lax.dynamic_index_in_dim(cur, 1 - mine_bit, pos, keepdims=False)
        cur = keep_part + _pair_swap(send_part, axis, 1 << bit, size)
        bits.pop(pos)
    return cur


def _doubling_gather(value, axis, size, order):
    me = lax.axis_index(axis)
    cur = value
    bits = []
    for bit in order:
        other = _pair_swap(cur, axis, 1 << bit, size)
        low_is_me = ((me >> bit) & 1) == 0
        low = jnp.where(low_is_me, cur, other)
        high = jnp.where(low_is_me, other, cur)
        cur = jnp.stack([low, high], axis=0)
        bits.insert(0, bit)
    want = sorted(bits, reverse=True)
    cur = jnp.transpose(cur, [bits.index(b) for b in want] + list(range(len(bits), cur.ndim)))
    return cur.reshape((size,) + value.shape)


def _direct_gather(value, axis, size):
    me = lax.axis_index(axis)
    parts = [value] + [
        lax.ppermute(value, axis, [(i, (i + k) % size) for i in range(size)])
        for k in range(1, size)
    ]
    stacked = jnp.stack(parts, axis=0)
    return jnp.take(stacked, (me - jnp.arange(size)) % size, axis=0)


def _orders(size):
    nbits = size.bit_length() - 1
    first = list(range(nbits))
    second = first[:]
    if nbits >= 2:
        second[0], second[1] = 1, 0
    return first, second


def _halving_cols(cols, axis, size, order):
    nbits = size.bit_length() - 1
    me = lax.axis_index(axis)
    cur = cols
    block = 0
    for step, bit in enumerate(order):
        half = cur.shape[1] // 2
        mine_bit = (me >> bit) & 1
        keep_part = lax.dynamic_slice_in_dim(cur, mine_bit * half, half, axis=1)
        send_part = lax.dynamic_slice_in_dim(cur, (1 - mine_bit) * half, half, axis=1)
        cur = keep_part + _pair_swap(send_part, axis, 1 << bit, size)
        block = block + (mine_bit << (nbits - 1 - step))
    return cur, block


def _block_owners(size, order):
    nbits = size.bit_length() - 1
    owned = [
        sum(((d >> bit) & 1) << (nbits - 1 - step) for step, bit in enumerate(order))
        for d in range(size)
    ]
    return [owned.index(k) for k in range(size)]


def _doubling_cols(cols, axis, size, order):
    me = lax.axis_index(axis)
    cur = cols
    for bit in order[::-1]:
        other = _pair_swap(cur, axis, 1 << bit, size)
        low_is_me = ((me >> bit) & 1) == 0
        low = jnp.where(low_is_me, cur, other)
        high = jnp.where(low_is_me, other, cur)
        cur = jnp.concatenate([low, high], axis=1)
    return cur


def local(
    activations,
    bag_rows,
    keep_cols,
    enc_weight,
    enc_bias,
    dec_weight,
    dec_bias,
    first_moment,
    second_moment,
):
    lat_size = LAT_SIZE[0]
    first, second = _orders(lat_size)
    if lat_size <= 8:
        act_blocks = _direct_gather(activations, "lat", lat_size)
    else:
        act_blocks = _doubling_gather(activations, "lat", lat_size, first[::-1])
    half_rows = jnp.transpose(act_blocks, (1, 0, 2)).reshape(activations.shape[0], -1)
    other_rows = lax.ppermute(half_rows, "seed", [(0, 1), (1, 0)])
    seed_first = lax.axis_index("seed") == 0
    gathered = jnp.concatenate(
        [jnp.where(seed_first, half_rows, other_rows), jnp.where(seed_first, other_rows, half_rows)],
        axis=0,
    )
    row_order = bag_rows[0]
    sample = jnp.take(gathered, row_order, axis=0)
    weight_in = enc_weight[0]
    decoder = dec_weight[0]
    bias_dec = dec_bias[0]
    keep = keep_cols[0].astype(jnp.float32)
    centered = (sample.astype(jnp.float32) - bias_dec).astype(jnp.bfloat16)
    pre_t = lax.dot_general(
        weight_in, centered, (((1,), (1,)), ((), ())), preferred_element_type=jnp.float32
    )
    pre_t = pre_t + enc_bias[0][:, None]
    latent_t = jnp.maximum(pre_t, 0.0).astype(jnp.bfloat16)
    width = bias_dec.shape[0] // lat_size
    partial_sum = lax.dot_general(
        latent_t, decoder, (((0,), (0,)), ((), ())), preferred_element_type=jnp.float32
    )
    half = partial_sum.shape[0] // 2
    error_parts = []
    for rows, order in ((slice(0, half), first), (slice(half, None), second)):
        total, block = _halving_cols(partial_sum[rows], "lat", lat_size, order)
        start = block * width
        sample_cols = lax.dynamic_slice_in_dim(sample[rows], start, width, axis=1)
        bias_cols = lax.dynamic_slice_in_dim(bias_dec, start, width)
        keep_cols_f = lax.dynamic_slice_in_dim(keep, start, width)
        error_cols = (
            (total + bias_cols - sample_cols.astype(jnp.float32)) * keep_cols_f
        ).astype(jnp.bfloat16)
        stacked = _doubling_gather(error_cols, "lat", lat_size, order[::-1])
        error_parts.append(stacked[jnp.array(_block_owners(lat_size, order))])
    error_blocks = jnp.concatenate(error_parts, axis=1)
    error = jnp.transpose(error_blocks, (1, 0, 2)).reshape(error_blocks.shape[1], -1)
    row_norm = jnp.sqrt(jnp.sum(jnp.square(decoder.astype(jnp.float32)), axis=1) + 1e-06)
    updated, moment_one, moment_two = tail(
        pre_t, row_norm[:, None], error, centered, decoder, weight_in, first_moment[0], second_moment[0]
    )
    return updated[None], moment_one[None], moment_two[None]


LAT_SIZE = [8]


def solution(mesh):
    LAT_SIZE[0] = mesh.shape["lat"]
    return jax.shard_map(
        local,
        mesh=mesh,
        in_specs=(
            P(("groups", "seed"), "lat"),
            P(("groups", "seed"), None),
            P(("groups", "seed"), None),
            P(("groups", "seed"), "lat", None),
            P(("groups", "seed"), "lat"),
            P(("groups", "seed"), "lat", None),
            P(("groups", "seed"), None),
            P(("groups", "seed"), "lat", None),
            P(("groups", "seed"), "lat", None),
        ),
        out_specs=(
            P(("groups", "seed"), "lat", None),
            P(("groups", "seed"), "lat", None),
            P(("groups", "seed"), "lat", None),
        ),
        check_vma=False,
    )
```

```python
import jax
import jax.numpy as jnp
from jax import lax
from jax.sharding import PartitionSpec as P
from jax.experimental import pallas as pl
from jax.experimental.pallas import tpu as pltpu

sparsity = 0.2
beta_one = 0.9
beta_two = 0.95
corr_one = 1.0 - 0.9**10
corr_two = 1.0 - 0.95**10
adam_eps = 1e-08
rate_step = 0.001
decay_rate = 0.1


def _tail_kernel(
    pre_ref, err_ref, cen_ref, dec_ref, enc_ref, m1_ref, m2_ref, w_out, m1_out, m2_out
):
    dec = dec_ref[...]
    dec32 = dec.astype(jnp.float32)
    row_norm = jnp.sqrt(jnp.sum(dec32 * dec32, axis=1, keepdims=True) + 1e-06)
    back_t = jnp.dot(dec, err_ref[...], preferred_element_type=jnp.float32)
    tokens = err_ref.shape[1]
    d_pre = (
        jnp.where(pre_ref[...] > 0, 2.0 * back_t + sparsity * row_norm, 0.0) / tokens
    ).astype(jnp.bfloat16)
    grad = jnp.dot(d_pre, cen_ref[...], preferred_element_type=jnp.float32)
    moment_one = beta_one * m1_ref[...].astype(jnp.float32) + (1.0 - beta_one) * grad
    moment_two = beta_two * m2_ref[...].astype(jnp.float32) + (1.0 - beta_two) * grad * grad
    direction = moment_one / (
        jnp.sqrt(moment_two * (corr_one * corr_one / corr_two)) + corr_one * adam_eps
    )
    old = enc_ref[...].astype(jnp.float32)
    w_out[...] = (old * (1.0 - rate_step * decay_rate) - rate_step * direction).astype(
        jnp.bfloat16
    )
    m1_out[...] = moment_one.astype(jnp.bfloat16)
    m2_out[...] = moment_two.astype(jnp.bfloat16)


def tail(pre_t, error, centered, decoder, weight_in, first, second, tile=256):
    n_lat, width = decoder.shape
    tokens = error.shape[0]
    error_t = error.T
    row_block = pl.BlockSpec((tile, width), lambda i: (i, 0))
    whole = pl.BlockSpec((tokens, width), lambda i: (0, 0))
    out = jax.ShapeDtypeStruct((n_lat, width), jnp.bfloat16)
    return pl.pallas_call(
        _tail_kernel,
        grid=(n_lat // tile,),
        in_specs=[
            pl.BlockSpec((tile, tokens), lambda i: (i, 0)),
            pl.BlockSpec((width, tokens), lambda i: (0, 0)),
            whole,
            row_block,
            row_block,
            row_block,
            row_block,
        ],
        out_specs=[row_block, row_block, row_block],
        out_shape=[out, out, out],
        compiler_params=pltpu.CompilerParams(vmem_limit_bytes=56 * 1024 * 1024),
    )(pre_t, error_t, centered, decoder, weight_in, first, second)


def _pair_swap(value, axis, mask, size):
    return lax.ppermute(value, axis, [(i, i ^ mask) for i in range(size)])


def _halving_sum(blocks, axis, size, order):
    nbits = size.bit_length() - 1
    me = lax.axis_index(axis)
    cur = blocks.reshape((2,) * nbits + blocks.shape[1:])
    bits = list(range(nbits - 1, -1, -1))
    for bit in order:
        pos = bits.index(bit)
        mine_bit = (me >> bit) & 1
        keep_part = lax.dynamic_index_in_dim(cur, mine_bit, pos, keepdims=False)
        send_part = lax.dynamic_index_in_dim(cur, 1 - mine_bit, pos, keepdims=False)
        cur = keep_part + _pair_swap(send_part, axis, 1 << bit, size)
        bits.pop(pos)
    return cur


def _doubling_gather(value, axis, size, order):
    me = lax.axis_index(axis)
    cur = value
    bits = []
    for bit in order:
        other = _pair_swap(cur, axis, 1 << bit, size)
        low_is_me = ((me >> bit) & 1) == 0
        low = jnp.where(low_is_me, cur, other)
        high = jnp.where(low_is_me, other, cur)
        cur = jnp.stack([low, high], axis=0)
        bits.insert(0, bit)
    want = sorted(bits, reverse=True)
    cur = jnp.transpose(cur, [bits.index(b) for b in want] + list(range(len(bits), cur.ndim)))
    return cur.reshape((size,) + value.shape)


def _direct_gather(value, axis, size):
    me = lax.axis_index(axis)
    parts = [value] + [
        lax.ppermute(value, axis, [(i, (i + k) % size) for i in range(size)])
        for k in range(1, size)
    ]
    stacked = jnp.stack(parts, axis=0)
    return jnp.take(stacked, (me - jnp.arange(size)) % size, axis=0)


def _orders(size):
    nbits = size.bit_length() - 1
    first = list(range(nbits))
    second = first[:]
    if nbits >= 2:
        second[0], second[1] = 1, 0
    return first, second


def _halving_cols(cols, axis, size, order):
    nbits = size.bit_length() - 1
    me = lax.axis_index(axis)
    cur = cols
    block = 0
    for step, bit in enumerate(order):
        half = cur.shape[1] // 2
        mine_bit = (me >> bit) & 1
        keep_part = lax.dynamic_slice_in_dim(cur, mine_bit * half, half, axis=1)
        send_part = lax.dynamic_slice_in_dim(cur, (1 - mine_bit) * half, half, axis=1)
        cur = keep_part + _pair_swap(send_part, axis, 1 << bit, size)
        block = block + (mine_bit << (nbits - 1 - step))
    return cur, block


def _block_owners(size, order):
    nbits = size.bit_length() - 1
    owned = [
        sum(((d >> bit) & 1) << (nbits - 1 - step) for step, bit in enumerate(order))
        for d in range(size)
    ]
    return [owned.index(k) for k in range(size)]


def _doubling_cols(cols, axis, size, order):
    me = lax.axis_index(axis)
    cur = cols
    for bit in order[::-1]:
        other = _pair_swap(cur, axis, 1 << bit, size)
        low_is_me = ((me >> bit) & 1) == 0
        low = jnp.where(low_is_me, cur, other)
        high = jnp.where(low_is_me, other, cur)
        cur = jnp.concatenate([low, high], axis=1)
    return cur


def local(
    activations,
    bag_rows,
    keep_cols,
    enc_weight,
    enc_bias,
    dec_weight,
    dec_bias,
    first_moment,
    second_moment,
):
    lat_size = LAT_SIZE[0]
    first, second = _orders(lat_size)
    copies = jnp.broadcast_to(activations[None], (lat_size,) + activations.shape)
    act_blocks = lax.all_to_all(copies, "lat", 0, 0, tiled=True)
    half_rows = jnp.transpose(act_blocks, (1, 0, 2)).reshape(activations.shape[0], -1)
    other_rows = lax.ppermute(half_rows, "seed", [(0, 1), (1, 0)])
    seed_first = lax.axis_index("seed") == 0
    gathered = jnp.concatenate(
        [jnp.where(seed_first, half_rows, other_rows), jnp.where(seed_first, other_rows, half_rows)],
        axis=0,
    )
    row_order = bag_rows[0]
    sample = jnp.take(gathered, row_order, axis=0)
    weight_in = enc_weight[0]
    decoder = dec_weight[0]
    bias_dec = dec_bias[0]
    keep = keep_cols[0].astype(jnp.float32)
    centered = (sample.astype(jnp.float32) - bias_dec).astype(jnp.bfloat16)
    pre_t = lax.dot_general(
        weight_in, centered, (((1,), (1,)), ((), ())), preferred_element_type=jnp.float32
    )
    pre_t = pre_t + enc_bias[0][:, None]
    latent_t = jnp.maximum(pre_t, 0.0).astype(jnp.bfloat16)
    width = bias_dec.shape[0] // lat_size
    partial_sum = lax.dot_general(
        latent_t, decoder, (((0,), (0,)), ((), ())), preferred_element_type=jnp.float32
    )
    half = partial_sum.shape[0] // 2
    error_parts = []
    for rows, order in ((slice(0, half), first), (slice(half, None), second)):
        total, block = _halving_cols(partial_sum[rows], "lat", lat_size, order)
        start = block * width
        sample_cols = lax.dynamic_slice_in_dim(sample[rows], start, width, axis=1)
        bias_cols = lax.dynamic_slice_in_dim(bias_dec, start, width)
        keep_cols_f = lax.dynamic_slice_in_dim(keep, start, width)
        error_cols = (
            (total + bias_cols - sample_cols.astype(jnp.float32)) * keep_cols_f
        ).astype(jnp.bfloat16)
        stacked = _doubling_gather(error_cols, "lat", lat_size, order[::-1])
        error_parts.append(stacked[jnp.array(_block_owners(lat_size, order))])
    error_blocks = jnp.concatenate(error_parts, axis=1)
    error = jnp.transpose(error_blocks, (1, 0, 2)).reshape(error_blocks.shape[1], -1)
    updated, moment_one, moment_two = tail(
        pre_t, error, centered, decoder, weight_in, first_moment[0], second_moment[0]
    )
    return updated[None], moment_one[None], moment_two[None]


LAT_SIZE = [8]


def solution(mesh):
    LAT_SIZE[0] = mesh.shape["lat"]
    return jax.shard_map(
        local,
        mesh=mesh,
        in_specs=(
            P(("groups", "seed"), "lat"),
            P(("groups", "seed"), None),
            P(("groups", "seed"), None),
            P(("groups", "seed"), "lat", None),
            P(("groups", "seed"), "lat"),
            P(("groups", "seed"), "lat", None),
            P(("groups", "seed"), None),
            P(("groups", "seed"), "lat", None),
            P(("groups", "seed"), "lat", None),
        ),
        out_specs=(
            P(("groups", "seed"), "lat", None),
            P(("groups", "seed"), "lat", None),
            P(("groups", "seed"), "lat", None),
        ),
        check_vma=False,
    )
```

```python
import jax
import jax.numpy as jnp
from jax import lax
from jax.sharding import PartitionSpec as P
from jax.experimental import pallas as pl
from jax.experimental.pallas import tpu as pltpu

sparsity = 0.2
beta_one = 0.9
beta_two = 0.95
corr_one = 1.0 - 0.9**10
corr_two = 1.0 - 0.95**10
adam_eps = 1e-08
rate_step = 0.001
decay_rate = 0.1


def _tail_kernel(
    pre_ref, err_ref, cen_ref, dec_ref, enc_ref, m1_ref, m2_ref, w_out, m1_out, m2_out
):
    dec = dec_ref[...]
    dec32 = dec.astype(jnp.float32)
    row_norm = jnp.sqrt(jnp.sum(dec32 * dec32, axis=1, keepdims=True) + 1e-06)
    back_t = jnp.dot(dec, err_ref[...], preferred_element_type=jnp.float32)
    tokens = err_ref.shape[1]
    d_pre = (
        jnp.where(pre_ref[...] > 0, 2.0 * back_t + sparsity * row_norm, 0.0) / tokens
    ).astype(jnp.bfloat16)
    grad = jnp.dot(d_pre, cen_ref[...], preferred_element_type=jnp.float32)
    moment_one = beta_one * m1_ref[...].astype(jnp.float32) + (1.0 - beta_one) * grad
    moment_two = beta_two * m2_ref[...].astype(jnp.float32) + (1.0 - beta_two) * grad * grad
    direction = moment_one / (
        jnp.sqrt(moment_two * (corr_one * corr_one / corr_two)) + corr_one * adam_eps
    )
    old = enc_ref[...].astype(jnp.float32)
    w_out[...] = (old * (1.0 - rate_step * decay_rate) - rate_step * direction).astype(
        jnp.bfloat16
    )
    m1_out[...] = moment_one.astype(jnp.bfloat16)
    m2_out[...] = moment_two.astype(jnp.bfloat16)


def tail(pre_t, error, centered, decoder, weight_in, first, second, tile=256):
    n_lat, width = decoder.shape
    tokens = error.shape[0]
    error_t = error.T
    row_block = pl.BlockSpec((tile, width), lambda i: (i, 0))
    whole = pl.BlockSpec((tokens, width), lambda i: (0, 0))
    out = jax.ShapeDtypeStruct((n_lat, width), jnp.bfloat16)
    return pl.pallas_call(
        _tail_kernel,
        grid=(n_lat // tile,),
        in_specs=[
            pl.BlockSpec((tile, tokens), lambda i: (i, 0)),
            pl.BlockSpec((width, tokens), lambda i: (0, 0)),
            whole,
            row_block,
            row_block,
            row_block,
            row_block,
        ],
        out_specs=[row_block, row_block, row_block],
        out_shape=[out, out, out],
        compiler_params=pltpu.CompilerParams(vmem_limit_bytes=56 * 1024 * 1024),
    )(pre_t, error_t, centered, decoder, weight_in, first, second)


def _pair_swap(value, axis, mask, size):
    return lax.ppermute(value, axis, [(i, i ^ mask) for i in range(size)])


def _halving_sum(blocks, axis, size, order):
    nbits = size.bit_length() - 1
    me = lax.axis_index(axis)
    cur = blocks.reshape((2,) * nbits + blocks.shape[1:])
    bits = list(range(nbits - 1, -1, -1))
    for bit in order:
        pos = bits.index(bit)
        mine_bit = (me >> bit) & 1
        keep_part = lax.dynamic_index_in_dim(cur, mine_bit, pos, keepdims=False)
        send_part = lax.dynamic_index_in_dim(cur, 1 - mine_bit, pos, keepdims=False)
        cur = keep_part + _pair_swap(send_part, axis, 1 << bit, size)
        bits.pop(pos)
    return cur


def _doubling_gather(value, axis, size, order):
    me = lax.axis_index(axis)
    cur = value
    bits = []
    for bit in order:
        other = _pair_swap(cur, axis, 1 << bit, size)
        low_is_me = ((me >> bit) & 1) == 0
        low = jnp.where(low_is_me, cur, other)
        high = jnp.where(low_is_me, other, cur)
        cur = jnp.stack([low, high], axis=0)
        bits.insert(0, bit)
    want = sorted(bits, reverse=True)
    cur = jnp.transpose(cur, [bits.index(b) for b in want] + list(range(len(bits), cur.ndim)))
    return cur.reshape((size,) + value.shape)


def _direct_gather(value, axis, size):
    me = lax.axis_index(axis)
    parts = [value] + [
        lax.ppermute(value, axis, [(i, (i + k) % size) for i in range(size)])
        for k in range(1, size)
    ]
    stacked = jnp.stack(parts, axis=0)
    return jnp.take(stacked, (me - jnp.arange(size)) % size, axis=0)


def _orders(size):
    nbits = size.bit_length() - 1
    first = list(range(nbits))
    second = first[:]
    if nbits >= 2:
        second[0], second[1] = 1, 0
    return first, second


def _halving_cols(cols, axis, size, order):
    nbits = size.bit_length() - 1
    me = lax.axis_index(axis)
    cur = cols
    block = 0
    for step, bit in enumerate(order):
        half = cur.shape[1] // 2
        mine_bit = (me >> bit) & 1
        keep_part = lax.dynamic_slice_in_dim(cur, mine_bit * half, half, axis=1)
        send_part = lax.dynamic_slice_in_dim(cur, (1 - mine_bit) * half, half, axis=1)
        cur = keep_part + _pair_swap(send_part, axis, 1 << bit, size)
        block = block + (mine_bit << (nbits - 1 - step))
    return cur, block


def _block_owners(size, order):
    nbits = size.bit_length() - 1
    owned = [
        sum(((d >> bit) & 1) << (nbits - 1 - step) for step, bit in enumerate(order))
        for d in range(size)
    ]
    return [owned.index(k) for k in range(size)]


def _doubling_cols(cols, axis, size, order):
    me = lax.axis_index(axis)
    cur = cols
    for bit in order[::-1]:
        other = _pair_swap(cur, axis, 1 << bit, size)
        low_is_me = ((me >> bit) & 1) == 0
        low = jnp.where(low_is_me, cur, other)
        high = jnp.where(low_is_me, other, cur)
        cur = jnp.concatenate([low, high], axis=1)
    return cur


def local(
    activations,
    bag_rows,
    keep_cols,
    enc_weight,
    enc_bias,
    dec_weight,
    dec_bias,
    first_moment,
    second_moment,
):
    lat_size = LAT_SIZE[0]
    first, second = _orders(lat_size)
    copies = jnp.broadcast_to(activations[None], (lat_size,) + activations.shape)
    act_blocks = lax.all_to_all(copies, "lat", 0, 0, tiled=True)
    half_rows = jnp.transpose(act_blocks, (1, 0, 2)).reshape(activations.shape[0], -1)
    other_rows = lax.ppermute(half_rows, "seed", [(0, 1), (1, 0)])
    seed_first = lax.axis_index("seed") == 0
    gathered = jnp.concatenate(
        [jnp.where(seed_first, half_rows, other_rows), jnp.where(seed_first, other_rows, half_rows)],
        axis=0,
    )
    row_order = bag_rows[0]
    sample = jnp.take(gathered, row_order, axis=0)
    weight_in = enc_weight[0]
    decoder = dec_weight[0]
    bias_dec = dec_bias[0]
    keep = keep_cols[0].astype(jnp.float32)
    centered = (sample.astype(jnp.float32) - bias_dec).astype(jnp.bfloat16)
    pre_t = lax.dot_general(
        weight_in, centered, (((1,), (1,)), ((), ())), preferred_element_type=jnp.float32
    )
    pre_t = pre_t + enc_bias[0][:, None]
    latent_t = jnp.maximum(pre_t, 0.0).astype(jnp.bfloat16)
    width = bias_dec.shape[0] // lat_size
    partial_sum = lax.dot_general(
        latent_t, decoder, (((0,), (0,)), ((), ())), preferred_element_type=jnp.float32
    )
    chunk = partial_sum.shape[0] // 4
    error_parts = []
    for part in range(4):
        rows = slice(part * chunk, (part + 1) * chunk)
        order = (first, second)[part % 2]
        total, block = _halving_cols(partial_sum[rows], "lat", lat_size, order)
        start = block * width
        sample_cols = lax.dynamic_slice_in_dim(sample[rows], start, width, axis=1)
        bias_cols = lax.dynamic_slice_in_dim(bias_dec, start, width)
        keep_cols_f = lax.dynamic_slice_in_dim(keep, start, width)
        error_cols = (
            (total + bias_cols - sample_cols.astype(jnp.float32)) * keep_cols_f
        ).astype(jnp.bfloat16)
        stacked = _doubling_gather(error_cols, "lat", lat_size, order[::-1])
        error_parts.append(stacked[jnp.array(_block_owners(lat_size, order))])
    error_blocks = jnp.concatenate(error_parts, axis=1)
    error = jnp.transpose(error_blocks, (1, 0, 2)).reshape(error_blocks.shape[1], -1)
    updated, moment_one, moment_two = tail(
        pre_t, error, centered, decoder, weight_in, first_moment[0], second_moment[0]
    )
    return updated[None], moment_one[None], moment_two[None]


LAT_SIZE = [8]


def solution(mesh):
    LAT_SIZE[0] = mesh.shape["lat"]
    return jax.shard_map(
        local,
        mesh=mesh,
        in_specs=(
            P(("groups", "seed"), "lat"),
            P(("groups", "seed"), None),
            P(("groups", "seed"), None),
            P(("groups", "seed"), "lat", None),
            P(("groups", "seed"), "lat"),
            P(("groups", "seed"), "lat", None),
            P(("groups", "seed"), None),
            P(("groups", "seed"), "lat", None),
            P(("groups", "seed"), "lat", None),
        ),
        out_specs=(
            P(("groups", "seed"), "lat", None),
            P(("groups", "seed"), "lat", None),
            P(("groups", "seed"), "lat", None),
        ),
        check_vma=False,
    )
```

```python
import jax
import jax.numpy as jnp
from jax import lax
from jax.sharding import PartitionSpec as P
from jax.experimental import pallas as pl
from jax.experimental.pallas import tpu as pltpu

sparsity = 0.2
beta_one = 0.9
beta_two = 0.95
corr_one = 1.0 - 0.9**10
corr_two = 1.0 - 0.95**10
adam_eps = 1e-08
rate_step = 0.001
decay_rate = 0.1


def _tail_kernel(
    pre_ref, err_ref, cen_ref, dec_ref, enc_ref, m1_ref, m2_ref, w_out, m1_out, m2_out
):
    dec = dec_ref[...]
    dec32 = dec.astype(jnp.float32)
    row_norm = jnp.sqrt(jnp.sum(dec32 * dec32, axis=1, keepdims=True) + 1e-06)
    back_t = jnp.dot(dec, err_ref[...], preferred_element_type=jnp.float32)
    tokens = err_ref.shape[1]
    d_pre = (
        jnp.where(pre_ref[...] > 0, 2.0 * back_t + sparsity * row_norm, 0.0) / tokens
    ).astype(jnp.bfloat16)
    grad = jnp.dot(d_pre, cen_ref[...], preferred_element_type=jnp.float32)
    moment_one = beta_one * m1_ref[...].astype(jnp.float32) + (1.0 - beta_one) * grad
    moment_two = beta_two * m2_ref[...].astype(jnp.float32) + (1.0 - beta_two) * grad * grad
    direction = moment_one / (
        jnp.sqrt(moment_two * (corr_one * corr_one / corr_two)) + corr_one * adam_eps
    )
    old = enc_ref[...].astype(jnp.float32)
    w_out[...] = (old * (1.0 - rate_step * decay_rate) - rate_step * direction).astype(
        jnp.bfloat16
    )
    m1_out[...] = moment_one.astype(jnp.bfloat16)
    m2_out[...] = moment_two.astype(jnp.bfloat16)


def tail(pre_t, error, centered, decoder, weight_in, first, second, tile=256):
    n_lat, width = decoder.shape
    tokens = error.shape[0]
    error_t = error.T
    row_block = pl.BlockSpec((tile, width), lambda i: (i, 0))
    whole = pl.BlockSpec((tokens, width), lambda i: (0, 0))
    out = jax.ShapeDtypeStruct((n_lat, width), jnp.bfloat16)
    return pl.pallas_call(
        _tail_kernel,
        grid=(n_lat // tile,),
        in_specs=[
            pl.BlockSpec((tile, tokens), lambda i: (i, 0)),
            pl.BlockSpec((width, tokens), lambda i: (0, 0)),
            whole,
            row_block,
            row_block,
            row_block,
            row_block,
        ],
        out_specs=[row_block, row_block, row_block],
        out_shape=[out, out, out],
        compiler_params=pltpu.CompilerParams(vmem_limit_bytes=56 * 1024 * 1024),
    )(pre_t, error_t, centered, decoder, weight_in, first, second)


def _pair_swap(value, axis, mask, size):
    return lax.ppermute(value, axis, [(i, i ^ mask) for i in range(size)])


def _halving_sum(blocks, axis, size, order):
    nbits = size.bit_length() - 1
    me = lax.axis_index(axis)
    cur = blocks.reshape((2,) * nbits + blocks.shape[1:])
    bits = list(range(nbits - 1, -1, -1))
    for bit in order:
        pos = bits.index(bit)
        mine_bit = (me >> bit) & 1
        keep_part = lax.dynamic_index_in_dim(cur, mine_bit, pos, keepdims=False)
        send_part = lax.dynamic_index_in_dim(cur, 1 - mine_bit, pos, keepdims=False)
        cur = keep_part + _pair_swap(send_part, axis, 1 << bit, size)
        bits.pop(pos)
    return cur


def _doubling_gather(value, axis, size, order):
    me = lax.axis_index(axis)
    cur = value
    bits = []
    for bit in order:
        other = _pair_swap(cur, axis, 1 << bit, size)
        low_is_me = ((me >> bit) & 1) == 0
        low = jnp.where(low_is_me, cur, other)
        high = jnp.where(low_is_me, other, cur)
        cur = jnp.stack([low, high], axis=0)
        bits.insert(0, bit)
    want = sorted(bits, reverse=True)
    cur = jnp.transpose(cur, [bits.index(b) for b in want] + list(range(len(bits), cur.ndim)))
    return cur.reshape((size,) + value.shape)


def _direct_gather(value, axis, size):
    me = lax.axis_index(axis)
    parts = [value] + [
        lax.ppermute(value, axis, [(i, (i + k) % size) for i in range(size)])
        for k in range(1, size)
    ]
    stacked = jnp.stack(parts, axis=0)
    return jnp.take(stacked, (me - jnp.arange(size)) % size, axis=0)


def _orders(size):
    nbits = size.bit_length() - 1
    first = list(range(nbits))
    second = first[:]
    if nbits >= 2:
        second[0], second[1] = 1, 0
    return first, second


def _halving_cols(cols, axis, size, order):
    nbits = size.bit_length() - 1
    me = lax.axis_index(axis)
    cur = cols
    block = 0
    for step, bit in enumerate(order):
        half = cur.shape[1] // 2
        mine_bit = (me >> bit) & 1
        keep_part = lax.dynamic_slice_in_dim(cur, mine_bit * half, half, axis=1)
        send_part = lax.dynamic_slice_in_dim(cur, (1 - mine_bit) * half, half, axis=1)
        cur = keep_part + _pair_swap(send_part, axis, 1 << bit, size)
        block = block + (mine_bit << (nbits - 1 - step))
    return cur, block


def _block_owners(size, order):
    nbits = size.bit_length() - 1
    owned = [
        sum(((d >> bit) & 1) << (nbits - 1 - step) for step, bit in enumerate(order))
        for d in range(size)
    ]
    return [owned.index(k) for k in range(size)]


def _doubling_cols(cols, axis, size, order):
    me = lax.axis_index(axis)
    cur = cols
    for bit in order[::-1]:
        other = _pair_swap(cur, axis, 1 << bit, size)
        low_is_me = ((me >> bit) & 1) == 0
        low = jnp.where(low_is_me, cur, other)
        high = jnp.where(low_is_me, other, cur)
        cur = jnp.concatenate([low, high], axis=1)
    return cur


def local(
    activations,
    bag_rows,
    keep_cols,
    enc_weight,
    enc_bias,
    dec_weight,
    dec_bias,
    first_moment,
    second_moment,
):
    lat_size = LAT_SIZE[0]
    first, second = _orders(lat_size)
    copies = jnp.broadcast_to(activations[None], (lat_size,) + activations.shape)
    act_blocks = lax.all_to_all(copies, "lat", 0, 0, tiled=True)
    half_rows = jnp.transpose(act_blocks, (1, 0, 2)).reshape(activations.shape[0], -1)
    other_rows = lax.ppermute(half_rows, "seed", [(0, 1), (1, 0)])
    seed_first = lax.axis_index("seed") == 0
    gathered = jnp.concatenate(
        [jnp.where(seed_first, half_rows, other_rows), jnp.where(seed_first, other_rows, half_rows)],
        axis=0,
    )
    row_order = bag_rows[0]
    sample = jnp.take(gathered, row_order, axis=0)
    weight_in = enc_weight[0]
    decoder = dec_weight[0]
    bias_dec = dec_bias[0]
    keep = keep_cols[0].astype(jnp.float32)
    centered = (sample.astype(jnp.float32) - bias_dec).astype(jnp.bfloat16)
    pre_t = lax.dot_general(
        weight_in, centered, (((1,), (1,)), ((), ())), preferred_element_type=jnp.float32
    )
    pre_t = pre_t + enc_bias[0][:, None]
    latent_t = jnp.maximum(pre_t, 0.0).astype(jnp.bfloat16)
    width = bias_dec.shape[0] // lat_size
    partial_sum = lax.dot_general(
        latent_t, decoder, (((0,), (0,)), ((), ())), preferred_element_type=jnp.float32
    )
    chunk = partial_sum.shape[0] // 4
    error_parts = []
    for part in range(4):
        rows = slice(part * chunk, (part + 1) * chunk)
        order = (first, second, first, first)[part]
        total, block = _halving_cols(partial_sum[rows], "lat", lat_size, order)
        start = block * width
        sample_cols = lax.dynamic_slice_in_dim(sample[rows], start, width, axis=1)
        bias_cols = lax.dynamic_slice_in_dim(bias_dec, start, width)
        keep_cols_f = lax.dynamic_slice_in_dim(keep, start, width)
        error_cols = (
            (total + bias_cols - sample_cols.astype(jnp.float32)) * keep_cols_f
        ).astype(jnp.bfloat16)
        stacked = _doubling_gather(error_cols, "lat", lat_size, order[::-1])
        error_parts.append(stacked[jnp.array(_block_owners(lat_size, order))])
    error_blocks = jnp.concatenate(error_parts, axis=1)
    error = jnp.transpose(error_blocks, (1, 0, 2)).reshape(error_blocks.shape[1], -1)
    updated, moment_one, moment_two = tail(
        pre_t, error, centered, decoder, weight_in, first_moment[0], second_moment[0]
    )
    return updated[None], moment_one[None], moment_two[None]


LAT_SIZE = [8]


def solution(mesh):
    LAT_SIZE[0] = mesh.shape["lat"]
    return jax.shard_map(
        local,
        mesh=mesh,
        in_specs=(
            P(("groups", "seed"), "lat"),
            P(("groups", "seed"), None),
            P(("groups", "seed"), None),
            P(("groups", "seed"), "lat", None),
            P(("groups", "seed"), "lat"),
            P(("groups", "seed"), "lat", None),
            P(("groups", "seed"), None),
            P(("groups", "seed"), "lat", None),
            P(("groups", "seed"), "lat", None),
        ),
        out_specs=(
            P(("groups", "seed"), "lat", None),
            P(("groups", "seed"), "lat", None),
            P(("groups", "seed"), "lat", None),
        ),
        check_vma=False,
    )
```

```python
import jax
import jax.numpy as jnp
from jax import lax
from jax.sharding import PartitionSpec as P
from jax.experimental import pallas as pl
from jax.experimental.pallas import tpu as pltpu

sparsity = 0.2
beta_one = 0.9
beta_two = 0.95
corr_one = 1.0 - 0.9**10
corr_two = 1.0 - 0.95**10
adam_eps = 1e-08
rate_step = 0.001
decay_rate = 0.1


def _tail_kernel(
    pre_ref, err_ref, cen_ref, dec_ref, enc_ref, m1_ref, m2_ref, w_out, m1_out, m2_out
):
    dec = dec_ref[...]
    dec32 = dec.astype(jnp.float32)
    row_norm = jnp.sqrt(jnp.sum(dec32 * dec32, axis=1, keepdims=True) + 1e-06)
    back_t = jnp.dot(dec, err_ref[...], preferred_element_type=jnp.float32)
    tokens = err_ref.shape[1]
    d_pre = (
        jnp.where(pre_ref[...] > 0, 2.0 * back_t + sparsity * row_norm, 0.0) / tokens
    ).astype(jnp.bfloat16)
    grad = jnp.dot(d_pre, cen_ref[...], preferred_element_type=jnp.float32)
    moment_one = beta_one * m1_ref[...].astype(jnp.float32) + (1.0 - beta_one) * grad
    moment_two = beta_two * m2_ref[...].astype(jnp.float32) + (1.0 - beta_two) * grad * grad
    direction = moment_one / (
        jnp.sqrt(moment_two * (corr_one * corr_one / corr_two)) + corr_one * adam_eps
    )
    old = enc_ref[...].astype(jnp.float32)
    w_out[...] = (old * (1.0 - rate_step * decay_rate) - rate_step * direction).astype(
        jnp.bfloat16
    )
    m1_out[...] = moment_one.astype(jnp.bfloat16)
    m2_out[...] = moment_two.astype(jnp.bfloat16)


def tail(pre_t, error, centered, decoder, weight_in, first, second, tile=256):
    n_lat, width = decoder.shape
    tokens = error.shape[0]
    error_t = error.T
    row_block = pl.BlockSpec((tile, width), lambda i: (i, 0))
    whole = pl.BlockSpec((tokens, width), lambda i: (0, 0))
    out = jax.ShapeDtypeStruct((n_lat, width), jnp.bfloat16)
    return pl.pallas_call(
        _tail_kernel,
        grid=(n_lat // tile,),
        in_specs=[
            pl.BlockSpec((tile, tokens), lambda i: (i, 0)),
            pl.BlockSpec((width, tokens), lambda i: (0, 0)),
            whole,
            row_block,
            row_block,
            row_block,
            row_block,
        ],
        out_specs=[row_block, row_block, row_block],
        out_shape=[out, out, out],
        compiler_params=pltpu.CompilerParams(vmem_limit_bytes=56 * 1024 * 1024),
    )(pre_t, error_t, centered, decoder, weight_in, first, second)


def _pair_swap(value, axis, mask, size):
    return lax.ppermute(value, axis, [(i, i ^ mask) for i in range(size)])


def _halving_sum(blocks, axis, size, order):
    nbits = size.bit_length() - 1
    me = lax.axis_index(axis)
    cur = blocks.reshape((2,) * nbits + blocks.shape[1:])
    bits = list(range(nbits - 1, -1, -1))
    for bit in order:
        pos = bits.index(bit)
        mine_bit = (me >> bit) & 1
        keep_part = lax.dynamic_index_in_dim(cur, mine_bit, pos, keepdims=False)
        send_part = lax.dynamic_index_in_dim(cur, 1 - mine_bit, pos, keepdims=False)
        cur = keep_part + _pair_swap(send_part, axis, 1 << bit, size)
        bits.pop(pos)
    return cur


def _doubling_gather(value, axis, size, order):
    me = lax.axis_index(axis)
    cur = value
    bits = []
    for bit in order:
        other = _pair_swap(cur, axis, 1 << bit, size)
        low_is_me = ((me >> bit) & 1) == 0
        low = jnp.where(low_is_me, cur, other)
        high = jnp.where(low_is_me, other, cur)
        cur = jnp.stack([low, high], axis=0)
        bits.insert(0, bit)
    want = sorted(bits, reverse=True)
    cur = jnp.transpose(cur, [bits.index(b) for b in want] + list(range(len(bits), cur.ndim)))
    return cur.reshape((size,) + value.shape)


def _direct_gather(value, axis, size):
    me = lax.axis_index(axis)
    parts = [value] + [
        lax.ppermute(value, axis, [(i, (i + k) % size) for i in range(size)])
        for k in range(1, size)
    ]
    stacked = jnp.stack(parts, axis=0)
    return jnp.take(stacked, (me - jnp.arange(size)) % size, axis=0)


def _orders(size):
    nbits = size.bit_length() - 1
    first = list(range(nbits))
    second = first[:]
    if nbits >= 2:
        second[0], second[1] = 1, 0
    return first, second


def _halving_cols(cols, axis, size, order):
    nbits = size.bit_length() - 1
    me = lax.axis_index(axis)
    cur = cols
    block = 0
    for step, bit in enumerate(order):
        half = cur.shape[1] // 2
        mine_bit = (me >> bit) & 1
        keep_part = lax.dynamic_slice_in_dim(cur, mine_bit * half, half, axis=1)
        send_part = lax.dynamic_slice_in_dim(cur, (1 - mine_bit) * half, half, axis=1)
        cur = keep_part + _pair_swap(send_part, axis, 1 << bit, size)
        block = block + (mine_bit << (nbits - 1 - step))
    return cur, block


def _block_owners(size, order):
    nbits = size.bit_length() - 1
    owned = [
        sum(((d >> bit) & 1) << (nbits - 1 - step) for step, bit in enumerate(order))
        for d in range(size)
    ]
    return [owned.index(k) for k in range(size)]


def _doubling_cols(cols, axis, size, order):
    me = lax.axis_index(axis)
    cur = cols
    for bit in order[::-1]:
        other = _pair_swap(cur, axis, 1 << bit, size)
        low_is_me = ((me >> bit) & 1) == 0
        low = jnp.where(low_is_me, cur, other)
        high = jnp.where(low_is_me, other, cur)
        cur = jnp.concatenate([low, high], axis=1)
    return cur


def local(
    activations,
    bag_rows,
    keep_cols,
    enc_weight,
    enc_bias,
    dec_weight,
    dec_bias,
    first_moment,
    second_moment,
):
    lat_size = LAT_SIZE[0]
    first, second = _orders(lat_size)
    copies = jnp.broadcast_to(activations[None], (lat_size,) + activations.shape)
    act_blocks = lax.all_to_all(copies, "lat", 0, 0, tiled=True)
    half_rows = jnp.transpose(act_blocks, (1, 0, 2)).reshape(activations.shape[0], -1)
    other_rows = lax.ppermute(half_rows, "seed", [(0, 1), (1, 0)])
    seed_first = lax.axis_index("seed") == 0
    gathered = jnp.concatenate(
        [jnp.where(seed_first, half_rows, other_rows), jnp.where(seed_first, other_rows, half_rows)],
        axis=0,
    )
    row_order = bag_rows[0]
    sample = jnp.take(gathered, row_order, axis=0)
    weight_in = enc_weight[0]
    decoder = dec_weight[0]
    bias_dec = dec_bias[0]
    keep = keep_cols[0].astype(jnp.float32)
    centered = (sample.astype(jnp.float32) - bias_dec).astype(jnp.bfloat16)
    pre_t = lax.dot_general(
        weight_in, centered, (((1,), (1,)), ((), ())), preferred_element_type=jnp.float32
    )
    pre_t = pre_t + enc_bias[0][:, None]
    latent_t = jnp.maximum(pre_t, 0.0).astype(jnp.bfloat16)
    width = bias_dec.shape[0] // lat_size
    partial_sum = lax.dot_general(
        latent_t, decoder, (((0,), (0,)), ((), ())), preferred_element_type=jnp.float32
    )
    chunk = partial_sum.shape[0] // 8
    error_parts = []
    for part in range(8):
        rows = slice(part * chunk, (part + 1) * chunk)
        order = (first, second)[part % 2]
        total, block = _halving_cols(partial_sum[rows], "lat", lat_size, order)
        start = block * width
        sample_cols = lax.dynamic_slice_in_dim(sample[rows], start, width, axis=1)
        bias_cols = lax.dynamic_slice_in_dim(bias_dec, start, width)
        keep_cols_f = lax.dynamic_slice_in_dim(keep, start, width)
        error_cols = (
            (total + bias_cols - sample_cols.astype(jnp.float32)) * keep_cols_f
        ).astype(jnp.bfloat16)
        stacked = _doubling_gather(error_cols, "lat", lat_size, order[::-1])
        error_parts.append(stacked[jnp.array(_block_owners(lat_size, order))])
    error_blocks = jnp.concatenate(error_parts, axis=1)
    error = jnp.transpose(error_blocks, (1, 0, 2)).reshape(error_blocks.shape[1], -1)
    updated, moment_one, moment_two = tail(
        pre_t, error, centered, decoder, weight_in, first_moment[0], second_moment[0]
    )
    return updated[None], moment_one[None], moment_two[None]


LAT_SIZE = [8]


def solution(mesh):
    LAT_SIZE[0] = mesh.shape["lat"]
    return jax.shard_map(
        local,
        mesh=mesh,
        in_specs=(
            P(("groups", "seed"), "lat"),
            P(("groups", "seed"), None),
            P(("groups", "seed"), None),
            P(("groups", "seed"), "lat", None),
            P(("groups", "seed"), "lat"),
            P(("groups", "seed"), "lat", None),
            P(("groups", "seed"), None),
            P(("groups", "seed"), "lat", None),
            P(("groups", "seed"), "lat", None),
        ),
        out_specs=(
            P(("groups", "seed"), "lat", None),
            P(("groups", "seed"), "lat", None),
            P(("groups", "seed"), "lat", None),
        ),
        check_vma=False,
    )
```

```python
import jax
import jax.numpy as jnp
from jax import lax
from jax.sharding import PartitionSpec as P
from jax.experimental import pallas as pl
from jax.experimental.pallas import tpu as pltpu

sparsity = 0.2
beta_one = 0.9
beta_two = 0.95
corr_one = 1.0 - 0.9**10
corr_two = 1.0 - 0.95**10
adam_eps = 1e-08
rate_step = 0.001
decay_rate = 0.1


def _tail_kernel(
    pre_ref, err_ref, cen_ref, dec_ref, enc_ref, m1_ref, m2_ref, w_out, m1_out, m2_out
):
    dec = dec_ref[...]
    dec32 = dec.astype(jnp.float32)
    row_norm = jnp.sqrt(jnp.sum(dec32 * dec32, axis=1, keepdims=True) + 1e-06)
    back_t = jnp.dot(dec, err_ref[...], preferred_element_type=jnp.float32)
    tokens = err_ref.shape[1]
    d_pre = (
        jnp.where(pre_ref[...] > 0, 2.0 * back_t + sparsity * row_norm, 0.0) / tokens
    ).astype(jnp.bfloat16)
    grad = jnp.dot(d_pre, cen_ref[...], preferred_element_type=jnp.float32)
    moment_one = beta_one * m1_ref[...].astype(jnp.float32) + (1.0 - beta_one) * grad
    moment_two = beta_two * m2_ref[...].astype(jnp.float32) + (1.0 - beta_two) * grad * grad
    scaled_two = moment_two * (corr_one * corr_one / corr_two)
    direction = moment_one / (scaled_two * lax.rsqrt(scaled_two) + corr_one * adam_eps)
    old = enc_ref[...].astype(jnp.float32)
    w_out[...] = (old * (1.0 - rate_step * decay_rate) - rate_step * direction).astype(
        jnp.bfloat16
    )
    m1_out[...] = moment_one.astype(jnp.bfloat16)
    m2_out[...] = moment_two.astype(jnp.bfloat16)


def tail(pre_t, error, centered, decoder, weight_in, first, second, tile=256):
    n_lat, width = decoder.shape
    tokens = error.shape[0]
    error_t = error.T
    row_block = pl.BlockSpec((tile, width), lambda i: (i, 0))
    whole = pl.BlockSpec((tokens, width), lambda i: (0, 0))
    out = jax.ShapeDtypeStruct((n_lat, width), jnp.bfloat16)
    return pl.pallas_call(
        _tail_kernel,
        grid=(n_lat // tile,),
        in_specs=[
            pl.BlockSpec((tile, tokens), lambda i: (i, 0)),
            pl.BlockSpec((width, tokens), lambda i: (0, 0)),
            whole,
            row_block,
            row_block,
            row_block,
            row_block,
        ],
        out_specs=[row_block, row_block, row_block],
        out_shape=[out, out, out],
        compiler_params=pltpu.CompilerParams(vmem_limit_bytes=56 * 1024 * 1024),
    )(pre_t, error_t, centered, decoder, weight_in, first, second)


def _pair_swap(value, axis, mask, size):
    return lax.ppermute(value, axis, [(i, i ^ mask) for i in range(size)])


def _halving_sum(blocks, axis, size, order):
    nbits = size.bit_length() - 1
    me = lax.axis_index(axis)
    cur = blocks.reshape((2,) * nbits + blocks.shape[1:])
    bits = list(range(nbits - 1, -1, -1))
    for bit in order:
        pos = bits.index(bit)
        mine_bit = (me >> bit) & 1
        keep_part = lax.dynamic_index_in_dim(cur, mine_bit, pos, keepdims=False)
        send_part = lax.dynamic_index_in_dim(cur, 1 - mine_bit, pos, keepdims=False)
        cur = keep_part + _pair_swap(send_part, axis, 1 << bit, size)
        bits.pop(pos)
    return cur


def _doubling_gather(value, axis, size, order):
    me = lax.axis_index(axis)
    cur = value
    bits = []
    for bit in order:
        other = _pair_swap(cur, axis, 1 << bit, size)
        low_is_me = ((me >> bit) & 1) == 0
        low = jnp.where(low_is_me, cur, other)
        high = jnp.where(low_is_me, other, cur)
        cur = jnp.stack([low, high], axis=0)
        bits.insert(0, bit)
    want = sorted(bits, reverse=True)
    cur = jnp.transpose(cur, [bits.index(b) for b in want] + list(range(len(bits), cur.ndim)))
    return cur.reshape((size,) + value.shape)


def _direct_gather(value, axis, size):
    me = lax.axis_index(axis)
    parts = [value] + [
        lax.ppermute(value, axis, [(i, (i + k) % size) for i in range(size)])
        for k in range(1, size)
    ]
    stacked = jnp.stack(parts, axis=0)
    return jnp.take(stacked, (me - jnp.arange(size)) % size, axis=0)


def _orders(size):
    nbits = size.bit_length() - 1
    first = list(range(nbits))
    second = first[:]
    if nbits >= 2:
        second[0], second[1] = 1, 0
    return first, second


def _halving_cols(cols, axis, size, order):
    nbits = size.bit_length() - 1
    me = lax.axis_index(axis)
    cur = cols
    block = 0
    for step, bit in enumerate(order):
        half = cur.shape[1] // 2
        mine_bit = (me >> bit) & 1
        keep_part = lax.dynamic_slice_in_dim(cur, mine_bit * half, half, axis=1)
        send_part = lax.dynamic_slice_in_dim(cur, (1 - mine_bit) * half, half, axis=1)
        cur = keep_part + _pair_swap(send_part, axis, 1 << bit, size)
        block = block + (mine_bit << (nbits - 1 - step))
    return cur, block


def _block_owners(size, order):
    nbits = size.bit_length() - 1
    owned = [
        sum(((d >> bit) & 1) << (nbits - 1 - step) for step, bit in enumerate(order))
        for d in range(size)
    ]
    return [owned.index(k) for k in range(size)]


def _doubling_cols(cols, axis, size, order):
    me = lax.axis_index(axis)
    cur = cols
    for bit in order[::-1]:
        other = _pair_swap(cur, axis, 1 << bit, size)
        low_is_me = ((me >> bit) & 1) == 0
        low = jnp.where(low_is_me, cur, other)
        high = jnp.where(low_is_me, other, cur)
        cur = jnp.concatenate([low, high], axis=1)
    return cur


def local(
    activations,
    bag_rows,
    keep_cols,
    enc_weight,
    enc_bias,
    dec_weight,
    dec_bias,
    first_moment,
    second_moment,
):
    lat_size = LAT_SIZE[0]
    first, second = _orders(lat_size)
    copies = jnp.broadcast_to(activations[None], (lat_size,) + activations.shape)
    act_blocks = lax.all_to_all(copies, "lat", 0, 0, tiled=True)
    half_rows = jnp.transpose(act_blocks, (1, 0, 2)).reshape(activations.shape[0], -1)
    other_rows = lax.ppermute(half_rows, "seed", [(0, 1), (1, 0)])
    seed_first = lax.axis_index("seed") == 0
    gathered = jnp.concatenate(
        [jnp.where(seed_first, half_rows, other_rows), jnp.where(seed_first, other_rows, half_rows)],
        axis=0,
    )
    row_order = bag_rows[0]
    sample = jnp.take(gathered, row_order, axis=0)
    weight_in = enc_weight[0]
    decoder = dec_weight[0]
    bias_dec = dec_bias[0]
    keep = keep_cols[0].astype(jnp.float32)
    centered = (sample.astype(jnp.float32) - bias_dec).astype(jnp.bfloat16)
    pre_t = lax.dot_general(
        weight_in, centered, (((1,), (1,)), ((), ())), preferred_element_type=jnp.float32
    )
    pre_t = pre_t + enc_bias[0][:, None]
    latent_t = jnp.maximum(pre_t, 0.0).astype(jnp.bfloat16)
    width = bias_dec.shape[0] // lat_size
    partial_sum = lax.dot_general(
        latent_t, decoder, (((0,), (0,)), ((), ())), preferred_element_type=jnp.float32
    )
    chunk = partial_sum.shape[0] // 4
    error_parts = []
    for part in range(4):
        rows = slice(part * chunk, (part + 1) * chunk)
        order = (first, second)[part % 2]
        total, block = _halving_cols(partial_sum[rows], "lat", lat_size, order)
        start = block * width
        sample_cols = lax.dynamic_slice_in_dim(sample[rows], start, width, axis=1)
        bias_cols = lax.dynamic_slice_in_dim(bias_dec, start, width)
        keep_cols_f = lax.dynamic_slice_in_dim(keep, start, width)
        error_cols = (
            (total + bias_cols - sample_cols.astype(jnp.float32)) * keep_cols_f
        ).astype(jnp.bfloat16)
        stacked = _doubling_gather(error_cols, "lat", lat_size, order[::-1])
        error_parts.append(stacked[jnp.array(_block_owners(lat_size, order))])
    error_blocks = jnp.concatenate(error_parts, axis=1)
    error = jnp.transpose(error_blocks, (1, 0, 2)).reshape(error_blocks.shape[1], -1)
    updated, moment_one, moment_two = tail(
        pre_t, error, centered, decoder, weight_in, first_moment[0], second_moment[0]
    )
    return updated[None], moment_one[None], moment_two[None]


LAT_SIZE = [8]


def solution(mesh):
    LAT_SIZE[0] = mesh.shape["lat"]
    return jax.shard_map(
        local,
        mesh=mesh,
        in_specs=(
            P(("groups", "seed"), "lat"),
            P(("groups", "seed"), None),
            P(("groups", "seed"), None),
            P(("groups", "seed"), "lat", None),
            P(("groups", "seed"), "lat"),
            P(("groups", "seed"), "lat", None),
            P(("groups", "seed"), None),
            P(("groups", "seed"), "lat", None),
            P(("groups", "seed"), "lat", None),
        ),
        out_specs=(
            P(("groups", "seed"), "lat", None),
            P(("groups", "seed"), "lat", None),
            P(("groups", "seed"), "lat", None),
        ),
        check_vma=False,
    )
```

```python
import jax
import jax.numpy as jnp
from jax import lax
from jax.sharding import PartitionSpec as P
from jax.experimental import pallas as pl
from jax.experimental.pallas import tpu as pltpu

sparsity = 0.2
beta_one = 0.9
beta_two = 0.95
corr_one = 1.0 - 0.9**10
corr_two = 1.0 - 0.95**10
adam_eps = 1e-08
rate_step = 0.001
decay_rate = 0.1


def _tail_kernel(
    pre_ref, err_ref, cen_ref, dec_ref, enc_ref, m1_ref, m2_ref, w_out, m1_out, m2_out
):
    dec = dec_ref[...]
    dec32 = dec.astype(jnp.float32)
    row_norm = jnp.sqrt(jnp.sum(dec32 * dec32, axis=1, keepdims=True) + 1e-06)
    back_t = jnp.dot(dec, err_ref[...], preferred_element_type=jnp.float32)
    tokens = err_ref.shape[1]
    d_pre = (
        jnp.where(pre_ref[...] > 0, 2.0 * back_t + sparsity * row_norm, 0.0) / tokens
    ).astype(jnp.bfloat16)
    grad = jnp.dot(d_pre, cen_ref[...], preferred_element_type=jnp.float32)
    moment_one = beta_one * m1_ref[...].astype(jnp.float32) + (1.0 - beta_one) * grad
    moment_two = beta_two * m2_ref[...].astype(jnp.float32) + (1.0 - beta_two) * grad * grad
    scaled_two = moment_two * (corr_one * corr_one / corr_two)
    direction = moment_one / (scaled_two * lax.rsqrt(scaled_two) + corr_one * adam_eps)
    old = enc_ref[...].astype(jnp.float32)
    w_out[...] = (old * (1.0 - rate_step * decay_rate) - rate_step * direction).astype(
        jnp.bfloat16
    )
    m1_out[...] = moment_one.astype(jnp.bfloat16)
    m2_out[...] = moment_two.astype(jnp.bfloat16)


def tail(pre_t, error, centered, decoder, weight_in, first, second, tile=256):
    n_lat, width = decoder.shape
    if n_lat % tile:
        tile = n_lat
    tokens = error.shape[0]
    error_t = error.T
    row_block = pl.BlockSpec((tile, width), lambda i: (i, 0))
    whole = pl.BlockSpec((tokens, width), lambda i: (0, 0))
    out = jax.ShapeDtypeStruct((n_lat, width), jnp.bfloat16)
    return pl.pallas_call(
        _tail_kernel,
        grid=(n_lat // tile,),
        in_specs=[
            pl.BlockSpec((tile, tokens), lambda i: (i, 0)),
            pl.BlockSpec((width, tokens), lambda i: (0, 0)),
            whole,
            row_block,
            row_block,
            row_block,
            row_block,
        ],
        out_specs=[row_block, row_block, row_block],
        out_shape=[out, out, out],
        compiler_params=pltpu.CompilerParams(vmem_limit_bytes=56 * 1024 * 1024),
    )(pre_t, error_t, centered, decoder, weight_in, first, second)


def _pair_swap(value, axis, mask, size):
    return lax.ppermute(value, axis, [(i, i ^ mask) for i in range(size)])


def _halving_sum(blocks, axis, size, order):
    nbits = size.bit_length() - 1
    me = lax.axis_index(axis)
    cur = blocks.reshape((2,) * nbits + blocks.shape[1:])
    bits = list(range(nbits - 1, -1, -1))
    for bit in order:
        pos = bits.index(bit)
        mine_bit = (me >> bit) & 1
        keep_part = lax.dynamic_index_in_dim(cur, mine_bit, pos, keepdims=False)
        send_part = lax.dynamic_index_in_dim(cur, 1 - mine_bit, pos, keepdims=False)
        cur = keep_part + _pair_swap(send_part, axis, 1 << bit, size)
        bits.pop(pos)
    return cur


def _doubling_gather(value, axis, size, order):
    me = lax.axis_index(axis)
    cur = value
    bits = []
    for bit in order:
        other = _pair_swap(cur, axis, 1 << bit, size)
        low_is_me = ((me >> bit) & 1) == 0
        low = jnp.where(low_is_me, cur, other)
        high = jnp.where(low_is_me, other, cur)
        cur = jnp.stack([low, high], axis=0)
        bits.insert(0, bit)
    want = sorted(bits, reverse=True)
    cur = jnp.transpose(cur, [bits.index(b) for b in want] + list(range(len(bits), cur.ndim)))
    return cur.reshape((size,) + value.shape)


def _direct_gather(value, axis, size):
    me = lax.axis_index(axis)
    parts = [value] + [
        lax.ppermute(value, axis, [(i, (i + k) % size) for i in range(size)])
        for k in range(1, size)
    ]
    stacked = jnp.stack(parts, axis=0)
    return jnp.take(stacked, (me - jnp.arange(size)) % size, axis=0)


def _orders(size):
    nbits = size.bit_length() - 1
    first = list(range(nbits))
    second = first[:]
    if nbits >= 2:
        second[0], second[1] = 1, 0
    return first, second


def _halving_cols(cols, axis, size, order):
    nbits = size.bit_length() - 1
    me = lax.axis_index(axis)
    cur = cols
    block = 0
    for step, bit in enumerate(order):
        half = cur.shape[1] // 2
        mine_bit = (me >> bit) & 1
        keep_part = lax.dynamic_slice_in_dim(cur, mine_bit * half, half, axis=1)
        send_part = lax.dynamic_slice_in_dim(cur, (1 - mine_bit) * half, half, axis=1)
        cur = keep_part + _pair_swap(send_part, axis, 1 << bit, size)
        block = block + (mine_bit << (nbits - 1 - step))
    return cur, block


def _block_owners(size, order):
    nbits = size.bit_length() - 1
    owned = [
        sum(((d >> bit) & 1) << (nbits - 1 - step) for step, bit in enumerate(order))
        for d in range(size)
    ]
    return [owned.index(k) for k in range(size)]


def _doubling_cols(cols, axis, size, order):
    me = lax.axis_index(axis)
    cur = cols
    for bit in order[::-1]:
        other = _pair_swap(cur, axis, 1 << bit, size)
        low_is_me = ((me >> bit) & 1) == 0
        low = jnp.where(low_is_me, cur, other)
        high = jnp.where(low_is_me, other, cur)
        cur = jnp.concatenate([low, high], axis=1)
    return cur


def local(
    activations,
    bag_rows,
    keep_cols,
    enc_weight,
    enc_bias,
    dec_weight,
    dec_bias,
    first_moment,
    second_moment,
):
    lat_size = LAT_SIZE[0]
    first, second = _orders(lat_size)
    copies = jnp.broadcast_to(activations[None], (lat_size,) + activations.shape)
    act_blocks = lax.all_to_all(copies, "lat", 0, 0, tiled=True)
    half_rows = jnp.transpose(act_blocks, (1, 0, 2)).reshape(activations.shape[0], -1)
    other_rows = lax.ppermute(half_rows, "seed", [(0, 1), (1, 0)])
    seed_first = lax.axis_index("seed") == 0
    gathered = jnp.concatenate(
        [jnp.where(seed_first, half_rows, other_rows), jnp.where(seed_first, other_rows, half_rows)],
        axis=0,
    )
    row_order = bag_rows[0]
    sample = jnp.take(gathered, row_order, axis=0)
    weight_in = enc_weight[0]
    decoder = dec_weight[0]
    bias_dec = dec_bias[0]
    keep = keep_cols[0].astype(jnp.float32)
    centered = (sample.astype(jnp.float32) - bias_dec).astype(jnp.bfloat16)
    pre_t = lax.dot_general(
        weight_in, centered, (((1,), (1,)), ((), ())), preferred_element_type=jnp.float32
    )
    pre_t = pre_t + enc_bias[0][:, None]
    latent_t = jnp.maximum(pre_t, 0.0).astype(jnp.bfloat16)
    width = bias_dec.shape[0] // lat_size
    partial_sum = lax.dot_general(
        latent_t, decoder, (((0,), (0,)), ((), ())), preferred_element_type=jnp.float32
    )
    chunk = partial_sum.shape[0] // 4
    error_parts = []
    for part in range(4):
        rows = slice(part * chunk, (part + 1) * chunk)
        order = (first, second)[part % 2]
        total, block = _halving_cols(partial_sum[rows], "lat", lat_size, order)
        start = block * width
        sample_cols = lax.dynamic_slice_in_dim(sample[rows], start, width, axis=1)
        bias_cols = lax.dynamic_slice_in_dim(bias_dec, start, width)
        keep_cols_f = lax.dynamic_slice_in_dim(keep, start, width)
        error_cols = (
            (total + bias_cols - sample_cols.astype(jnp.float32)) * keep_cols_f
        ).astype(jnp.bfloat16)
        stacked = _doubling_gather(error_cols, "lat", lat_size, order[::-1])
        error_parts.append(stacked[jnp.array(_block_owners(lat_size, order))])
    error_blocks = jnp.concatenate(error_parts, axis=1)
    error = jnp.transpose(error_blocks, (1, 0, 2)).reshape(error_blocks.shape[1], -1)
    updated, moment_one, moment_two = tail(
        pre_t, error, centered, decoder, weight_in, first_moment[0], second_moment[0]
    )
    return updated[None], moment_one[None], moment_two[None]


LAT_SIZE = [8]


def solution(mesh):
    LAT_SIZE[0] = mesh.shape["lat"]
    return jax.shard_map(
        local,
        mesh=mesh,
        in_specs=(
            P(("groups", "seed"), "lat"),
            P(("groups", "seed"), None),
            P(("groups", "seed"), None),
            P(("groups", "seed"), "lat", None),
            P(("groups", "seed"), "lat"),
            P(("groups", "seed"), "lat", None),
            P(("groups", "seed"), None),
            P(("groups", "seed"), "lat", None),
            P(("groups", "seed"), "lat", None),
        ),
        out_specs=(
            P(("groups", "seed"), "lat", None),
            P(("groups", "seed"), "lat", None),
            P(("groups", "seed"), "lat", None),
        ),
        check_vma=False,
    )
```

```python
import jax
import jax.numpy as jnp
from jax import lax
from jax.sharding import PartitionSpec as P
from jax.experimental import pallas as pl
from jax.experimental.pallas import tpu as pltpu

sparsity = 0.2
beta_one = 0.9
beta_two = 0.95
corr_one = 1.0 - 0.9**10
corr_two = 1.0 - 0.95**10
adam_eps = 1e-08
rate_step = 0.001
decay_rate = 0.1


def _tail_kernel(
    pre_ref, err_ref, cen_ref, dec_ref, enc_ref, m1_ref, m2_ref, w_out, m1_out, m2_out
):
    dec = dec_ref[...]
    dec32 = dec.astype(jnp.float32)
    row_norm = jnp.sqrt(jnp.sum(dec32 * dec32, axis=1, keepdims=True) + 1e-06)
    back_t = jnp.dot(dec, err_ref[...], preferred_element_type=jnp.float32)
    tokens = err_ref.shape[1]
    d_pre = (
        jnp.where(pre_ref[...] > 0, 2.0 * back_t + sparsity * row_norm, 0.0) / tokens
    ).astype(jnp.bfloat16)
    grad = jnp.dot(d_pre, cen_ref[...], preferred_element_type=jnp.float32)
    moment_one = beta_one * m1_ref[...].astype(jnp.float32) + (1.0 - beta_one) * grad
    moment_two = beta_two * m2_ref[...].astype(jnp.float32) + (1.0 - beta_two) * grad * grad
    scaled_two = moment_two * (corr_one * corr_one / corr_two)
    direction = moment_one / (scaled_two * lax.rsqrt(scaled_two) + corr_one * adam_eps)
    old = enc_ref[...].astype(jnp.float32)
    w_out[...] = (old * (1.0 - rate_step * decay_rate) - rate_step * direction).astype(
        jnp.bfloat16
    )
    m1_out[...] = moment_one.astype(jnp.bfloat16)
    m2_out[...] = moment_two.astype(jnp.bfloat16)


def tail(pre_t, error, centered, decoder, weight_in, first, second, tile=512):
    n_lat, width = decoder.shape
    if n_lat % tile:
        tile = n_lat
    tokens = error.shape[0]
    error_t = error.T
    row_block = pl.BlockSpec((tile, width), lambda i: (i, 0))
    whole = pl.BlockSpec((tokens, width), lambda i: (0, 0))
    out = jax.ShapeDtypeStruct((n_lat, width), jnp.bfloat16)
    return pl.pallas_call(
        _tail_kernel,
        grid=(n_lat // tile,),
        in_specs=[
            pl.BlockSpec((tile, tokens), lambda i: (i, 0)),
            pl.BlockSpec((width, tokens), lambda i: (0, 0)),
            whole,
            row_block,
            row_block,
            row_block,
            row_block,
        ],
        out_specs=[row_block, row_block, row_block],
        out_shape=[out, out, out],
        compiler_params=pltpu.CompilerParams(vmem_limit_bytes=56 * 1024 * 1024),
    )(pre_t, error_t, centered, decoder, weight_in, first, second)


def _pair_swap(value, axis, mask, size):
    return lax.ppermute(value, axis, [(i, i ^ mask) for i in range(size)])


def _halving_sum(blocks, axis, size, order):
    nbits = size.bit_length() - 1
    me = lax.axis_index(axis)
    cur = blocks.reshape((2,) * nbits + blocks.shape[1:])
    bits = list(range(nbits - 1, -1, -1))
    for bit in order:
        pos = bits.index(bit)
        mine_bit = (me >> bit) & 1
        keep_part = lax.dynamic_index_in_dim(cur, mine_bit, pos, keepdims=False)
        send_part = lax.dynamic_index_in_dim(cur, 1 - mine_bit, pos, keepdims=False)
        cur = keep_part + _pair_swap(send_part, axis, 1 << bit, size)
        bits.pop(pos)
    return cur


def _doubling_gather(value, axis, size, order):
    me = lax.axis_index(axis)
    cur = value
    bits = []
    for bit in order:
        other = _pair_swap(cur, axis, 1 << bit, size)
        low_is_me = ((me >> bit) & 1) == 0
        low = jnp.where(low_is_me, cur, other)
        high = jnp.where(low_is_me, other, cur)
        cur = jnp.stack([low, high], axis=0)
        bits.insert(0, bit)
    want = sorted(bits, reverse=True)
    cur = jnp.transpose(cur, [bits.index(b) for b in want] + list(range(len(bits), cur.ndim)))
    return cur.reshape((size,) + value.shape)


def _direct_gather(value, axis, size):
    me = lax.axis_index(axis)
    parts = [value] + [
        lax.ppermute(value, axis, [(i, (i + k) % size) for i in range(size)])
        for k in range(1, size)
    ]
    stacked = jnp.stack(parts, axis=0)
    return jnp.take(stacked, (me - jnp.arange(size)) % size, axis=0)


def _orders(size):
    nbits = size.bit_length() - 1
    first = list(range(nbits))
    second = first[:]
    if nbits >= 2:
        second[0], second[1] = 1, 0
    return first, second


def _halving_cols(cols, axis, size, order):
    nbits = size.bit_length() - 1
    me = lax.axis_index(axis)
    cur = cols
    block = 0
    for step, bit in enumerate(order):
        half = cur.shape[1] // 2
        mine_bit = (me >> bit) & 1
        keep_part = lax.dynamic_slice_in_dim(cur, mine_bit * half, half, axis=1)
        send_part = lax.dynamic_slice_in_dim(cur, (1 - mine_bit) * half, half, axis=1)
        cur = keep_part + _pair_swap(send_part, axis, 1 << bit, size)
        block = block + (mine_bit << (nbits - 1 - step))
    return cur, block


def _block_owners(size, order):
    nbits = size.bit_length() - 1
    owned = [
        sum(((d >> bit) & 1) << (nbits - 1 - step) for step, bit in enumerate(order))
        for d in range(size)
    ]
    return [owned.index(k) for k in range(size)]


def _doubling_cols(cols, axis, size, order):
    me = lax.axis_index(axis)
    cur = cols
    for bit in order[::-1]:
        other = _pair_swap(cur, axis, 1 << bit, size)
        low_is_me = ((me >> bit) & 1) == 0
        low = jnp.where(low_is_me, cur, other)
        high = jnp.where(low_is_me, other, cur)
        cur = jnp.concatenate([low, high], axis=1)
    return cur


def local(
    activations,
    bag_rows,
    keep_cols,
    enc_weight,
    enc_bias,
    dec_weight,
    dec_bias,
    first_moment,
    second_moment,
):
    lat_size = LAT_SIZE[0]
    first, second = _orders(lat_size)
    copies = jnp.broadcast_to(activations[None], (lat_size,) + activations.shape)
    act_blocks = lax.all_to_all(copies, "lat", 0, 0, tiled=True)
    half_rows = jnp.transpose(act_blocks, (1, 0, 2)).reshape(activations.shape[0], -1)
    other_rows = lax.ppermute(half_rows, "seed", [(0, 1), (1, 0)])
    seed_first = lax.axis_index("seed") == 0
    gathered = jnp.concatenate(
        [jnp.where(seed_first, half_rows, other_rows), jnp.where(seed_first, other_rows, half_rows)],
        axis=0,
    )
    row_order = bag_rows[0]
    sample = jnp.take(gathered, row_order, axis=0)
    weight_in = enc_weight[0]
    decoder = dec_weight[0]
    bias_dec = dec_bias[0]
    keep = keep_cols[0].astype(jnp.float32)
    centered = (sample.astype(jnp.float32) - bias_dec).astype(jnp.bfloat16)
    pre_t = lax.dot_general(
        weight_in, centered, (((1,), (1,)), ((), ())), preferred_element_type=jnp.float32
    )
    pre_t = pre_t + enc_bias[0][:, None]
    latent_t = jnp.maximum(pre_t, 0.0).astype(jnp.bfloat16)
    width = bias_dec.shape[0] // lat_size
    partial_sum = lax.dot_general(
        latent_t, decoder, (((0,), (0,)), ((), ())), preferred_element_type=jnp.float32
    )
    chunk = partial_sum.shape[0] // 4
    error_parts = []
    for part in range(4):
        rows = slice(part * chunk, (part + 1) * chunk)
        order = (first, second)[part % 2]
        total, block = _halving_cols(partial_sum[rows], "lat", lat_size, order)
        start = block * width
        sample_cols = lax.dynamic_slice_in_dim(sample[rows], start, width, axis=1)
        bias_cols = lax.dynamic_slice_in_dim(bias_dec, start, width)
        keep_cols_f = lax.dynamic_slice_in_dim(keep, start, width)
        error_cols = (
            (total + bias_cols - sample_cols.astype(jnp.float32)) * keep_cols_f
        ).astype(jnp.bfloat16)
        stacked = _doubling_gather(error_cols, "lat", lat_size, order[::-1])
        error_parts.append(stacked[jnp.array(_block_owners(lat_size, order))])
    error_blocks = jnp.concatenate(error_parts, axis=1)
    error = jnp.transpose(error_blocks, (1, 0, 2)).reshape(error_blocks.shape[1], -1)
    updated, moment_one, moment_two = tail(
        pre_t, error, centered, decoder, weight_in, first_moment[0], second_moment[0]
    )
    return updated[None], moment_one[None], moment_two[None]


LAT_SIZE = [8]


def solution(mesh):
    LAT_SIZE[0] = mesh.shape["lat"]
    return jax.shard_map(
        local,
        mesh=mesh,
        in_specs=(
            P(("groups", "seed"), "lat"),
            P(("groups", "seed"), None),
            P(("groups", "seed"), None),
            P(("groups", "seed"), "lat", None),
            P(("groups", "seed"), "lat"),
            P(("groups", "seed"), "lat", None),
            P(("groups", "seed"), None),
            P(("groups", "seed"), "lat", None),
            P(("groups", "seed"), "lat", None),
        ),
        out_specs=(
            P(("groups", "seed"), "lat", None),
            P(("groups", "seed"), "lat", None),
            P(("groups", "seed"), "lat", None),
        ),
        check_vma=False,
    )
```

```python
import jax
import jax.numpy as jnp
from jax import lax
from jax.sharding import PartitionSpec as P
from jax.experimental import pallas as pl
from jax.experimental.pallas import tpu as pltpu

sparsity = 0.2
beta_one = 0.9
beta_two = 0.95
corr_one = 1.0 - 0.9**10
corr_two = 1.0 - 0.95**10
adam_eps = 1e-08
rate_step = 0.001
decay_rate = 0.1


def _tail_kernel(
    pre_ref, err_ref, cen_ref, dec_ref, enc_ref, m1_ref, m2_ref, w_out, m1_out, m2_out
):
    dec = dec_ref[...]
    dec32 = dec.astype(jnp.float32)
    row_norm = jnp.sqrt(jnp.sum(dec32 * dec32, axis=1, keepdims=True) + 1e-06)
    back_t = jnp.dot(dec, err_ref[...], preferred_element_type=jnp.float32)
    tokens = err_ref.shape[1]
    d_pre = (
        jnp.where(pre_ref[...] > 0, 2.0 * back_t + sparsity * row_norm, 0.0) / tokens
    ).astype(jnp.bfloat16)
    grad = jnp.dot(d_pre, cen_ref[...], preferred_element_type=jnp.float32)
    moment_one = beta_one * m1_ref[...].astype(jnp.float32) + (1.0 - beta_one) * grad
    moment_two = beta_two * m2_ref[...].astype(jnp.float32) + (1.0 - beta_two) * grad * grad
    scaled_two = moment_two * (corr_one * corr_one / corr_two)
    direction = moment_one / (scaled_two * lax.rsqrt(scaled_two) + corr_one * adam_eps)
    old = enc_ref[...].astype(jnp.float32)
    w_out[...] = (old * (1.0 - rate_step * decay_rate) - rate_step * direction).astype(
        jnp.bfloat16
    )
    m1_out[...] = moment_one.astype(jnp.bfloat16)
    m2_out[...] = moment_two.astype(jnp.bfloat16)


def tail(pre_t, error, centered, decoder, weight_in, first, second, tile=512):
    n_lat, width = decoder.shape
    if n_lat % tile:
        tile = n_lat
    tokens = error.shape[0]
    error_t = error.T
    row_block = pl.BlockSpec((tile, width), lambda i: (i, 0))
    whole = pl.BlockSpec((tokens, width), lambda i: (0, 0))
    out = jax.ShapeDtypeStruct((n_lat, width), jnp.bfloat16)
    return pl.pallas_call(
        _tail_kernel,
        grid=(n_lat // tile,),
        in_specs=[
            pl.BlockSpec((tile, tokens), lambda i: (i, 0)),
            pl.BlockSpec((width, tokens), lambda i: (0, 0)),
            whole,
            row_block,
            row_block,
            row_block,
            row_block,
        ],
        out_specs=[row_block, row_block, row_block],
        out_shape=[out, out, out],
        compiler_params=pltpu.CompilerParams(vmem_limit_bytes=56 * 1024 * 1024),
    )(pre_t, error_t, centered, decoder, weight_in, first, second)


def _pair_swap(value, axis, mask, size):
    return lax.ppermute(value, axis, [(i, i ^ mask) for i in range(size)])


def _halving_sum(blocks, axis, size, order):
    nbits = size.bit_length() - 1
    me = lax.axis_index(axis)
    cur = blocks.reshape((2,) * nbits + blocks.shape[1:])
    bits = list(range(nbits - 1, -1, -1))
    for bit in order:
        pos = bits.index(bit)
        mine_bit = (me >> bit) & 1
        keep_part = lax.dynamic_index_in_dim(cur, mine_bit, pos, keepdims=False)
        send_part = lax.dynamic_index_in_dim(cur, 1 - mine_bit, pos, keepdims=False)
        cur = keep_part + _pair_swap(send_part, axis, 1 << bit, size)
        bits.pop(pos)
    return cur


def _doubling_gather(value, axis, size, order):
    me = lax.axis_index(axis)
    cur = value
    bits = []
    for bit in order:
        other = _pair_swap(cur, axis, 1 << bit, size)
        low_is_me = ((me >> bit) & 1) == 0
        low = jnp.where(low_is_me, cur, other)
        high = jnp.where(low_is_me, other, cur)
        cur = jnp.stack([low, high], axis=0)
        bits.insert(0, bit)
    want = sorted(bits, reverse=True)
    cur = jnp.transpose(cur, [bits.index(b) for b in want] + list(range(len(bits), cur.ndim)))
    return cur.reshape((size,) + value.shape)


def _direct_gather(value, axis, size):
    me = lax.axis_index(axis)
    parts = [value] + [
        lax.ppermute(value, axis, [(i, (i + k) % size) for i in range(size)])
        for k in range(1, size)
    ]
    stacked = jnp.stack(parts, axis=0)
    return jnp.take(stacked, (me - jnp.arange(size)) % size, axis=0)


def _orders(size):
    nbits = size.bit_length() - 1
    first = list(range(nbits))
    second = first[:]
    if nbits >= 2:
        second[0], second[1] = 1, 0
    return first, second


def _halving_cols(cols, axis, size, order):
    nbits = size.bit_length() - 1
    me = lax.axis_index(axis)
    cur = cols
    block = 0
    for step, bit in enumerate(order):
        half = cur.shape[1] // 2
        mine_bit = (me >> bit) & 1
        keep_part = lax.dynamic_slice_in_dim(cur, mine_bit * half, half, axis=1)
        send_part = lax.dynamic_slice_in_dim(cur, (1 - mine_bit) * half, half, axis=1)
        cur = keep_part + _pair_swap(send_part, axis, 1 << bit, size)
        block = block + (mine_bit << (nbits - 1 - step))
    return cur, block


def _block_owners(size, order):
    nbits = size.bit_length() - 1
    owned = [
        sum(((d >> bit) & 1) << (nbits - 1 - step) for step, bit in enumerate(order))
        for d in range(size)
    ]
    return [owned.index(k) for k in range(size)]


def _doubling_cols(cols, axis, size, order):
    me = lax.axis_index(axis)
    cur = cols
    for bit in order[::-1]:
        other = _pair_swap(cur, axis, 1 << bit, size)
        low_is_me = ((me >> bit) & 1) == 0
        low = jnp.where(low_is_me, cur, other)
        high = jnp.where(low_is_me, other, cur)
        cur = jnp.concatenate([low, high], axis=1)
    return cur


def local(
    activations,
    bag_rows,
    keep_cols,
    enc_weight,
    enc_bias,
    dec_weight,
    dec_bias,
    first_moment,
    second_moment,
):
    lat_size = LAT_SIZE[0]
    first, second = _orders(lat_size)
    copies = jnp.broadcast_to(activations[None], (lat_size,) + activations.shape)
    act_blocks = lax.all_to_all(copies, "lat", 0, 0, tiled=True)
    half_rows = jnp.transpose(act_blocks, (1, 0, 2)).reshape(activations.shape[0], -1)
    other_rows = lax.ppermute(half_rows, "seed", [(0, 1), (1, 0)])
    seed_first = lax.axis_index("seed") == 0
    gathered = jnp.concatenate(
        [jnp.where(seed_first, half_rows, other_rows), jnp.where(seed_first, other_rows, half_rows)],
        axis=0,
    )
    row_order = bag_rows[0]
    sample = jnp.take(gathered, row_order, axis=0)
    weight_in = enc_weight[0]
    decoder = dec_weight[0]
    bias_dec = dec_bias[0]
    keep = keep_cols[0].astype(jnp.float32)
    centered = (sample.astype(jnp.float32) - bias_dec).astype(jnp.bfloat16)
    pre_t = lax.dot_general(
        weight_in, centered, (((1,), (1,)), ((), ())), preferred_element_type=jnp.float32
    )
    pre_t = pre_t + enc_bias[0][:, None]
    latent_t = jnp.maximum(pre_t, 0.0).astype(jnp.bfloat16)
    width = bias_dec.shape[0] // lat_size
    partial_sum = lax.dot_general(
        latent_t, decoder, (((0,), (0,)), ((), ())), preferred_element_type=jnp.float32
    )
    chunk = partial_sum.shape[0] // 4
    error_parts = []
    for part in range(4):
        rows = slice(part * chunk, (part + 1) * chunk)
        order = (first, second)[part % 2]
        total, block = _halving_cols(partial_sum[rows], "lat", lat_size, order)
        start = block * width
        sample_cols = lax.dynamic_slice_in_dim(sample[rows], start, width, axis=1)
        bias_cols = lax.dynamic_slice_in_dim(bias_dec, start, width)
        keep_cols_f = lax.dynamic_slice_in_dim(keep, start, width)
        error_cols = (
            (total + bias_cols - sample_cols.astype(jnp.float32)) * keep_cols_f
        ).astype(jnp.bfloat16)
        error_parts.append(error_cols)
    gathered_parts = []
    for group, order in enumerate((first, second)):
        joined = jnp.concatenate(error_parts[group::2], axis=0)
        stacked = _doubling_gather(joined, "lat", lat_size, order[::-1])
        gathered_parts.append(stacked[jnp.array(_block_owners(lat_size, order))])
    error_blocks = jnp.concatenate(
        [
            gathered_parts[part % 2][:, (part // 2) * chunk : (part // 2 + 1) * chunk]
            for part in range(4)
        ],
        axis=1,
    )
    error = jnp.transpose(error_blocks, (1, 0, 2)).reshape(error_blocks.shape[1], -1)
    updated, moment_one, moment_two = tail(
        pre_t, error, centered, decoder, weight_in, first_moment[0], second_moment[0]
    )
    return updated[None], moment_one[None], moment_two[None]


LAT_SIZE = [8]


def solution(mesh):
    LAT_SIZE[0] = mesh.shape["lat"]
    return jax.shard_map(
        local,
        mesh=mesh,
        in_specs=(
            P(("groups", "seed"), "lat"),
            P(("groups", "seed"), None),
            P(("groups", "seed"), None),
            P(("groups", "seed"), "lat", None),
            P(("groups", "seed"), "lat"),
            P(("groups", "seed"), "lat", None),
            P(("groups", "seed"), None),
            P(("groups", "seed"), "lat", None),
            P(("groups", "seed"), "lat", None),
        ),
        out_specs=(
            P(("groups", "seed"), "lat", None),
            P(("groups", "seed"), "lat", None),
            P(("groups", "seed"), "lat", None),
        ),
        check_vma=False,
    )
```

```python
import jax
import jax.numpy as jnp
from jax import lax
from jax.sharding import PartitionSpec as P
from jax.experimental import pallas as pl
from jax.experimental.pallas import tpu as pltpu

sparsity = 0.2
beta_one = 0.9
beta_two = 0.95
corr_one = 1.0 - 0.9**10
corr_two = 1.0 - 0.95**10
adam_eps = 1e-08
rate_step = 0.001
decay_rate = 0.1


def _tail_kernel(
    pre_ref, err_ref, cen_ref, dec_ref, enc_ref, m1_ref, m2_ref, w_out, m1_out, m2_out
):
    dec = dec_ref[...]
    dec32 = dec.astype(jnp.float32)
    row_norm = jnp.sqrt(jnp.sum(dec32 * dec32, axis=1, keepdims=True) + 1e-06)
    back_t = jnp.dot(dec, err_ref[...], preferred_element_type=jnp.float32)
    tokens = err_ref.shape[1]
    d_pre = (
        jnp.where(pre_ref[...].astype(jnp.float32) > 0, 2.0 * back_t + sparsity * row_norm, 0.0) / tokens
    ).astype(jnp.bfloat16)
    grad = jnp.dot(d_pre, cen_ref[...], preferred_element_type=jnp.float32)
    moment_one = beta_one * m1_ref[...].astype(jnp.float32) + (1.0 - beta_one) * grad
    moment_two = beta_two * m2_ref[...].astype(jnp.float32) + (1.0 - beta_two) * grad * grad
    scaled_two = moment_two * (corr_one * corr_one / corr_two)
    direction = moment_one / (scaled_two * lax.rsqrt(scaled_two) + corr_one * adam_eps)
    old = enc_ref[...].astype(jnp.float32)
    w_out[...] = (old * (1.0 - rate_step * decay_rate) - rate_step * direction).astype(
        jnp.bfloat16
    )
    m1_out[...] = moment_one.astype(jnp.bfloat16)
    m2_out[...] = moment_two.astype(jnp.bfloat16)


def tail(pre_t, error, centered, decoder, weight_in, first, second, tile=512):
    n_lat, width = decoder.shape
    if n_lat % tile:
        tile = n_lat
    tokens = error.shape[0]
    error_t = error.T
    row_block = pl.BlockSpec((tile, width), lambda i: (i, 0))
    whole = pl.BlockSpec((tokens, width), lambda i: (0, 0))
    out = jax.ShapeDtypeStruct((n_lat, width), jnp.bfloat16)
    return pl.pallas_call(
        _tail_kernel,
        grid=(n_lat // tile,),
        in_specs=[
            pl.BlockSpec((tile, tokens), lambda i: (i, 0)),
            pl.BlockSpec((width, tokens), lambda i: (0, 0)),
            whole,
            row_block,
            row_block,
            row_block,
            row_block,
        ],
        out_specs=[row_block, row_block, row_block],
        out_shape=[out, out, out],
        compiler_params=pltpu.CompilerParams(vmem_limit_bytes=56 * 1024 * 1024),
    )(pre_t, error_t, centered, decoder, weight_in, first, second)


def _pair_swap(value, axis, mask, size):
    return lax.ppermute(value, axis, [(i, i ^ mask) for i in range(size)])


def _halving_sum(blocks, axis, size, order):
    nbits = size.bit_length() - 1
    me = lax.axis_index(axis)
    cur = blocks.reshape((2,) * nbits + blocks.shape[1:])
    bits = list(range(nbits - 1, -1, -1))
    for bit in order:
        pos = bits.index(bit)
        mine_bit = (me >> bit) & 1
        keep_part = lax.dynamic_index_in_dim(cur, mine_bit, pos, keepdims=False)
        send_part = lax.dynamic_index_in_dim(cur, 1 - mine_bit, pos, keepdims=False)
        cur = keep_part + _pair_swap(send_part, axis, 1 << bit, size)
        bits.pop(pos)
    return cur


def _doubling_gather(value, axis, size, order):
    me = lax.axis_index(axis)
    cur = value
    bits = []
    for bit in order:
        other = _pair_swap(cur, axis, 1 << bit, size)
        low_is_me = ((me >> bit) & 1) == 0
        low = jnp.where(low_is_me, cur, other)
        high = jnp.where(low_is_me, other, cur)
        cur = jnp.stack([low, high], axis=0)
        bits.insert(0, bit)
    want = sorted(bits, reverse=True)
    cur = jnp.transpose(cur, [bits.index(b) for b in want] + list(range(len(bits), cur.ndim)))
    return cur.reshape((size,) + value.shape)


def _direct_gather(value, axis, size):
    me = lax.axis_index(axis)
    parts = [value] + [
        lax.ppermute(value, axis, [(i, (i + k) % size) for i in range(size)])
        for k in range(1, size)
    ]
    stacked = jnp.stack(parts, axis=0)
    return jnp.take(stacked, (me - jnp.arange(size)) % size, axis=0)


def _orders(size):
    nbits = size.bit_length() - 1
    first = list(range(nbits))
    second = first[:]
    if nbits >= 2:
        second[0], second[1] = 1, 0
    return first, second


def _halving_cols(cols, axis, size, order):
    nbits = size.bit_length() - 1
    me = lax.axis_index(axis)
    cur = cols
    block = 0
    for step, bit in enumerate(order):
        half = cur.shape[1] // 2
        mine_bit = (me >> bit) & 1
        keep_part = lax.dynamic_slice_in_dim(cur, mine_bit * half, half, axis=1)
        send_part = lax.dynamic_slice_in_dim(cur, (1 - mine_bit) * half, half, axis=1)
        cur = keep_part + _pair_swap(send_part, axis, 1 << bit, size)
        block = block + (mine_bit << (nbits - 1 - step))
    return cur, block


def _block_owners(size, order):
    nbits = size.bit_length() - 1
    owned = [
        sum(((d >> bit) & 1) << (nbits - 1 - step) for step, bit in enumerate(order))
        for d in range(size)
    ]
    return [owned.index(k) for k in range(size)]


def _doubling_cols(cols, axis, size, order):
    me = lax.axis_index(axis)
    cur = cols
    for bit in order[::-1]:
        other = _pair_swap(cur, axis, 1 << bit, size)
        low_is_me = ((me >> bit) & 1) == 0
        low = jnp.where(low_is_me, cur, other)
        high = jnp.where(low_is_me, other, cur)
        cur = jnp.concatenate([low, high], axis=1)
    return cur


def local(
    activations,
    bag_rows,
    keep_cols,
    enc_weight,
    enc_bias,
    dec_weight,
    dec_bias,
    first_moment,
    second_moment,
):
    lat_size = LAT_SIZE[0]
    first, second = _orders(lat_size)
    copies = jnp.broadcast_to(activations[None], (lat_size,) + activations.shape)
    act_blocks = lax.all_to_all(copies, "lat", 0, 0, tiled=True)
    half_rows = jnp.transpose(act_blocks, (1, 0, 2)).reshape(activations.shape[0], -1)
    other_rows = lax.ppermute(half_rows, "seed", [(0, 1), (1, 0)])
    seed_first = lax.axis_index("seed") == 0
    gathered = jnp.concatenate(
        [jnp.where(seed_first, half_rows, other_rows), jnp.where(seed_first, other_rows, half_rows)],
        axis=0,
    )
    row_order = bag_rows[0]
    sample = jnp.take(gathered, row_order, axis=0)
    weight_in = enc_weight[0]
    decoder = dec_weight[0]
    bias_dec = dec_bias[0]
    keep = keep_cols[0].astype(jnp.float32)
    centered = (sample.astype(jnp.float32) - bias_dec).astype(jnp.bfloat16)
    pre_t = lax.dot_general(
        weight_in, centered, (((1,), (1,)), ((), ())), preferred_element_type=jnp.float32
    )
    pre_t = pre_t + enc_bias[0][:, None]
    latent_t = jnp.maximum(pre_t, 0.0).astype(jnp.bfloat16)
    width = bias_dec.shape[0] // lat_size
    partial_sum = lax.dot_general(
        latent_t, decoder, (((0,), (0,)), ((), ())), preferred_element_type=jnp.float32
    )
    chunk = partial_sum.shape[0] // 4
    error_parts = []
    for part in range(4):
        rows = slice(part * chunk, (part + 1) * chunk)
        order = (first, second)[part % 2]
        total, block = _halving_cols(partial_sum[rows], "lat", lat_size, order)
        start = block * width
        sample_cols = lax.dynamic_slice_in_dim(sample[rows], start, width, axis=1)
        bias_cols = lax.dynamic_slice_in_dim(bias_dec, start, width)
        keep_cols_f = lax.dynamic_slice_in_dim(keep, start, width)
        error_cols = (
            (total + bias_cols - sample_cols.astype(jnp.float32)) * keep_cols_f
        ).astype(jnp.bfloat16)
        stacked = _doubling_gather(error_cols, "lat", lat_size, order[::-1])
        error_parts.append(stacked[jnp.array(_block_owners(lat_size, order))])
    error_blocks = jnp.concatenate(error_parts, axis=1)
    error = jnp.transpose(error_blocks, (1, 0, 2)).reshape(error_blocks.shape[1], -1)
    updated, moment_one, moment_two = tail(
        latent_t, error, centered, decoder, weight_in, first_moment[0], second_moment[0]
    )
    return updated[None], moment_one[None], moment_two[None]


LAT_SIZE = [8]


def solution(mesh):
    LAT_SIZE[0] = mesh.shape["lat"]
    return jax.shard_map(
        local,
        mesh=mesh,
        in_specs=(
            P(("groups", "seed"), "lat"),
            P(("groups", "seed"), None),
            P(("groups", "seed"), None),
            P(("groups", "seed"), "lat", None),
            P(("groups", "seed"), "lat"),
            P(("groups", "seed"), "lat", None),
            P(("groups", "seed"), None),
            P(("groups", "seed"), "lat", None),
            P(("groups", "seed"), "lat", None),
        ),
        out_specs=(
            P(("groups", "seed"), "lat", None),
            P(("groups", "seed"), "lat", None),
            P(("groups", "seed"), "lat", None),
        ),
        check_vma=False,
    )
```

```python
import jax
import jax.numpy as jnp
from jax import lax
from jax.sharding import PartitionSpec as P
from jax.experimental import pallas as pl
from jax.experimental.pallas import tpu as pltpu

sparsity = 0.2
beta_one = 0.9
beta_two = 0.95
corr_one = 1.0 - 0.9**10
corr_two = 1.0 - 0.95**10
adam_eps = 1e-08
rate_step = 0.001
decay_rate = 0.1


def _tail_kernel(
    pre_ref, err_ref, cen_ref, dec_ref, enc_ref, m1_ref, m2_ref, w_out, m1_out, m2_out
):
    dec = dec_ref[...]
    dec32 = dec.astype(jnp.float32)
    row_norm = jnp.sqrt(jnp.sum(dec32 * dec32, axis=1, keepdims=True) + 1e-06)
    back_t = jnp.dot(dec, err_ref[...], preferred_element_type=jnp.float32)
    tokens = err_ref.shape[1]
    d_pre = (
        jnp.where(pre_ref[...].astype(jnp.float32) > 0, 2.0 * back_t + sparsity * row_norm, 0.0) / tokens
    ).astype(jnp.bfloat16)
    grad = jnp.dot(d_pre, cen_ref[...], preferred_element_type=jnp.float32)
    moment_one = beta_one * m1_ref[...].astype(jnp.float32) + (1.0 - beta_one) * grad
    moment_two = beta_two * m2_ref[...].astype(jnp.float32) + (1.0 - beta_two) * grad * grad
    scaled_two = moment_two * (corr_one * corr_one / corr_two)
    direction = moment_one / (scaled_two * lax.rsqrt(scaled_two) + corr_one * adam_eps)
    old = enc_ref[...].astype(jnp.float32)
    w_out[...] = (old * (1.0 - rate_step * decay_rate) - rate_step * direction).astype(
        jnp.bfloat16
    )
    m1_out[...] = moment_one.astype(jnp.bfloat16)
    m2_out[...] = moment_two.astype(jnp.bfloat16)


def tail(pre_t, error, centered, decoder, weight_in, first, second, tile=128):
    n_lat, width = decoder.shape
    if n_lat % tile:
        tile = n_lat
    tokens = error.shape[0]
    error_t = error.T
    row_block = pl.BlockSpec((tile, width), lambda i: (i, 0))
    whole = pl.BlockSpec((tokens, width), lambda i: (0, 0))
    out = jax.ShapeDtypeStruct((n_lat, width), jnp.bfloat16)
    return pl.pallas_call(
        _tail_kernel,
        grid=(n_lat // tile,),
        in_specs=[
            pl.BlockSpec((tile, tokens), lambda i: (i, 0)),
            pl.BlockSpec((width, tokens), lambda i: (0, 0)),
            whole,
            row_block,
            row_block,
            row_block,
            row_block,
        ],
        out_specs=[row_block, row_block, row_block],
        out_shape=[out, out, out],
        compiler_params=pltpu.CompilerParams(vmem_limit_bytes=56 * 1024 * 1024),
    )(pre_t, error_t, centered, decoder, weight_in, first, second)


def _pair_swap(value, axis, mask, size):
    return lax.ppermute(value, axis, [(i, i ^ mask) for i in range(size)])


def _halving_sum(blocks, axis, size, order):
    nbits = size.bit_length() - 1
    me = lax.axis_index(axis)
    cur = blocks.reshape((2,) * nbits + blocks.shape[1:])
    bits = list(range(nbits - 1, -1, -1))
    for bit in order:
        pos = bits.index(bit)
        mine_bit = (me >> bit) & 1
        keep_part = lax.dynamic_index_in_dim(cur, mine_bit, pos, keepdims=False)
        send_part = lax.dynamic_index_in_dim(cur, 1 - mine_bit, pos, keepdims=False)
        cur = keep_part + _pair_swap(send_part, axis, 1 << bit, size)
        bits.pop(pos)
    return cur


def _doubling_gather(value, axis, size, order):
    me = lax.axis_index(axis)
    cur = value
    bits = []
    for bit in order:
        other = _pair_swap(cur, axis, 1 << bit, size)
        low_is_me = ((me >> bit) & 1) == 0
        low = jnp.where(low_is_me, cur, other)
        high = jnp.where(low_is_me, other, cur)
        cur = jnp.stack([low, high], axis=0)
        bits.insert(0, bit)
    want = sorted(bits, reverse=True)
    cur = jnp.transpose(cur, [bits.index(b) for b in want] + list(range(len(bits), cur.ndim)))
    return cur.reshape((size,) + value.shape)


def _direct_gather(value, axis, size):
    me = lax.axis_index(axis)
    parts = [value] + [
        lax.ppermute(value, axis, [(i, (i + k) % size) for i in range(size)])
        for k in range(1, size)
    ]
    stacked = jnp.stack(parts, axis=0)
    return jnp.take(stacked, (me - jnp.arange(size)) % size, axis=0)


def _orders(size):
    nbits = size.bit_length() - 1
    first = list(range(nbits))
    second = first[:]
    if nbits >= 2:
        second[0], second[1] = 1, 0
    return first, second


def _halving_cols(cols, axis, size, order):
    nbits = size.bit_length() - 1
    me = lax.axis_index(axis)
    cur = cols
    block = 0
    for step, bit in enumerate(order):
        half = cur.shape[1] // 2
        mine_bit = (me >> bit) & 1
        keep_part = lax.dynamic_slice_in_dim(cur, mine_bit * half, half, axis=1)
        send_part = lax.dynamic_slice_in_dim(cur, (1 - mine_bit) * half, half, axis=1)
        cur = keep_part + _pair_swap(send_part, axis, 1 << bit, size)
        block = block + (mine_bit << (nbits - 1 - step))
    return cur, block


def _block_owners(size, order):
    nbits = size.bit_length() - 1
    owned = [
        sum(((d >> bit) & 1) << (nbits - 1 - step) for step, bit in enumerate(order))
        for d in range(size)
    ]
    return [owned.index(k) for k in range(size)]


def _doubling_cols(cols, axis, size, order):
    me = lax.axis_index(axis)
    cur = cols
    for bit in order[::-1]:
        other = _pair_swap(cur, axis, 1 << bit, size)
        low_is_me = ((me >> bit) & 1) == 0
        low = jnp.where(low_is_me, cur, other)
        high = jnp.where(low_is_me, other, cur)
        cur = jnp.concatenate([low, high], axis=1)
    return cur


def local(
    activations,
    bag_rows,
    keep_cols,
    enc_weight,
    enc_bias,
    dec_weight,
    dec_bias,
    first_moment,
    second_moment,
):
    lat_size = LAT_SIZE[0]
    first, second = _orders(lat_size)
    copies = jnp.broadcast_to(activations[None], (lat_size,) + activations.shape)
    act_blocks = lax.all_to_all(copies, "lat", 0, 0, tiled=True)
    half_rows = jnp.transpose(act_blocks, (1, 0, 2)).reshape(activations.shape[0], -1)
    other_rows = lax.ppermute(half_rows, "seed", [(0, 1), (1, 0)])
    seed_first = lax.axis_index("seed") == 0
    gathered = jnp.concatenate(
        [jnp.where(seed_first, half_rows, other_rows), jnp.where(seed_first, other_rows, half_rows)],
        axis=0,
    )
    row_order = bag_rows[0]
    sample = jnp.take(gathered, row_order, axis=0)
    weight_in = enc_weight[0]
    decoder = dec_weight[0]
    bias_dec = dec_bias[0]
    keep = keep_cols[0].astype(jnp.float32)
    centered = (sample.astype(jnp.float32) - bias_dec).astype(jnp.bfloat16)
    pre_t = lax.dot_general(
        weight_in, centered, (((1,), (1,)), ((), ())), preferred_element_type=jnp.float32
    )
    pre_t = pre_t + enc_bias[0][:, None]
    latent_t = jnp.maximum(pre_t, 0.0).astype(jnp.bfloat16)
    width = bias_dec.shape[0] // lat_size
    partial_sum = lax.dot_general(
        latent_t, decoder, (((0,), (0,)), ((), ())), preferred_element_type=jnp.float32
    )
    chunk = partial_sum.shape[0] // 4
    error_parts = []
    for part in range(4):
        rows = slice(part * chunk, (part + 1) * chunk)
        order = (first, second)[part % 2]
        total, block = _halving_cols(partial_sum[rows], "lat", lat_size, order)
        start = block * width
        sample_cols = lax.dynamic_slice_in_dim(sample[rows], start, width, axis=1)
        bias_cols = lax.dynamic_slice_in_dim(bias_dec, start, width)
        keep_cols_f = lax.dynamic_slice_in_dim(keep, start, width)
        error_cols = (
            (total + bias_cols - sample_cols.astype(jnp.float32)) * keep_cols_f
        ).astype(jnp.bfloat16)
        stacked = _doubling_gather(error_cols, "lat", lat_size, order[::-1])
        error_parts.append(stacked[jnp.array(_block_owners(lat_size, order))])
    error_blocks = jnp.concatenate(error_parts, axis=1)
    error = jnp.transpose(error_blocks, (1, 0, 2)).reshape(error_blocks.shape[1], -1)
    updated, moment_one, moment_two = tail(
        latent_t, error, centered, decoder, weight_in, first_moment[0], second_moment[0]
    )
    return updated[None], moment_one[None], moment_two[None]


LAT_SIZE = [8]


def solution(mesh):
    LAT_SIZE[0] = mesh.shape["lat"]
    return jax.shard_map(
        local,
        mesh=mesh,
        in_specs=(
            P(("groups", "seed"), "lat"),
            P(("groups", "seed"), None),
            P(("groups", "seed"), None),
            P(("groups", "seed"), "lat", None),
            P(("groups", "seed"), "lat"),
            P(("groups", "seed"), "lat", None),
            P(("groups", "seed"), None),
            P(("groups", "seed"), "lat", None),
            P(("groups", "seed"), "lat", None),
        ),
        out_specs=(
            P(("groups", "seed"), "lat", None),
            P(("groups", "seed"), "lat", None),
            P(("groups", "seed"), "lat", None),
        ),
        check_vma=False,
    )
```

```python
import functools
import jax
import jax.numpy as jnp
from jax import lax
from jax.sharding import PartitionSpec as P
from jax.experimental import pallas as pl
from jax.experimental.pallas import tpu as pltpu

sparsity = 0.2
beta_one = 0.9
beta_two = 0.95
corr_one = 1.0 - 0.9**10
corr_two = 1.0 - 0.95**10
adam_eps = 1e-08
rate_step = 0.001
decay_rate = 0.1


def _tail_kernel(
    stacked,
    pre_ref, err_ref, cen_ref, dec_ref, enc_ref, m1_ref, m2_ref, w_out, m1_out, m2_out
):
    dec = dec_ref[...]
    dec32 = dec.astype(jnp.float32)
    row_norm = jnp.sqrt(jnp.sum(dec32 * dec32, axis=1, keepdims=True) + 1e-06)
    if stacked:
        blocks, tokens, part = err_ref.shape
        back_t = lax.dot_general(
            dec[:, :part], err_ref[0], (((1,), (1,)), ((), ())), preferred_element_type=jnp.float32
        )
        for b in range(1, blocks):
            back_t = back_t + lax.dot_general(
                dec[:, b * part : (b + 1) * part],
                err_ref[b],
                (((1,), (1,)), ((), ())),
                preferred_element_type=jnp.float32,
            )
    else:
        back_t = jnp.dot(dec, err_ref[...], preferred_element_type=jnp.float32)
        tokens = err_ref.shape[1]
    d_pre = (
        jnp.where(pre_ref[...].astype(jnp.float32) > 0, 2.0 * back_t + sparsity * row_norm, 0.0) / tokens
    ).astype(jnp.bfloat16)
    grad = jnp.dot(d_pre, cen_ref[...], preferred_element_type=jnp.float32)
    moment_one = beta_one * m1_ref[...].astype(jnp.float32) + (1.0 - beta_one) * grad
    moment_two = beta_two * m2_ref[...].astype(jnp.float32) + (1.0 - beta_two) * grad * grad
    scaled_two = moment_two * (corr_one * corr_one / corr_two)
    direction = moment_one / (scaled_two * lax.rsqrt(scaled_two) + corr_one * adam_eps)
    old = enc_ref[...].astype(jnp.float32)
    w_out[...] = (old * (1.0 - rate_step * decay_rate) - rate_step * direction).astype(
        jnp.bfloat16
    )
    m1_out[...] = moment_one.astype(jnp.bfloat16)
    m2_out[...] = moment_two.astype(jnp.bfloat16)


def tail(pre_t, error_blocks, centered, decoder, weight_in, first, second, tile=512):
    n_lat, width = decoder.shape
    if n_lat % tile:
        tile = n_lat
    tokens = error_blocks.shape[1]
    stacked = error_blocks.shape[0] <= 8
    if stacked:
        error_in = error_blocks
        error_spec = pl.BlockSpec(error_blocks.shape, lambda i: (0, 0, 0))
    else:
        error_in = jnp.transpose(error_blocks, (0, 2, 1)).reshape(width, tokens)
        error_spec = pl.BlockSpec((width, tokens), lambda i: (0, 0))
    row_block = pl.BlockSpec((tile, width), lambda i: (i, 0))
    whole = pl.BlockSpec((tokens, width), lambda i: (0, 0))
    out = jax.ShapeDtypeStruct((n_lat, width), jnp.bfloat16)
    return pl.pallas_call(
        functools.partial(_tail_kernel, stacked),
        grid=(n_lat // tile,),
        in_specs=[
            pl.BlockSpec((tile, tokens), lambda i: (i, 0)),
            error_spec,
            whole,
            row_block,
            row_block,
            row_block,
            row_block,
        ],
        out_specs=[row_block, row_block, row_block],
        out_shape=[out, out, out],
        compiler_params=pltpu.CompilerParams(vmem_limit_bytes=56 * 1024 * 1024),
    )(pre_t, error_in, centered, decoder, weight_in, first, second)


def _pair_swap(value, axis, mask, size):
    return lax.ppermute(value, axis, [(i, i ^ mask) for i in range(size)])


def _halving_sum(blocks, axis, size, order):
    nbits = size.bit_length() - 1
    me = lax.axis_index(axis)
    cur = blocks.reshape((2,) * nbits + blocks.shape[1:])
    bits = list(range(nbits - 1, -1, -1))
    for bit in order:
        pos = bits.index(bit)
        mine_bit = (me >> bit) & 1
        keep_part = lax.dynamic_index_in_dim(cur, mine_bit, pos, keepdims=False)
        send_part = lax.dynamic_index_in_dim(cur, 1 - mine_bit, pos, keepdims=False)
        cur = keep_part + _pair_swap(send_part, axis, 1 << bit, size)
        bits.pop(pos)
    return cur


def _doubling_gather(value, axis, size, order):
    me = lax.axis_index(axis)
    cur = value
    bits = []
    for bit in order:
        other = _pair_swap(cur, axis, 1 << bit, size)
        low_is_me = ((me >> bit) & 1) == 0
        low = jnp.where(low_is_me, cur, other)
        high = jnp.where(low_is_me, other, cur)
        cur = jnp.stack([low, high], axis=0)
        bits.insert(0, bit)
    want = sorted(bits, reverse=True)
    cur = jnp.transpose(cur, [bits.index(b) for b in want] + list(range(len(bits), cur.ndim)))
    return cur.reshape((size,) + value.shape)


def _direct_gather(value, axis, size):
    me = lax.axis_index(axis)
    parts = [value] + [
        lax.ppermute(value, axis, [(i, (i + k) % size) for i in range(size)])
        for k in range(1, size)
    ]
    stacked = jnp.stack(parts, axis=0)
    return jnp.take(stacked, (me - jnp.arange(size)) % size, axis=0)


def _orders(size):
    nbits = size.bit_length() - 1
    first = list(range(nbits))
    second = first[:]
    if nbits >= 2:
        second[0], second[1] = 1, 0
    return first, second


def _halving_cols(cols, axis, size, order):
    nbits = size.bit_length() - 1
    me = lax.axis_index(axis)
    cur = cols
    block = 0
    for step, bit in enumerate(order):
        half = cur.shape[1] // 2
        mine_bit = (me >> bit) & 1
        keep_part = lax.dynamic_slice_in_dim(cur, mine_bit * half, half, axis=1)
        send_part = lax.dynamic_slice_in_dim(cur, (1 - mine_bit) * half, half, axis=1)
        cur = keep_part + _pair_swap(send_part, axis, 1 << bit, size)
        block = block + (mine_bit << (nbits - 1 - step))
    return cur, block


def _block_owners(size, order):
    nbits = size.bit_length() - 1
    owned = [
        sum(((d >> bit) & 1) << (nbits - 1 - step) for step, bit in enumerate(order))
        for d in range(size)
    ]
    return [owned.index(k) for k in range(size)]


def _doubling_cols(cols, axis, size, order):
    me = lax.axis_index(axis)
    cur = cols
    for bit in order[::-1]:
        other = _pair_swap(cur, axis, 1 << bit, size)
        low_is_me = ((me >> bit) & 1) == 0
        low = jnp.where(low_is_me, cur, other)
        high = jnp.where(low_is_me, other, cur)
        cur = jnp.concatenate([low, high], axis=1)
    return cur


def local(
    activations,
    bag_rows,
    keep_cols,
    enc_weight,
    enc_bias,
    dec_weight,
    dec_bias,
    first_moment,
    second_moment,
):
    lat_size = LAT_SIZE[0]
    first, second = _orders(lat_size)
    copies = jnp.broadcast_to(activations[None], (lat_size,) + activations.shape)
    act_blocks = lax.all_to_all(copies, "lat", 0, 0, tiled=True)
    half_rows = jnp.transpose(act_blocks, (1, 0, 2)).reshape(activations.shape[0], -1)
    other_rows = lax.ppermute(half_rows, "seed", [(0, 1), (1, 0)])
    seed_first = lax.axis_index("seed") == 0
    gathered = jnp.concatenate(
        [jnp.where(seed_first, half_rows, other_rows), jnp.where(seed_first, other_rows, half_rows)],
        axis=0,
    )
    row_order = bag_rows[0]
    sample = jnp.take(gathered, row_order, axis=0)
    weight_in = enc_weight[0]
    decoder = dec_weight[0]
    bias_dec = dec_bias[0]
    keep = keep_cols[0].astype(jnp.float32)
    centered = (sample.astype(jnp.float32) - bias_dec).astype(jnp.bfloat16)
    pre_t = lax.dot_general(
        weight_in, centered, (((1,), (1,)), ((), ())), preferred_element_type=jnp.float32
    )
    pre_t = pre_t + enc_bias[0][:, None]
    latent_t = jnp.maximum(pre_t, 0.0).astype(jnp.bfloat16)
    width = bias_dec.shape[0] // lat_size
    partial_sum = lax.dot_general(
        latent_t, decoder, (((0,), (0,)), ((), ())), preferred_element_type=jnp.float32
    )
    chunk = partial_sum.shape[0] // 4
    error_parts = []
    for part in range(4):
        rows = slice(part * chunk, (part + 1) * chunk)
        order = (first, second)[part % 2]
        total, block = _halving_cols(partial_sum[rows], "lat", lat_size, order)
        start = block * width
        sample_cols = lax.dynamic_slice_in_dim(sample[rows], start, width, axis=1)
        bias_cols = lax.dynamic_slice_in_dim(bias_dec, start, width)
        keep_cols_f = lax.dynamic_slice_in_dim(keep, start, width)
        error_cols = (
            (total + bias_cols - sample_cols.astype(jnp.float32)) * keep_cols_f
        ).astype(jnp.bfloat16)
        stacked = _doubling_gather(error_cols, "lat", lat_size, order[::-1])
        error_parts.append(stacked[jnp.array(_block_owners(lat_size, order))])
    error_blocks = jnp.concatenate(error_parts, axis=1)
    updated, moment_one, moment_two = tail(
        latent_t, error_blocks, centered, decoder, weight_in, first_moment[0], second_moment[0]
    )
    return updated[None], moment_one[None], moment_two[None]


LAT_SIZE = [8]


def solution(mesh):
    LAT_SIZE[0] = mesh.shape["lat"]
    return jax.shard_map(
        local,
        mesh=mesh,
        in_specs=(
            P(("groups", "seed"), "lat"),
            P(("groups", "seed"), None),
            P(("groups", "seed"), None),
            P(("groups", "seed"), "lat", None),
            P(("groups", "seed"), "lat"),
            P(("groups", "seed"), "lat", None),
            P(("groups", "seed"), None),
            P(("groups", "seed"), "lat", None),
            P(("groups", "seed"), "lat", None),
        ),
        out_specs=(
            P(("groups", "seed"), "lat", None),
            P(("groups", "seed"), "lat", None),
            P(("groups", "seed"), "lat", None),
        ),
        check_vma=False,
    )
```

```python
import functools
import jax
import jax.numpy as jnp
from jax import lax
from jax.sharding import PartitionSpec as P
from jax.experimental import pallas as pl
from jax.experimental.pallas import tpu as pltpu

sparsity = 0.2
beta_one = 0.9
beta_two = 0.95
corr_one = 1.0 - 0.9**10
corr_two = 1.0 - 0.95**10
adam_eps = 1e-08
rate_step = 0.001
decay_rate = 0.1


def _tail_kernel(
    stacked,
    pre_ref, err_ref, cen_ref, dec_ref, enc_ref, m1_ref, m2_ref, w_out, m1_out, m2_out
):
    dec = dec_ref[...]
    dec32 = dec.astype(jnp.float32)
    row_norm = jnp.sqrt(jnp.sum(dec32 * dec32, axis=1, keepdims=True) + 1e-06)
    if stacked:
        groups, blocks, group_tokens, part = err_ref.shape
        tokens = groups * group_tokens
        pieces = []
        for g in range(groups):
            piece = None
            for k in range(blocks):
                term = lax.dot_general(
                    dec[:, k * part : (k + 1) * part],
                    err_ref[g, stacked[g][k]],
                    (((1,), (1,)), ((), ())),
                    preferred_element_type=jnp.float32,
                )
                piece = term if piece is None else piece + term
            pieces.append(piece)
        back_t = jnp.concatenate(pieces, axis=1)
    else:
        back_t = jnp.dot(dec, err_ref[...], preferred_element_type=jnp.float32)
        tokens = err_ref.shape[1]
    d_pre = (
        jnp.where(pre_ref[...].astype(jnp.float32) > 0, 2.0 * back_t + sparsity * row_norm, 0.0) / tokens
    ).astype(jnp.bfloat16)
    grad = jnp.dot(d_pre, cen_ref[...], preferred_element_type=jnp.float32)
    moment_one = beta_one * m1_ref[...].astype(jnp.float32) + (1.0 - beta_one) * grad
    moment_two = beta_two * m2_ref[...].astype(jnp.float32) + (1.0 - beta_two) * grad * grad
    scaled_two = moment_two * (corr_one * corr_one / corr_two)
    direction = moment_one / (scaled_two * lax.rsqrt(scaled_two) + corr_one * adam_eps)
    old = enc_ref[...].astype(jnp.float32)
    w_out[...] = (old * (1.0 - rate_step * decay_rate) - rate_step * direction).astype(
        jnp.bfloat16
    )
    m1_out[...] = moment_one.astype(jnp.bfloat16)
    m2_out[...] = moment_two.astype(jnp.bfloat16)


def tail(pre_t, error_blocks, owners, centered, decoder, weight_in, first, second, tile=512):
    n_lat, width = decoder.shape
    if n_lat % tile:
        tile = n_lat
    groups, blocks, group_tokens, part = error_blocks.shape
    tokens = groups * group_tokens
    if blocks <= 8:
        stacked = tuple(tuple(o) for o in owners)
        error_in = error_blocks
        error_spec = pl.BlockSpec(error_blocks.shape, lambda i: (0, 0, 0, 0))
    else:
        stacked = None
        ordered = jnp.stack([error_blocks[g][jnp.array(owners[g])] for g in range(groups)])
        error_in = jnp.transpose(ordered, (1, 3, 0, 2)).reshape(width, tokens)
        error_spec = pl.BlockSpec((width, tokens), lambda i: (0, 0))
    row_block = pl.BlockSpec((tile, width), lambda i: (i, 0))
    whole = pl.BlockSpec((tokens, width), lambda i: (0, 0))
    out = jax.ShapeDtypeStruct((n_lat, width), jnp.bfloat16)
    return pl.pallas_call(
        functools.partial(_tail_kernel, stacked),
        grid=(n_lat // tile,),
        in_specs=[
            pl.BlockSpec((tile, tokens), lambda i: (i, 0)),
            error_spec,
            whole,
            row_block,
            row_block,
            row_block,
            row_block,
        ],
        out_specs=[row_block, row_block, row_block],
        out_shape=[out, out, out],
        compiler_params=pltpu.CompilerParams(vmem_limit_bytes=56 * 1024 * 1024),
    )(pre_t, error_in, centered, decoder, weight_in, first, second)


def _pair_swap(value, axis, mask, size):
    return lax.ppermute(value, axis, [(i, i ^ mask) for i in range(size)])


def _halving_sum(blocks, axis, size, order):
    nbits = size.bit_length() - 1
    me = lax.axis_index(axis)
    cur = blocks.reshape((2,) * nbits + blocks.shape[1:])
    bits = list(range(nbits - 1, -1, -1))
    for bit in order:
        pos = bits.index(bit)
        mine_bit = (me >> bit) & 1
        keep_part = lax.dynamic_index_in_dim(cur, mine_bit, pos, keepdims=False)
        send_part = lax.dynamic_index_in_dim(cur, 1 - mine_bit, pos, keepdims=False)
        cur = keep_part + _pair_swap(send_part, axis, 1 << bit, size)
        bits.pop(pos)
    return cur


def _doubling_gather(value, axis, size, order):
    me = lax.axis_index(axis)
    cur = value
    bits = []
    for bit in order:
        other = _pair_swap(cur, axis, 1 << bit, size)
        low_is_me = ((me >> bit) & 1) == 0
        low = jnp.where(low_is_me, cur, other)
        high = jnp.where(low_is_me, other, cur)
        cur = jnp.stack([low, high], axis=0)
        bits.insert(0, bit)
    want = sorted(bits, reverse=True)
    cur = jnp.transpose(cur, [bits.index(b) for b in want] + list(range(len(bits), cur.ndim)))
    return cur.reshape((size,) + value.shape)


def _direct_gather(value, axis, size):
    me = lax.axis_index(axis)
    parts = [value] + [
        lax.ppermute(value, axis, [(i, (i + k) % size) for i in range(size)])
        for k in range(1, size)
    ]
    stacked = jnp.stack(parts, axis=0)
    return jnp.take(stacked, (me - jnp.arange(size)) % size, axis=0)


def _orders(size):
    nbits = size.bit_length() - 1
    first = list(range(nbits))
    second = first[:]
    if nbits >= 2:
        second[0], second[1] = 1, 0
    return first, second


def _halving_cols(cols, axis, size, order):
    nbits = size.bit_length() - 1
    me = lax.axis_index(axis)
    cur = cols
    block = 0
    for step, bit in enumerate(order):
        half = cur.shape[1] // 2
        mine_bit = (me >> bit) & 1
        keep_part = lax.dynamic_slice_in_dim(cur, mine_bit * half, half, axis=1)
        send_part = lax.dynamic_slice_in_dim(cur, (1 - mine_bit) * half, half, axis=1)
        cur = keep_part + _pair_swap(send_part, axis, 1 << bit, size)
        block = block + (mine_bit << (nbits - 1 - step))
    return cur, block


def _block_owners(size, order):
    nbits = size.bit_length() - 1
    owned = [
        sum(((d >> bit) & 1) << (nbits - 1 - step) for step, bit in enumerate(order))
        for d in range(size)
    ]
    return [owned.index(k) for k in range(size)]


def _doubling_cols(cols, axis, size, order):
    me = lax.axis_index(axis)
    cur = cols
    for bit in order[::-1]:
        other = _pair_swap(cur, axis, 1 << bit, size)
        low_is_me = ((me >> bit) & 1) == 0
        low = jnp.where(low_is_me, cur, other)
        high = jnp.where(low_is_me, other, cur)
        cur = jnp.concatenate([low, high], axis=1)
    return cur


def local(
    activations,
    bag_rows,
    keep_cols,
    enc_weight,
    enc_bias,
    dec_weight,
    dec_bias,
    first_moment,
    second_moment,
):
    lat_size = LAT_SIZE[0]
    first, second = _orders(lat_size)
    copies = jnp.broadcast_to(activations[None], (lat_size,) + activations.shape)
    act_blocks = lax.all_to_all(copies, "lat", 0, 0, tiled=True)
    half_rows = jnp.transpose(act_blocks, (1, 0, 2)).reshape(activations.shape[0], -1)
    other_rows = lax.ppermute(half_rows, "seed", [(0, 1), (1, 0)])
    seed_first = lax.axis_index("seed") == 0
    gathered = jnp.concatenate(
        [jnp.where(seed_first, half_rows, other_rows), jnp.where(seed_first, other_rows, half_rows)],
        axis=0,
    )
    row_order = bag_rows[0]
    sample = jnp.take(gathered, row_order, axis=0)
    weight_in = enc_weight[0]
    decoder = dec_weight[0]
    bias_dec = dec_bias[0]
    keep = keep_cols[0].astype(jnp.float32)
    centered = (sample.astype(jnp.float32) - bias_dec).astype(jnp.bfloat16)
    pre_t = lax.dot_general(
        weight_in, centered, (((1,), (1,)), ((), ())), preferred_element_type=jnp.float32
    )
    pre_t = pre_t + enc_bias[0][:, None]
    latent_t = jnp.maximum(pre_t, 0.0).astype(jnp.bfloat16)
    width = bias_dec.shape[0] // lat_size
    partial_sum = lax.dot_general(
        latent_t, decoder, (((0,), (0,)), ((), ())), preferred_element_type=jnp.float32
    )
    chunk = partial_sum.shape[0] // 4
    error_parts = []
    for part in range(4):
        rows = slice(part * chunk, (part + 1) * chunk)
        order = (first, second)[part // 2]
        total, block = _halving_cols(partial_sum[rows], "lat", lat_size, order)
        start = block * width
        sample_cols = lax.dynamic_slice_in_dim(sample[rows], start, width, axis=1)
        bias_cols = lax.dynamic_slice_in_dim(bias_dec, start, width)
        keep_cols_f = lax.dynamic_slice_in_dim(keep, start, width)
        error_cols = (
            (total + bias_cols - sample_cols.astype(jnp.float32)) * keep_cols_f
        ).astype(jnp.bfloat16)
        error_parts.append(_doubling_gather(error_cols, "lat", lat_size, order[::-1]))
    error_blocks = jnp.stack(
        [jnp.concatenate(error_parts[0:2], axis=1), jnp.concatenate(error_parts[2:4], axis=1)]
    )
    owners = [_block_owners(lat_size, first), _block_owners(lat_size, second)]
    updated, moment_one, moment_two = tail(
        latent_t,
        error_blocks,
        owners,
        centered,
        decoder,
        weight_in,
        first_moment[0],
        second_moment[0],
    )
    return updated[None], moment_one[None], moment_two[None]


LAT_SIZE = [8]


def solution(mesh):
    LAT_SIZE[0] = mesh.shape["lat"]
    return jax.shard_map(
        local,
        mesh=mesh,
        in_specs=(
            P(("groups", "seed"), "lat"),
            P(("groups", "seed"), None),
            P(("groups", "seed"), None),
            P(("groups", "seed"), "lat", None),
            P(("groups", "seed"), "lat"),
            P(("groups", "seed"), "lat", None),
            P(("groups", "seed"), None),
            P(("groups", "seed"), "lat", None),
            P(("groups", "seed"), "lat", None),
        ),
        out_specs=(
            P(("groups", "seed"), "lat", None),
            P(("groups", "seed"), "lat", None),
            P(("groups", "seed"), "lat", None),
        ),
        check_vma=False,
    )
```

```python
import functools
import jax
import jax.numpy as jnp
from jax import lax
from jax.sharding import PartitionSpec as P
from jax.experimental import pallas as pl
from jax.experimental.pallas import tpu as pltpu

sparsity = 0.2
beta_one = 0.9
beta_two = 0.95
corr_one = 1.0 - 0.9**10
corr_two = 1.0 - 0.95**10
adam_eps = 1e-08
rate_step = 0.001
decay_rate = 0.1


def _tail_kernel(
    stacked,
    pre_ref, err_ref, cen_ref, dec_ref, enc_ref, m1_ref, m2_ref, w_out, m1_out, m2_out
):
    dec = dec_ref[...]
    dec32 = dec.astype(jnp.float32)
    row_norm = jnp.sqrt(jnp.sum(dec32 * dec32, axis=1, keepdims=True) + 1e-06)
    if stacked:
        groups, blocks, group_tokens, part = err_ref.shape
        tokens = groups * group_tokens
        pieces = []
        for g in range(groups):
            piece = None
            for k in range(blocks):
                term = lax.dot_general(
                    dec[:, k * part : (k + 1) * part],
                    err_ref[g, stacked[g][k]],
                    (((1,), (1,)), ((), ())),
                    preferred_element_type=jnp.float32,
                )
                piece = term if piece is None else piece + term
            pieces.append(piece)
        back_t = jnp.concatenate(pieces, axis=1)
    else:
        back_t = jnp.dot(dec, err_ref[...], preferred_element_type=jnp.float32)
        tokens = err_ref.shape[1]
    d_pre = (
        jnp.where(pre_ref[...].astype(jnp.float32) > 0, 2.0 * back_t + sparsity * row_norm, 0.0) / tokens
    ).astype(jnp.bfloat16)
    grad = jnp.dot(d_pre, cen_ref[...], preferred_element_type=jnp.float32)
    moment_one = beta_one * m1_ref[...].astype(jnp.float32) + (1.0 - beta_one) * grad
    moment_two = beta_two * m2_ref[...].astype(jnp.float32) + (1.0 - beta_two) * grad * grad
    scaled_two = moment_two * (corr_one * corr_one / corr_two)
    direction = moment_one / (scaled_two * lax.rsqrt(scaled_two) + corr_one * adam_eps)
    old = enc_ref[...].astype(jnp.float32)
    w_out[...] = (old * (1.0 - rate_step * decay_rate) - rate_step * direction).astype(
        jnp.bfloat16
    )
    m1_out[...] = moment_one.astype(jnp.bfloat16)
    m2_out[...] = moment_two.astype(jnp.bfloat16)


def tail(pre_t, error_blocks, owners, centered, decoder, weight_in, first, second, tile=512):
    n_lat, width = decoder.shape
    if n_lat % tile:
        tile = n_lat
    groups, blocks, group_tokens, part = error_blocks.shape
    tokens = groups * group_tokens
    if blocks <= 8:
        stacked = tuple(tuple(o) for o in owners)
        error_in = error_blocks
        error_spec = pl.BlockSpec(error_blocks.shape, lambda i: (0, 0, 0, 0))
    else:
        stacked = None
        ordered = jnp.stack([error_blocks[g][jnp.array(owners[g])] for g in range(groups)])
        error_in = jnp.transpose(ordered, (1, 3, 0, 2)).reshape(width, tokens)
        error_spec = pl.BlockSpec((width, tokens), lambda i: (0, 0))
    row_block = pl.BlockSpec((tile, width), lambda i: (i, 0))
    whole = pl.BlockSpec((tokens, width), lambda i: (0, 0))
    out = jax.ShapeDtypeStruct((n_lat, width), jnp.bfloat16)
    return pl.pallas_call(
        functools.partial(_tail_kernel, stacked),
        grid=(n_lat // tile,),
        in_specs=[
            pl.BlockSpec((tile, tokens), lambda i: (i, 0)),
            error_spec,
            whole,
            row_block,
            row_block,
            row_block,
            row_block,
        ],
        out_specs=[row_block, row_block, row_block],
        out_shape=[out, out, out],
        compiler_params=pltpu.CompilerParams(vmem_limit_bytes=56 * 1024 * 1024),
    )(pre_t, error_in, centered, decoder, weight_in, first, second)


def _pair_swap(value, axis, mask, size):
    return lax.ppermute(value, axis, [(i, i ^ mask) for i in range(size)])


def _halving_sum(blocks, axis, size, order):
    nbits = size.bit_length() - 1
    me = lax.axis_index(axis)
    cur = blocks.reshape((2,) * nbits + blocks.shape[1:])
    bits = list(range(nbits - 1, -1, -1))
    for bit in order:
        pos = bits.index(bit)
        mine_bit = (me >> bit) & 1
        keep_part = lax.dynamic_index_in_dim(cur, mine_bit, pos, keepdims=False)
        send_part = lax.dynamic_index_in_dim(cur, 1 - mine_bit, pos, keepdims=False)
        cur = keep_part + _pair_swap(send_part, axis, 1 << bit, size)
        bits.pop(pos)
    return cur


def _doubling_gather(value, axis, size, order):
    me = lax.axis_index(axis)
    cur = value
    bits = []
    for bit in order:
        other = _pair_swap(cur, axis, 1 << bit, size)
        low_is_me = ((me >> bit) & 1) == 0
        low = jnp.where(low_is_me, cur, other)
        high = jnp.where(low_is_me, other, cur)
        cur = jnp.stack([low, high], axis=0)
        bits.insert(0, bit)
    want = sorted(bits, reverse=True)
    cur = jnp.transpose(cur, [bits.index(b) for b in want] + list(range(len(bits), cur.ndim)))
    return cur.reshape((size,) + value.shape)


def _direct_gather(value, axis, size):
    me = lax.axis_index(axis)
    parts = [value] + [
        lax.ppermute(value, axis, [(i, (i + k) % size) for i in range(size)])
        for k in range(1, size)
    ]
    stacked = jnp.stack(parts, axis=0)
    return jnp.take(stacked, (me - jnp.arange(size)) % size, axis=0)


def _orders(size):
    nbits = size.bit_length() - 1
    first = list(range(nbits))
    second = first[:]
    if nbits >= 2:
        second[0], second[1] = 1, 0
    return first, second


def _halving_cols(cols, axis, size, order):
    nbits = size.bit_length() - 1
    me = lax.axis_index(axis)
    cur = cols
    block = 0
    for step, bit in enumerate(order):
        half = cur.shape[1] // 2
        mine_bit = (me >> bit) & 1
        keep_part = lax.dynamic_slice_in_dim(cur, mine_bit * half, half, axis=1)
        send_part = lax.dynamic_slice_in_dim(cur, (1 - mine_bit) * half, half, axis=1)
        cur = keep_part + _pair_swap(send_part, axis, 1 << bit, size)
        block = block + (mine_bit << (nbits - 1 - step))
    return cur, block


def _block_owners(size, order):
    nbits = size.bit_length() - 1
    owned = [
        sum(((d >> bit) & 1) << (nbits - 1 - step) for step, bit in enumerate(order))
        for d in range(size)
    ]
    return [owned.index(k) for k in range(size)]


def _doubling_cols(cols, axis, size, order):
    me = lax.axis_index(axis)
    cur = cols
    for bit in order[::-1]:
        other = _pair_swap(cur, axis, 1 << bit, size)
        low_is_me = ((me >> bit) & 1) == 0
        low = jnp.where(low_is_me, cur, other)
        high = jnp.where(low_is_me, other, cur)
        cur = jnp.concatenate([low, high], axis=1)
    return cur


def local(
    activations,
    bag_rows,
    keep_cols,
    enc_weight,
    enc_bias,
    dec_weight,
    dec_bias,
    first_moment,
    second_moment,
):
    lat_size = LAT_SIZE[0]
    first, second = _orders(lat_size)
    if lat_size <= 8:
        act_blocks = _direct_gather(activations, "lat", lat_size)
    else:
        copies = jnp.broadcast_to(activations[None], (lat_size,) + activations.shape)
        act_blocks = lax.all_to_all(copies, "lat", 0, 0, tiled=True)
    half_rows = jnp.transpose(act_blocks, (1, 0, 2)).reshape(activations.shape[0], -1)
    other_rows = lax.ppermute(half_rows, "seed", [(0, 1), (1, 0)])
    seed_first = lax.axis_index("seed") == 0
    gathered = jnp.concatenate(
        [jnp.where(seed_first, half_rows, other_rows), jnp.where(seed_first, other_rows, half_rows)],
        axis=0,
    )
    row_order = bag_rows[0]
    sample = jnp.take(gathered, row_order, axis=0)
    weight_in = enc_weight[0]
    decoder = dec_weight[0]
    bias_dec = dec_bias[0]
    keep = keep_cols[0].astype(jnp.float32)
    centered = (sample.astype(jnp.float32) - bias_dec).astype(jnp.bfloat16)
    pre_t = lax.dot_general(
        weight_in, centered, (((1,), (1,)), ((), ())), preferred_element_type=jnp.float32
    )
    pre_t = pre_t + enc_bias[0][:, None]
    latent_t = jnp.maximum(pre_t, 0.0).astype(jnp.bfloat16)
    width = bias_dec.shape[0] // lat_size
    partial_sum = lax.dot_general(
        latent_t, decoder, (((0,), (0,)), ((), ())), preferred_element_type=jnp.float32
    )
    chunk = partial_sum.shape[0] // 4
    error_parts = []
    for part in range(4):
        rows = slice(part * chunk, (part + 1) * chunk)
        order = (first, second)[part // 2]
        total, block = _halving_cols(partial_sum[rows], "lat", lat_size, order)
        start = block * width
        sample_cols = lax.dynamic_slice_in_dim(sample[rows], start, width, axis=1)
        bias_cols = lax.dynamic_slice_in_dim(bias_dec, start, width)
        keep_cols_f = lax.dynamic_slice_in_dim(keep, start, width)
        error_cols = (
            (total + bias_cols - sample_cols.astype(jnp.float32)) * keep_cols_f
        ).astype(jnp.bfloat16)
        error_parts.append(_doubling_gather(error_cols, "lat", lat_size, order[::-1]))
    error_blocks = jnp.stack(
        [jnp.concatenate(error_parts[0:2], axis=1), jnp.concatenate(error_parts[2:4], axis=1)]
    )
    owners = [_block_owners(lat_size, first), _block_owners(lat_size, second)]
    updated, moment_one, moment_two = tail(
        latent_t,
        error_blocks,
        owners,
        centered,
        decoder,
        weight_in,
        first_moment[0],
        second_moment[0],
    )
    return updated[None], moment_one[None], moment_two[None]


LAT_SIZE = [8]


def solution(mesh):
    LAT_SIZE[0] = mesh.shape["lat"]
    return jax.shard_map(
        local,
        mesh=mesh,
        in_specs=(
            P(("groups", "seed"), "lat"),
            P(("groups", "seed"), None),
            P(("groups", "seed"), None),
            P(("groups", "seed"), "lat", None),
            P(("groups", "seed"), "lat"),
            P(("groups", "seed"), "lat", None),
            P(("groups", "seed"), None),
            P(("groups", "seed"), "lat", None),
            P(("groups", "seed"), "lat", None),
        ),
        out_specs=(
            P(("groups", "seed"), "lat", None),
            P(("groups", "seed"), "lat", None),
            P(("groups", "seed"), "lat", None),
        ),
        check_vma=False,
    )
```
